32 devices in a mesh: grp: 2 (over x), blk: 2 (over core), head: 8 (over z, y).
Axes of the slice: x: 2, y: 2, z: 4, core: 2. Of those that a mesh axis runs over, the one named last changes fastest.
Arguments:
- stream: bfloat16 [1024, 3072], P(('grp', 'blk', 'head')), parts along dimension 0, may hold values from -6 to 6
- gains: float32 [3, 3072], replicated, may hold values from 0.25 to 1.75
- dilations: int32 [2], replicated, may hold values from 1 to 64, as said below
- w_conv: bfloat16 [2, 3, 3072, 2, 3072], P(None, None, None, None, 'head'), may hold values from -0.0625 to 0.0625
- w_mix: bfloat16 [2, 3072, 3072], P(None, 'head'), may hold values from -0.109375 to 0.109375
- w_qkv: bfloat16 [3072, 3, 8, 128], P(None, None, 'head')
- w_out: bfloat16 [8, 128, 3072], P('head'), may hold values from -0.1875 to 0.1875
Outputs:
- mixed: bfloat16 [1024, 3072], P(('grp', 'blk', 'head')), parts along dimension 0
The draws below stay inside these ranges and needn't reach their ends.
There are 2 independent parts, one for each index of `grp`. The reference program is written for one: setup_inputs(seed, part) draws one part's arguments, and reference() takes and returns one part's arrays. A program takes and returns all parts, laid end to end along the dimension named above; an argument that names none is the same for every part. Nothing has to cross between parts.
Inputs may be any that keep to these rules, and one draw needn't show every extreme that they name: `dilations`: each dilation is a whole number; one is exactly 64.
All inputs are finite; a program needn't handle non-finite values.
Results may differ from the reference program's by a relative error of at most 0.03.
Values may be sent and summed in bfloat16 or wider, within the bound.
No kernel may reach another device: no remote copies, remote signals or barrier semaphores. Data moves between devices by JAX's collectives and lax.ppermute only.
A program may use at most 128 MiB of HBM per device.

```python
import jax
import jax.numpy as jnp
from jax import lax

C = 3072
HD = 128
CONV_LAYERS = 2
LARGEST_DILATION = 64
HEADS = 8
SEQ = 512
N_HEAD = 8


def draw_dilations(key, part):
    first_key, second_key = jax.random.split(key)
    values = jax.random.randint(first_key, (CONV_LAYERS,), 1, LARGEST_DILATION + 1)
    chosen = jax.random.randint(second_key, (), 0, CONV_LAYERS)
    values = jnp.where(jnp.arange(CONV_LAYERS) == chosen, LARGEST_DILATION, values)
    return values.astype(jnp.int32)


def draw_w_qkv(key, part):
    first_key = jax.random.fold_in(key, 0)
    base = jax.random.normal(first_key, (C, 3, HEADS, HD), jnp.float32) * C ** (-0.5)
    return base.astype(jnp.bfloat16)


def steps_of(own_key, shape, cuts, low, high):
    def one(axis_at, shards_of):
        draws = jax.random.uniform(jax.random.fold_in(jax.random.fold_in(own_key, 6), axis_at), (shards_of,), jnp.float32, low / len(cuts), high / len(cuts))
        return jnp.repeat(jnp.exp(draws), shape[axis_at] // shards_of).reshape((-1,) + (1,) * (len(shape) - axis_at - 1))

    loudness = one(*cuts[0])
    for cut in cuts[1:]:
        loudness = loudness * one(*cut)
    return loudness


def scatter_about(rng, shape, width, limit, cuts=(), held_as=jnp.bfloat16):
    array = jax.random.normal(rng, shape, jnp.float32) * width
    if len(cuts) > 0:
        array = steps_of(rng, shape, cuts, -0.22, 0.18) * array
    return jnp.clip(array, min=-limit, max=limit).astype(held_as)


def setup_inputs(seed: int = 0, part: int = 0) -> dict:
    key_of = jax.random.split(jax.random.key(seed), 8)
    part_keys = jax.random.split(jax.random.fold_in(key_of[7], part), 8)
    return {
        "stream": scatter_about(part_keys[0], (SEQ, C), 1.0, 6.0, ((0, 16),)),
        "gains": jnp.clip(1.0 + 0.15 * jax.random.normal(key_of[1], (CONV_LAYERS + 1, C), jnp.float32), 0.25, 1.75),
        "dilations": draw_dilations(jax.random.fold_in(key_of[7], 71), part),
        "w_conv": scatter_about(key_of[3], (CONV_LAYERS, 3, C, 2, C), (3 * C) ** -0.5, 0.0625, ((4, 8),)),
        "w_mix": scatter_about(key_of[4], (CONV_LAYERS, C, C), C ** -0.5, 0.109375, ((1, 8),)),
        "w_qkv": draw_w_qkv(jax.random.fold_in(key_of[7], 71), part),
        "w_out": scatter_about(key_of[6], (HEADS, HD, C), (HEADS * HD) ** -0.5, 0.1875, ((0, 8),)),
    }


def normed(values, gain):
    wide = values.astype(jnp.float32)
    scale = lax.rsqrt(lax.optimization_barrier(jnp.mean(wide * wide, axis=-1, keepdims=True)) + 1e-06)
    return (wide * scale * gain.astype(jnp.float32)).astype(jnp.bfloat16)

def mix_partials(gated, weight):
    seq_len = gated.shape[0]
    group = C // N_HEAD
    pieces = gated.reshape(seq_len, N_HEAD, group).transpose(1, 0, 2)
    blocks = weight.reshape(N_HEAD, group, C)

    def append_fragment(carry, pair):
        piece, block = pair
        term = jnp.dot(piece, block, preferred_element_type=jnp.float32)
        return (carry + lax.optimization_barrier(term.astype(jnp.bfloat16)).astype(jnp.float32), None)
    total, unused_out = lax.scan(append_fragment, jnp.zeros((seq_len, C), jnp.float32), (pieces, blocks))
    return total

def reference(stream, gains, dilations, w_conv, w_mix, w_qkv, w_out):
    seq_len = stream.shape[0]
    border_rows = 2 * LARGEST_DILATION
    state = stream
    for layer_idx in range(CONV_LAYERS):
        hidden = normed(state, gains[layer_idx])
        padded = jnp.concatenate([jnp.zeros((border_rows, C), jnp.bfloat16), hidden], axis=0)
        dilation_factor = dilations[layer_idx].astype(jnp.int32)
        pre_act = jnp.zeros((seq_len, 2 * C), jnp.float32)
        for tap_idx in range(3):
            start = (border_rows - tap_idx * dilation_factor).astype(jnp.int32)
            slab = lax.dynamic_slice_in_dim(padded, start, seq_len, 0)
            pre_act = pre_act + jnp.dot(slab, w_conv[layer_idx, tap_idx].reshape(C, 2 * C), preferred_element_type=jnp.float32)
        pre_act = pre_act.reshape(seq_len, 2, C)
        gated = (jnp.tanh(pre_act[:, 0]) * jax.nn.sigmoid(pre_act[:, 1])).astype(jnp.bfloat16)
        state = (state.astype(jnp.float32) + mix_partials(gated, w_mix[layer_idx])).astype(jnp.bfloat16)
    attn_in = normed(state, gains[CONV_LAYERS])
    scale = HD ** (-0.5)
    positions = jnp.arange(seq_len, dtype=jnp.int32)
    causal = positions[:, None] >= positions[None, :]

    def head_step(carry, head_idx):
        weight = lax.dynamic_index_in_dim(w_qkv, head_idx, 2, keepdims=False).reshape(C, 3 * HD)
        projected = jnp.dot(attn_in, weight, preferred_element_type=jnp.float32).astype(jnp.bfloat16)
        queries = projected[:, :HD]
        keys_all = projected[:, HD:2 * HD]
        values_all = projected[:, 2 * HD:]
        scores = jnp.dot(queries, keys_all.T, preferred_element_type=jnp.float32) * scale
        scores = jnp.where(causal, scores, -1e+30)
        peak = lax.optimization_barrier(jnp.max(scores, axis=1, keepdims=True))
        probs = jnp.exp(scores - peak)
        denom = lax.optimization_barrier(jnp.sum(probs, axis=1, keepdims=True))
        heads_out = (jnp.dot(probs.astype(jnp.bfloat16), values_all, preferred_element_type=jnp.float32) / denom).astype(jnp.bfloat16)
        out_block = lax.dynamic_index_in_dim(w_out, head_idx, 0, keepdims=False)
        term = jnp.dot(heads_out, out_block, preferred_element_type=jnp.float32)
        return (carry + lax.optimization_barrier(term.astype(jnp.bfloat16)).astype(jnp.float32), None)
    total, unused_out = lax.scan(head_step, jnp.zeros((seq_len, C), jnp.float32), jnp.arange(HEADS, dtype=jnp.int32))
    return (state.astype(jnp.float32) + total).astype(jnp.bfloat16)
```

```python
import jax
import jax.numpy as jnp
from jax import lax
from jax.sharding import PartitionSpec as P

LARGEST_DILATION = 64


def shifted(value, axis, by):
    length = lax.axis_size(axis)
    pairs = [(i, i + by) for i in range(length) if 0 <= i + by < length]
    return lax.ppermute(value, axis, pairs)


def ring_order(length):
    if length % 2:
        return list(range(length))
    return list(range(0, length, 2)) + list(range(length - 1, 0, -2))


def ring_tables(axis):
    length = lax.axis_size(axis)
    order = ring_order(length)
    place = [0] * length
    for p, h in enumerate(order):
        place[h] = p
    me = jnp.array(place, jnp.int32)[lax.axis_index(axis)]
    return length, order, jnp.array(order, jnp.int32), me


def ring_gather(value, axis):
    length, order, order_arr, me = ring_tables(axis)
    forward = [(order[p], order[(p + 1) % length]) for p in range(length)]
    backward = [(order[p], order[(p - 1) % length]) for p in range(length)]
    ahead = length // 2
    behind = length - 1 - ahead
    rows = value.shape[0]
    out = jnp.zeros((length * rows,) + value.shape[1:], value.dtype)
    out = lax.dynamic_update_slice_in_dim(out, value, order_arr[me] * rows, 0)
    fwd = value
    bwd = value
    for k in range(1, ahead + 1):
        fwd = lax.ppermute(fwd, axis, forward)
        out = lax.dynamic_update_slice_in_dim(out, fwd, order_arr[(me - k) % length] * rows, 0)
        if k <= behind:
            bwd = lax.ppermute(bwd, axis, backward)
            out = lax.dynamic_update_slice_in_dim(out, bwd, order_arr[(me + k) % length] * rows, 0)
    return out


def ring_scatter_sum(value, axis):
    length, order, order_arr, me = ring_tables(axis)
    forward = [(order[p], order[(p + 1) % length]) for p in range(length)]
    backward = [(order[p], order[(p - 1) % length]) for p in range(length)]
    ahead = length // 2
    behind = length - 1 - ahead
    blocks = value.reshape((length, value.shape[0] // length) + value.shape[1:])

    def own(offset):
        return lax.dynamic_index_in_dim(blocks, order_arr[(me + offset) % length], 0, keepdims=False).astype(jnp.float32)

    total = own(0)
    fwd = None
    bwd = None
    for k in range(1, ahead + 1):
        part = own(ahead + 1 - k)
        if fwd is not None:
            part = part + fwd.astype(jnp.float32)
        fwd = lax.ppermute(part.astype(value.dtype), axis, forward)
        if k <= behind:
            part = own(k - behind - 1)
            if bwd is not None:
                part = part + bwd.astype(jnp.float32)
            bwd = lax.ppermute(part.astype(value.dtype), axis, backward)
    total = total + fwd.astype(jnp.float32)
    if bwd is not None:
        total = total + bwd.astype(jnp.float32)
    return total


def normed(values, gain):
    wide = values.astype(jnp.float32)
    scale = lax.rsqrt(jnp.mean(wide * wide, axis=-1, keepdims=True) + 1e-06)
    return (wide * scale * gain).astype(jnp.bfloat16)


def rounded_term(left, right):
    term = jnp.dot(left, right, preferred_element_type=jnp.float32)
    return lax.optimization_barrier(term.astype(jnp.bfloat16)).astype(jnp.float32)


def convolution_gate(hidden, kernel, dilation_factor):
    all_rows = hidden.shape[0]
    width = hidden.shape[1]
    own_width = kernel.shape[-1]
    border_rows = 2 * LARGEST_DILATION
    before = shifted(hidden[all_rows - border_rows :], "blk", 1)
    padded = jnp.concatenate([before, hidden], axis=0)
    pre_act = jnp.zeros((all_rows, 2 * own_width), jnp.float32)
    for tap_idx in range(3):
        start = border_rows - tap_idx * dilation_factor
        slab = lax.dynamic_slice_in_dim(padded, start, all_rows, 0)
        pre_act = pre_act + jnp.dot(
            slab, kernel[tap_idx].reshape(width, 2 * own_width), preferred_element_type=jnp.float32
        )
    return (jnp.tanh(pre_act[:, :own_width]) * jax.nn.sigmoid(pre_act[:, own_width:])).astype(
        jnp.bfloat16
    )


def conv_share(gated, weight, tok_rows):

    def term(start, count):
        return rounded_term(gated, weight)

    return ring_scatter_sum(
        term(jnp.int32(0), tok_rows * lax.axis_size("head")).astype(jnp.bfloat16), "head"
    )


def attention_portion_for(heads_out, out_block, tok_rows):

    def term(start, count):
        return rounded_term(heads_out, out_block)

    return ring_scatter_sum(
        term(jnp.int32(0), tok_rows * lax.axis_size("head")).astype(jnp.bfloat16), "head"
    )


def attend(queries, keys_in, values_in, causal):
    scale = queries.shape[1] ** (-0.5)
    scores = jnp.einsum("qd,kd->qk", queries, keys_in, preferred_element_type=jnp.float32) * scale
    if causal:
        rows_q = lax.broadcasted_iota(jnp.int32, scores.shape, 0)
        rows_k = lax.broadcasted_iota(jnp.int32, scores.shape, 1)
        scores = jnp.where(rows_q >= rows_k, scores, -1e30)
    peak = jnp.max(scores, axis=1)
    probs = jnp.exp(scores - peak[:, None])
    denom = jnp.sum(probs, axis=1)
    weighted = jnp.dot(probs.astype(jnp.bfloat16), values_in, preferred_element_type=jnp.float32)
    return (peak, denom, weighted)


def neutral(count, head_size):
    return (
        jnp.full((count,), -1e30, jnp.float32),
        jnp.zeros((count,), jnp.float32),
        jnp.zeros((count, head_size), jnp.float32),
    )


def combine(first, second):
    peak = jnp.maximum(first[0], second[0])
    scale_one = jnp.exp(first[0] - peak)
    scale_two = jnp.exp(second[0] - peak)
    denom = first[1] * scale_one + second[1] * scale_two
    weighted = first[2] * scale_one[:, None] + second[2] * scale_two[:, None]
    return (peak, denom, weighted)


def per_device(stream, gains, dilations, w_conv, w_mix, w_qkv, w_out):
    blk_pos = lax.axis_index("blk")
    tok_rows = stream.shape[0]
    width = stream.shape[1]
    head_size = w_qkv.shape[3]
    layers = w_conv.shape[0]
    qkv_weight = w_qkv.reshape(width, 3 * head_size)
    share = stream
    state = ring_gather(stream, "head")
    for layer_idx in range(layers):
        gated = convolution_gate(
            normed(state, gains[layer_idx]), w_conv[layer_idx], dilations[layer_idx]
        )
        summed = conv_share(gated, w_mix[layer_idx], tok_rows)
        share = (share.astype(jnp.float32) + summed).astype(jnp.bfloat16)
        state = ring_gather(share, "head")
    all_rows = state.shape[0]
    attn_in = normed(state, gains[layers])
    projected = jnp.dot(attn_in, qkv_weight, preferred_element_type=jnp.float32).astype(
        jnp.bfloat16
    )
    queries = projected[:, :head_size]
    keys_own = projected[:, head_size : 2 * head_size]
    values_own = projected[:, 2 * head_size :]
    keys_prev, values_prev = shifted((keys_own, values_own), "blk", 1)
    own_part = attend(queries, keys_own, values_own, True)
    crossing_portion = lax.cond(
        blk_pos > 0,
        lambda: attend(queries, keys_prev, values_prev, False),
        lambda: neutral(all_rows, head_size),
    )
    peak, denom, weighted = combine(own_part, crossing_portion)
    heads_out = (weighted / denom[:, None]).astype(jnp.bfloat16)
    attn_share = attention_portion_for(heads_out, w_out[0], tok_rows)
    return (share.astype(jnp.float32) + attn_share).astype(jnp.bfloat16)


def solution(mesh):
    placed = (
        P(("grp", "blk", "head"), None),
        P(),
        P(),
        P(None, None, None, None, "head"),
        P(None, "head", None),
        P(None, None, "head", None),
        P("head", None, None),
    )
    return jax.shard_map(
        per_device,
        mesh=mesh,
        in_specs=placed,
        out_specs=P(("grp", "blk", "head"), None),
        check_vma=False,
    )
```

```python
import jax
import jax.numpy as jnp
from jax import lax
from jax.sharding import PartitionSpec as P

LARGEST_DILATION = 64


def shifted(value, axis, by):
    length = lax.axis_size(axis)
    pairs = [(i, i + by) for i in range(length) if 0 <= i + by < length]
    return lax.ppermute(value, axis, pairs)


def ring_order(length):
    if length % 2:
        return list(range(length))
    return list(range(0, length, 2)) + list(range(length - 1, 0, -2))


def ring_tables(axis):
    length = lax.axis_size(axis)
    order = ring_order(length)
    place = [0] * length
    for p, h in enumerate(order):
        place[h] = p
    me = jnp.array(place, jnp.int32)[lax.axis_index(axis)]
    return length, order, jnp.array(order, jnp.int32), me


def ring_gather(value, axis):
    length, order, order_arr, me = ring_tables(axis)
    forward = [(order[p], order[(p + 1) % length]) for p in range(length)]
    backward = [(order[p], order[(p - 1) % length]) for p in range(length)]
    ahead = length // 2
    behind = length - 1 - ahead
    rows = value.shape[0]
    out = jnp.zeros((length * rows,) + value.shape[1:], value.dtype)
    out = lax.dynamic_update_slice_in_dim(out, value, order_arr[me] * rows, 0)
    fwd = value
    bwd = value
    for k in range(1, ahead + 1):
        fwd = lax.ppermute(fwd, axis, forward)
        out = lax.dynamic_update_slice_in_dim(out, fwd, order_arr[(me - k) % length] * rows, 0)
        if k <= behind:
            bwd = lax.ppermute(bwd, axis, backward)
            out = lax.dynamic_update_slice_in_dim(out, bwd, order_arr[(me + k) % length] * rows, 0)
    return out


def ring_scatter_sum(value, axis):
    length, order, order_arr, me = ring_tables(axis)
    forward = [(order[p], order[(p + 1) % length]) for p in range(length)]
    backward = [(order[p], order[(p - 1) % length]) for p in range(length)]
    ahead = length // 2
    behind = length - 1 - ahead
    blocks = value.reshape((length, value.shape[0] // length) + value.shape[1:])

    def own(offset):
        return lax.dynamic_index_in_dim(blocks, order_arr[(me + offset) % length], 0, keepdims=False).astype(jnp.float32)

    total = own(0)
    fwd = None
    bwd = None
    for k in range(1, ahead + 1):
        part = own(ahead + 1 - k)
        if fwd is not None:
            part = part + fwd.astype(jnp.float32)
        fwd = lax.ppermute(part.astype(value.dtype), axis, forward)
        if k <= behind:
            part = own(k - behind - 1)
            if bwd is not None:
                part = part + bwd.astype(jnp.float32)
            bwd = lax.ppermute(part.astype(value.dtype), axis, backward)
    total = total + fwd.astype(jnp.float32)
    if bwd is not None:
        total = total + bwd.astype(jnp.float32)
    return total


def normed(values, gain):
    wide = values.astype(jnp.float32)
    scale = lax.rsqrt(jnp.mean(wide * wide, axis=-1, keepdims=True) + 1e-06)
    return (wide * scale * gain).astype(jnp.bfloat16)


def rounded_term(left, right):
    term = jnp.dot(left, right, preferred_element_type=jnp.float32)
    return lax.optimization_barrier(term.astype(jnp.bfloat16)).astype(jnp.float32)


def convolution_gate(hidden, kernel, dilation_factor):
    all_rows = hidden.shape[0]
    width = hidden.shape[1]
    own_width = kernel.shape[-1]
    border_rows = 2 * LARGEST_DILATION
    before = shifted(hidden[all_rows - border_rows :], "blk", 1)
    padded = jnp.concatenate([before, hidden], axis=0)
    by_half = jnp.transpose(kernel, (0, 2, 1, 3))
    filt = jnp.zeros((all_rows, own_width), jnp.float32)
    gate = jnp.zeros((all_rows, own_width), jnp.float32)
    for tap_idx in range(3):
        start = border_rows - tap_idx * dilation_factor
        slab = lax.dynamic_slice_in_dim(padded, start, all_rows, 0)
        filt = filt + jnp.dot(slab, by_half[tap_idx, 0], preferred_element_type=jnp.float32)
        gate = gate + jnp.dot(slab, by_half[tap_idx, 1], preferred_element_type=jnp.float32)
    return (jnp.tanh(filt) * jax.nn.sigmoid(gate)).astype(jnp.bfloat16)


def conv_share(gated, weight, tok_rows):

    def term(start, count):
        return rounded_term(gated, weight)

    return ring_scatter_sum(
        term(jnp.int32(0), tok_rows * lax.axis_size("head")).astype(jnp.bfloat16), "head"
    )


def attention_portion_for(heads_out, out_block, tok_rows):

    def term(start, count):
        return rounded_term(heads_out, out_block)

    return ring_scatter_sum(
        term(jnp.int32(0), tok_rows * lax.axis_size("head")).astype(jnp.bfloat16), "head"
    )


def attend(queries, keys_in, values_in, causal):
    scale = queries.shape[1] ** (-0.5)
    scores = jnp.einsum("qd,kd->qk", queries, keys_in, preferred_element_type=jnp.float32) * scale
    if causal:
        rows_q = lax.broadcasted_iota(jnp.int32, scores.shape, 0)
        rows_k = lax.broadcasted_iota(jnp.int32, scores.shape, 1)
        scores = jnp.where(rows_q >= rows_k, scores, -1e30)
    peak = jnp.max(scores, axis=1)
    probs = jnp.exp(scores - peak[:, None])
    denom = jnp.sum(probs, axis=1)
    weighted = jnp.dot(probs.astype(jnp.bfloat16), values_in, preferred_element_type=jnp.float32)
    return (peak, denom, weighted)


def neutral(count, head_size):
    return (
        jnp.full((count,), -1e30, jnp.float32),
        jnp.zeros((count,), jnp.float32),
        jnp.zeros((count, head_size), jnp.float32),
    )


def combine(first, second):
    peak = jnp.maximum(first[0], second[0])
    scale_one = jnp.exp(first[0] - peak)
    scale_two = jnp.exp(second[0] - peak)
    denom = first[1] * scale_one + second[1] * scale_two
    weighted = first[2] * scale_one[:, None] + second[2] * scale_two[:, None]
    return (peak, denom, weighted)


def per_device(stream, gains, dilations, w_conv, w_mix, w_qkv, w_out):
    blk_pos = lax.axis_index("blk")
    tok_rows = stream.shape[0]
    width = stream.shape[1]
    head_size = w_qkv.shape[3]
    layers = w_conv.shape[0]
    share = stream
    state = ring_gather(stream, "head")
    for layer_idx in range(layers):
        gated = convolution_gate(
            normed(state, gains[layer_idx]), w_conv[layer_idx], dilations[layer_idx]
        )
        summed = conv_share(gated, w_mix[layer_idx], tok_rows)
        share = (share.astype(jnp.float32) + summed).astype(jnp.bfloat16)
        state = ring_gather(share, "head")
    all_rows = state.shape[0]
    attn_in = normed(state, gains[layers])
    qkv_parts = jnp.transpose(w_qkv[:, :, 0, :], (1, 0, 2))
    queries, keys_own, values_own = (
        jnp.dot(attn_in, qkv_parts[i], preferred_element_type=jnp.float32).astype(jnp.bfloat16)
        for i in range(3)
    )
    keys_prev, values_prev = shifted((keys_own, values_own), "blk", 1)
    own_part = attend(queries, keys_own, values_own, True)
    crossing_portion = lax.cond(
        blk_pos > 0,
        lambda: attend(queries, keys_prev, values_prev, False),
        lambda: neutral(all_rows, head_size),
    )
    peak, denom, weighted = combine(own_part, crossing_portion)
    heads_out = (weighted / denom[:, None]).astype(jnp.bfloat16)
    attn_share = attention_portion_for(heads_out, w_out[0], tok_rows)
    return (share.astype(jnp.float32) + attn_share).astype(jnp.bfloat16)


def solution(mesh):
    placed = (
        P(("grp", "blk", "head"), None),
        P(),
        P(),
        P(None, None, None, None, "head"),
        P(None, "head", None),
        P(None, None, "head", None),
        P("head", None, None),
    )
    return jax.shard_map(
        per_device,
        mesh=mesh,
        in_specs=placed,
        out_specs=P(("grp", "blk", "head"), None),
        check_vma=False,
    )
```

```python
import jax
import jax.numpy as jnp
from jax import lax
from jax.sharding import PartitionSpec as P
from jax.experimental import pallas as pl
from jax.experimental.pallas import tpu as pltpu

LARGEST_DILATION = 64


def shifted(value, axis, by):
    length = lax.axis_size(axis)
    pairs = [(i, i + by) for i in range(length) if 0 <= i + by < length]
    return lax.ppermute(value, axis, pairs)


def ring_order(length):
    if length % 2:
        return list(range(length))
    return list(range(0, length, 2)) + list(range(length - 1, 0, -2))


def ring_tables(axis):
    length = lax.axis_size(axis)
    order = ring_order(length)
    place = [0] * length
    for p, h in enumerate(order):
        place[h] = p
    me = jnp.array(place, jnp.int32)[lax.axis_index(axis)]
    return length, order, jnp.array(order, jnp.int32), me


def ring_gather(value, axis):
    length, order, order_arr, me = ring_tables(axis)
    forward = [(order[p], order[(p + 1) % length]) for p in range(length)]
    backward = [(order[p], order[(p - 1) % length]) for p in range(length)]
    ahead = length // 2
    behind = length - 1 - ahead
    rows = value.shape[0]
    out = jnp.zeros((length * rows,) + value.shape[1:], value.dtype)
    out = lax.dynamic_update_slice_in_dim(out, value, order_arr[me] * rows, 0)
    fwd = value
    bwd = value
    for k in range(1, ahead + 1):
        fwd = lax.ppermute(fwd, axis, forward)
        out = lax.dynamic_update_slice_in_dim(out, fwd, order_arr[(me - k) % length] * rows, 0)
        if k <= behind:
            bwd = lax.ppermute(bwd, axis, backward)
            out = lax.dynamic_update_slice_in_dim(out, bwd, order_arr[(me + k) % length] * rows, 0)
    return out


def ring_scatter_sum(value, axis):
    length, order, order_arr, me = ring_tables(axis)
    forward = [(order[p], order[(p + 1) % length]) for p in range(length)]
    backward = [(order[p], order[(p - 1) % length]) for p in range(length)]
    ahead = length // 2
    behind = length - 1 - ahead
    blocks = value.reshape((length, value.shape[0] // length) + value.shape[1:])

    def own(offset):
        return lax.dynamic_index_in_dim(blocks, order_arr[(me + offset) % length], 0, keepdims=False).astype(jnp.float32)

    total = own(0)
    fwd = None
    bwd = None
    for k in range(1, ahead + 1):
        part = own(ahead + 1 - k)
        if fwd is not None:
            part = part + fwd.astype(jnp.float32)
        fwd = lax.ppermute(part.astype(value.dtype), axis, forward)
        if k <= behind:
            part = own(k - behind - 1)
            if bwd is not None:
                part = part + bwd.astype(jnp.float32)
            bwd = lax.ppermute(part.astype(value.dtype), axis, backward)
    total = total + fwd.astype(jnp.float32)
    if bwd is not None:
        total = total + bwd.astype(jnp.float32)
    return total


def normed(values, gain):
    wide = values.astype(jnp.float32)
    scale = lax.rsqrt(jnp.mean(wide * wide, axis=-1, keepdims=True) + 1e-06)
    return (wide * scale * gain).astype(jnp.bfloat16)


def rounded_term(left, right):
    term = jnp.dot(left, right, preferred_element_type=jnp.float32)
    return lax.optimization_barrier(term.astype(jnp.bfloat16)).astype(jnp.float32)


def conv_gate_kernel(slab_ref, weight_ref, out_ref, filt_acc, gate_acc):
    tap = pl.program_id(0)
    chunk = pl.program_id(1)

    @pl.when((tap == 0) & (chunk == 0))
    def _():
        filt_acc[...] = jnp.zeros_like(filt_acc)
        gate_acc[...] = jnp.zeros_like(gate_acc)

    rows = slab_ref[...]
    filt_acc[...] += jnp.dot(rows, weight_ref[0], preferred_element_type=jnp.float32)
    gate_acc[...] += jnp.dot(rows, weight_ref[1], preferred_element_type=jnp.float32)

    @pl.when((tap == pl.num_programs(0) - 1) & (chunk == pl.num_programs(1) - 1))
    def _():
        out_ref[...] = (jnp.tanh(filt_acc[...]) * jax.nn.sigmoid(gate_acc[...])).astype(out_ref.dtype)


def convolution_gate(hidden, conv_by_half, layer_idx, dilation_factor):
    all_rows = hidden.shape[0]
    width = hidden.shape[1]
    taps = conv_by_half.shape[1]
    own_width = conv_by_half.shape[-1]
    border_rows = 2 * LARGEST_DILATION
    before = shifted(hidden[all_rows - border_rows :], "blk", 1)
    padded = jnp.concatenate([before, hidden], axis=0)
    slabs = jnp.stack(
        [
            lax.dynamic_slice_in_dim(padded, border_rows - tap_idx * dilation_factor, all_rows, 0)
            for tap_idx in range(taps)
        ]
    )
    chunk = 1024 if width % 1024 == 0 else width
    return pl.pallas_call(
        conv_gate_kernel,
        out_shape=jax.ShapeDtypeStruct((all_rows, own_width), jnp.bfloat16),
        grid=(taps, width // chunk),
        in_specs=[
            pl.BlockSpec((None, all_rows, chunk), lambda t, k: (t, 0, k)),
            pl.BlockSpec((None, None, 2, chunk, own_width), lambda t, k: (layer_idx, t, 0, k, 0)),
        ],
        out_specs=pl.BlockSpec((all_rows, own_width), lambda t, k: (0, 0)),
        scratch_shapes=[pltpu.VMEM((all_rows, own_width), jnp.float32)] * 2,
        compiler_params=pltpu.CompilerParams(dimension_semantics=("arbitrary", "arbitrary")),
        cost_estimate=pl.CostEstimate(
            flops=4 * taps * all_rows * width * own_width,
            transcendentals=2 * all_rows * own_width,
            bytes_accessed=2 * taps * (all_rows * width + 2 * width * own_width + all_rows * own_width // taps),
        ),
    )(slabs, conv_by_half)


def conv_share(gated, weight, tok_rows):

    def term(start, count):
        return rounded_term(gated, weight)

    return ring_scatter_sum(
        term(jnp.int32(0), tok_rows * lax.axis_size("head")).astype(jnp.bfloat16), "head"
    )


def attention_portion_for(heads_out, out_block, tok_rows):

    def term(start, count):
        return rounded_term(heads_out, out_block)

    return ring_scatter_sum(
        term(jnp.int32(0), tok_rows * lax.axis_size("head")).astype(jnp.bfloat16), "head"
    )


def attend(queries, keys_in, values_in, causal):
    scale = queries.shape[1] ** (-0.5)
    scores = jnp.einsum("qd,kd->qk", queries, keys_in, preferred_element_type=jnp.float32) * scale
    if causal:
        rows_q = lax.broadcasted_iota(jnp.int32, scores.shape, 0)
        rows_k = lax.broadcasted_iota(jnp.int32, scores.shape, 1)
        scores = jnp.where(rows_q >= rows_k, scores, -1e30)
    peak = jnp.max(scores, axis=1)
    probs = jnp.exp(scores - peak[:, None])
    denom = jnp.sum(probs, axis=1)
    weighted = jnp.dot(probs.astype(jnp.bfloat16), values_in, preferred_element_type=jnp.float32)
    return (peak, denom, weighted)


def neutral(count, head_size):
    return (
        jnp.full((count,), -1e30, jnp.float32),
        jnp.zeros((count,), jnp.float32),
        jnp.zeros((count, head_size), jnp.float32),
    )


def combine(first, second):
    peak = jnp.maximum(first[0], second[0])
    scale_one = jnp.exp(first[0] - peak)
    scale_two = jnp.exp(second[0] - peak)
    denom = first[1] * scale_one + second[1] * scale_two
    weighted = first[2] * scale_one[:, None] + second[2] * scale_two[:, None]
    return (peak, denom, weighted)


def per_device(stream, gains, dilations, w_conv, w_mix, w_qkv, w_out):
    blk_pos = lax.axis_index("blk")
    tok_rows = stream.shape[0]
    width = stream.shape[1]
    head_size = w_qkv.shape[3]
    layers = w_conv.shape[0]
    share = stream
    state = ring_gather(stream, "head")
    conv_by_half = jnp.transpose(w_conv, (0, 1, 3, 2, 4))
    for layer_idx in range(layers):
        gated = convolution_gate(
            normed(state, gains[layer_idx]), conv_by_half, layer_idx, dilations[layer_idx]
        )
        summed = conv_share(gated, w_mix[layer_idx], tok_rows)
        share = (share.astype(jnp.float32) + summed).astype(jnp.bfloat16)
        state = ring_gather(share, "head")
    all_rows = state.shape[0]
    attn_in = normed(state, gains[layers])
    qkv_parts = jnp.transpose(w_qkv[:, :, 0, :], (1, 0, 2))
    queries, keys_own, values_own = (
        jnp.dot(attn_in, qkv_parts[i], preferred_element_type=jnp.float32).astype(jnp.bfloat16)
        for i in range(3)
    )
    keys_prev, values_prev = shifted((keys_own, values_own), "blk", 1)
    own_part = attend(queries, keys_own, values_own, True)
    crossing_portion = lax.cond(
        blk_pos > 0,
        lambda: attend(queries, keys_prev, values_prev, False),
        lambda: neutral(all_rows, head_size),
    )
    peak, denom, weighted = combine(own_part, crossing_portion)
    heads_out = (weighted / denom[:, None]).astype(jnp.bfloat16)
    attn_share = attention_portion_for(heads_out, w_out[0], tok_rows)
    return (share.astype(jnp.float32) + attn_share).astype(jnp.bfloat16)


def solution(mesh):
    placed = (
        P(("grp", "blk", "head"), None),
        P(),
        P(),
        P(None, None, None, None, "head"),
        P(None, "head", None),
        P(None, None, "head", None),
        P("head", None, None),
    )
    return jax.shard_map(
        per_device,
        mesh=mesh,
        in_specs=placed,
        out_specs=P(("grp", "blk", "head"), None),
        check_vma=False,
    )
```

```python
import jax
import jax.numpy as jnp
from jax import lax
from jax.sharding import PartitionSpec as P
from jax.experimental import pallas as pl
from jax.experimental.pallas import tpu as pltpu

LARGEST_DILATION = 64


def shifted(value, axis, by):
    length = lax.axis_size(axis)
    pairs = [(i, i + by) for i in range(length) if 0 <= i + by < length]
    return lax.ppermute(value, axis, pairs)


def ring_order(length):
    if length % 2:
        return list(range(length))
    return list(range(0, length, 2)) + list(range(length - 1, 0, -2))


def ring_tables(axis):
    length = lax.axis_size(axis)
    order = ring_order(length)
    place = [0] * length
    for p, h in enumerate(order):
        place[h] = p
    me = jnp.array(place, jnp.int32)[lax.axis_index(axis)]
    return length, order, jnp.array(order, jnp.int32), me


def ring_gather(value, axis):
    length, order, order_arr, me = ring_tables(axis)
    forward = [(order[p], order[(p + 1) % length]) for p in range(length)]
    backward = [(order[p], order[(p - 1) % length]) for p in range(length)]
    ahead = length // 2
    behind = length - 1 - ahead
    rows = value.shape[0]
    split = behind < ahead and rows % 2 == 0
    half = rows // 2
    out = jnp.zeros((length * rows,) + value.shape[1:], value.dtype)
    out = lax.dynamic_update_slice_in_dim(out, value, order_arr[me] * rows, 0)
    fwd = value
    bwd = value
    for k in range(1, ahead + 1):
        if k == ahead and split:
            fwd = lax.ppermute(fwd[:half], axis, forward)
            bwd = lax.ppermute(bwd[half:], axis, backward)
            far = order_arr[(me - k) % length] * rows
            out = lax.dynamic_update_slice_in_dim(out, fwd, far, 0)
            out = lax.dynamic_update_slice_in_dim(out, bwd, far + half, 0)
            break
        fwd = lax.ppermute(fwd, axis, forward)
        out = lax.dynamic_update_slice_in_dim(out, fwd, order_arr[(me - k) % length] * rows, 0)
        if k <= behind:
            bwd = lax.ppermute(bwd, axis, backward)
            out = lax.dynamic_update_slice_in_dim(out, bwd, order_arr[(me + k) % length] * rows, 0)
    return out


def ring_scatter_sum(value, axis):
    length, order, order_arr, me = ring_tables(axis)
    forward = [(order[p], order[(p + 1) % length]) for p in range(length)]
    backward = [(order[p], order[(p - 1) % length]) for p in range(length)]
    ahead = length // 2
    behind = length - 1 - ahead
    rows = value.shape[0] // length
    split = behind < ahead and rows % 2 == 0
    half = rows // 2
    blocks = value.reshape((length, rows) + value.shape[1:])

    def own(offset):
        return lax.dynamic_index_in_dim(blocks, order_arr[(me + offset) % length], 0, keepdims=False).astype(jnp.float32)

    def chain(offsets, pairs, first_rows):
        passed = None
        for step, offset in enumerate(offsets):
            part = own(offset)
            if step == 0:
                part = part[first_rows]
            elif step == 1 and passed.shape[0] != rows:
                part = part.at[first_rows].add(passed.astype(jnp.float32))
            else:
                part = part + passed.astype(jnp.float32)
            passed = lax.ppermute(part.astype(value.dtype), axis, pairs)
        return passed

    fwd_offsets = list(range(ahead, 0, -1))
    bwd_offsets = list(range(-behind, 0))
    fwd_rows = slice(0, rows)
    bwd_rows = slice(0, rows)
    if split:
        bwd_offsets = [-ahead] + bwd_offsets
        fwd_rows = slice(0, half)
        bwd_rows = slice(half, rows)
    total = own(0)
    total = total + chain(fwd_offsets, forward, fwd_rows).astype(jnp.float32)
    if bwd_offsets:
        total = total + chain(bwd_offsets, backward, bwd_rows).astype(jnp.float32)
    return total


def normed(values, gain):
    wide = values.astype(jnp.float32)
    scale = lax.rsqrt(jnp.mean(wide * wide, axis=-1, keepdims=True) + 1e-06)
    return (wide * scale * gain).astype(jnp.bfloat16)


def rounded_term(left, right):
    term = jnp.dot(left, right, preferred_element_type=jnp.float32)
    return lax.optimization_barrier(term.astype(jnp.bfloat16)).astype(jnp.float32)


def conv_gate_kernel(slab_ref, weight_ref, out_ref, filt_acc, gate_acc):
    tap = pl.program_id(0)
    chunk = pl.program_id(1)

    @pl.when((tap == 0) & (chunk == 0))
    def _():
        filt_acc[...] = jnp.zeros_like(filt_acc)
        gate_acc[...] = jnp.zeros_like(gate_acc)

    rows = slab_ref[...]
    filt_acc[...] += jnp.dot(rows, weight_ref[0], preferred_element_type=jnp.float32)
    gate_acc[...] += jnp.dot(rows, weight_ref[1], preferred_element_type=jnp.float32)

    @pl.when((tap == pl.num_programs(0) - 1) & (chunk == pl.num_programs(1) - 1))
    def _():
        out_ref[...] = (jnp.tanh(filt_acc[...]) * jax.nn.sigmoid(gate_acc[...])).astype(out_ref.dtype)


def convolution_gate(hidden, conv_by_half, layer_idx, dilation_factor):
    all_rows = hidden.shape[0]
    width = hidden.shape[1]
    taps = conv_by_half.shape[1]
    own_width = conv_by_half.shape[-1]
    border_rows = 2 * LARGEST_DILATION
    before = shifted(hidden[all_rows - border_rows :], "blk", 1)
    padded = jnp.concatenate([before, hidden], axis=0)
    slabs = jnp.stack(
        [
            lax.dynamic_slice_in_dim(padded, border_rows - tap_idx * dilation_factor, all_rows, 0)
            for tap_idx in range(taps)
        ]
    )
    chunk = 1024 if width % 1024 == 0 else width
    return pl.pallas_call(
        conv_gate_kernel,
        out_shape=jax.ShapeDtypeStruct((all_rows, own_width), jnp.bfloat16),
        grid=(taps, width // chunk),
        in_specs=[
            pl.BlockSpec((None, all_rows, chunk), lambda t, k: (t, 0, k)),
            pl.BlockSpec((None, None, 2, chunk, own_width), lambda t, k: (layer_idx, t, 0, k, 0)),
        ],
        out_specs=pl.BlockSpec((all_rows, own_width), lambda t, k: (0, 0)),
        scratch_shapes=[pltpu.VMEM((all_rows, own_width), jnp.float32)] * 2,
        compiler_params=pltpu.CompilerParams(dimension_semantics=("arbitrary", "arbitrary")),
        cost_estimate=pl.CostEstimate(
            flops=4 * taps * all_rows * width * own_width,
            transcendentals=2 * all_rows * own_width,
            bytes_accessed=2 * taps * (all_rows * width + 2 * width * own_width + all_rows * own_width // taps),
        ),
    )(slabs, conv_by_half)


def conv_share(gated, weight, tok_rows):

    def term(start, count):
        return rounded_term(gated, weight)

    return ring_scatter_sum(
        term(jnp.int32(0), tok_rows * lax.axis_size("head")).astype(jnp.bfloat16), "head"
    )


def attention_portion_for(heads_out, out_block, tok_rows):

    def term(start, count):
        return rounded_term(heads_out, out_block)

    return ring_scatter_sum(
        term(jnp.int32(0), tok_rows * lax.axis_size("head")).astype(jnp.bfloat16), "head"
    )


def attend(queries, keys_in, values_in, causal):
    scale = queries.shape[1] ** (-0.5)
    scores = jnp.einsum("qd,kd->qk", queries, keys_in, preferred_element_type=jnp.float32) * scale
    if causal:
        rows_q = lax.broadcasted_iota(jnp.int32, scores.shape, 0)
        rows_k = lax.broadcasted_iota(jnp.int32, scores.shape, 1)
        scores = jnp.where(rows_q >= rows_k, scores, -1e30)
    peak = jnp.max(scores, axis=1)
    probs = jnp.exp(scores - peak[:, None])
    denom = jnp.sum(probs, axis=1)
    weighted = jnp.dot(probs.astype(jnp.bfloat16), values_in, preferred_element_type=jnp.float32)
    return (peak, denom, weighted)


def neutral(count, head_size):
    return (
        jnp.full((count,), -1e30, jnp.float32),
        jnp.zeros((count,), jnp.float32),
        jnp.zeros((count, head_size), jnp.float32),
    )


def combine(first, second):
    peak = jnp.maximum(first[0], second[0])
    scale_one = jnp.exp(first[0] - peak)
    scale_two = jnp.exp(second[0] - peak)
    denom = first[1] * scale_one + second[1] * scale_two
    weighted = first[2] * scale_one[:, None] + second[2] * scale_two[:, None]
    return (peak, denom, weighted)


def per_device(stream, gains, dilations, w_conv, w_mix, w_qkv, w_out):
    blk_pos = lax.axis_index("blk")
    tok_rows = stream.shape[0]
    width = stream.shape[1]
    head_size = w_qkv.shape[3]
    layers = w_conv.shape[0]
    share = stream
    state = ring_gather(stream, "head")
    conv_by_half = jnp.transpose(w_conv, (0, 1, 3, 2, 4))
    for layer_idx in range(layers):
        gated = convolution_gate(
            normed(state, gains[layer_idx]), conv_by_half, layer_idx, dilations[layer_idx]
        )
        summed = conv_share(gated, w_mix[layer_idx], tok_rows)
        share = (share.astype(jnp.float32) + summed).astype(jnp.bfloat16)
        state = ring_gather(share, "head")
    all_rows = state.shape[0]
    attn_in = normed(state, gains[layers])
    qkv_parts = jnp.transpose(w_qkv[:, :, 0, :], (1, 0, 2))
    queries, keys_own, values_own = (
        jnp.dot(attn_in, qkv_parts[i], preferred_element_type=jnp.float32).astype(jnp.bfloat16)
        for i in range(3)
    )
    keys_prev, values_prev = shifted((keys_own, values_own), "blk", 1)
    own_part = attend(queries, keys_own, values_own, True)
    crossing_portion = lax.cond(
        blk_pos > 0,
        lambda: attend(queries, keys_prev, values_prev, False),
        lambda: neutral(all_rows, head_size),
    )
    peak, denom, weighted = combine(own_part, crossing_portion)
    heads_out = (weighted / denom[:, None]).astype(jnp.bfloat16)
    attn_share = attention_portion_for(heads_out, w_out[0], tok_rows)
    return (share.astype(jnp.float32) + attn_share).astype(jnp.bfloat16)


def solution(mesh):
    placed = (
        P(("grp", "blk", "head"), None),
        P(),
        P(),
        P(None, None, None, None, "head"),
        P(None, "head", None),
        P(None, None, "head", None),
        P("head", None, None),
    )
    return jax.shard_map(
        per_device,
        mesh=mesh,
        in_specs=placed,
        out_specs=P(("grp", "blk", "head"), None),
        check_vma=False,
    )
```

```python
import jax
import jax.numpy as jnp
from jax import lax
from jax.sharding import PartitionSpec as P
from jax.experimental import pallas as pl
from jax.experimental.pallas import tpu as pltpu

LARGEST_DILATION = 64


def shifted(value, axis, by):
    length = lax.axis_size(axis)
    pairs = [(i, i + by) for i in range(length) if 0 <= i + by < length]
    return lax.ppermute(value, axis, pairs)


def ring_order(length):
    if length % 2:
        return list(range(length))
    return list(range(0, length, 2)) + list(range(length - 1, 0, -2))


def ring_tables(axis):
    length = lax.axis_size(axis)
    order = ring_order(length)
    place = [0] * length
    for p, h in enumerate(order):
        place[h] = p
    head_at = [[order[(place[h] + m) % length] for m in range(length)] for h in range(length)]
    offset_of = [[(place[j] - place[h]) % length for j in range(length)] for h in range(length)]
    table = jnp.array([head_at, offset_of], jnp.int32)
    mine = lax.dynamic_index_in_dim(table, lax.axis_index(axis), 1, keepdims=False)
    return mine[0], mine[1]


def ring_pairs(length):
    order = ring_order(length)
    forward = [(order[p], order[(p + 1) % length]) for p in range(length)]
    backward = [(order[p], order[(p - 1) % length]) for p in range(length)]
    return forward, backward


def ring_gather(value, axis, tables):
    length = lax.axis_size(axis)
    forward, backward = ring_pairs(length)
    ahead = length // 2
    behind = length - 1 - ahead
    rows = value.shape[0]
    split = behind < ahead and rows % 2 == 0
    half = rows // 2
    pieces = [None] * length
    pieces[0] = value
    fwd = value
    bwd = value
    for k in range(1, ahead + 1):
        if k == ahead and split:
            fwd = lax.ppermute(fwd[:half], axis, forward)
            bwd = lax.ppermute(bwd[half:], axis, backward)
            pieces[k] = jnp.concatenate([fwd, bwd], axis=0)
            break
        fwd = lax.ppermute(fwd, axis, forward)
        pieces[length - k] = fwd
        if k <= behind:
            bwd = lax.ppermute(bwd, axis, backward)
            pieces[k] = bwd
    stacked = jnp.stack(pieces)
    return jnp.take(stacked, tables[1], axis=0, mode="clip").reshape((length * rows,) + value.shape[1:])


def ring_scatter_sum(value, axis, tables):
    length = lax.axis_size(axis)
    forward, backward = ring_pairs(length)
    ahead = length // 2
    behind = length - 1 - ahead
    rows = value.shape[0] // length
    split = behind < ahead and rows % 2 == 0
    half = rows // 2
    blocks = value.reshape((length, rows) + value.shape[1:])
    by_offset = jnp.take(blocks, tables[0], axis=0, mode="clip")

    def own(offset):
        return by_offset[offset % length].astype(jnp.float32)

    def chain(offsets, pairs, first_rows):
        passed = None
        for step, offset in enumerate(offsets):
            part = own(offset)
            if step == 0:
                part = part[first_rows]
            elif step == 1 and passed.shape[0] != rows:
                part = part.at[first_rows].add(passed.astype(jnp.float32))
            else:
                part = part + passed.astype(jnp.float32)
            passed = lax.ppermute(part.astype(value.dtype), axis, pairs)
        return passed

    fwd_offsets = list(range(ahead, 0, -1))
    bwd_offsets = list(range(-behind, 0))
    fwd_rows = slice(0, rows)
    bwd_rows = slice(0, rows)
    if split:
        bwd_offsets = [-ahead] + bwd_offsets
        fwd_rows = slice(0, half)
        bwd_rows = slice(half, rows)
    total = own(0)
    total = total + chain(fwd_offsets, forward, fwd_rows).astype(jnp.float32)
    if bwd_offsets:
        total = total + chain(bwd_offsets, backward, bwd_rows).astype(jnp.float32)
    return total


def normed(values, gain):
    wide = values.astype(jnp.float32)
    scale = lax.rsqrt(jnp.mean(wide * wide, axis=-1, keepdims=True) + 1e-06)
    return (wide * scale * gain).astype(jnp.bfloat16)


def rounded_term(left, right):
    term = jnp.dot(left, right, preferred_element_type=jnp.float32)
    return lax.optimization_barrier(term.astype(jnp.bfloat16)).astype(jnp.float32)


def conv_gate_kernel(slab_ref, weight_ref, out_ref, filt_acc, gate_acc):
    tap = pl.program_id(0)
    chunk = pl.program_id(1)

    @pl.when((tap == 0) & (chunk == 0))
    def _():
        filt_acc[...] = jnp.zeros_like(filt_acc)
        gate_acc[...] = jnp.zeros_like(gate_acc)

    rows = slab_ref[...]
    filt_acc[...] += jnp.dot(rows, weight_ref[0], preferred_element_type=jnp.float32)
    gate_acc[...] += jnp.dot(rows, weight_ref[1], preferred_element_type=jnp.float32)

    @pl.when((tap == pl.num_programs(0) - 1) & (chunk == pl.num_programs(1) - 1))
    def _():
        out_ref[...] = (jnp.tanh(filt_acc[...]) * jax.nn.sigmoid(gate_acc[...])).astype(out_ref.dtype)


def convolution_gate(hidden, conv_by_half, layer_idx, dilation_factor):
    all_rows = hidden.shape[0]
    width = hidden.shape[1]
    taps = conv_by_half.shape[1]
    own_width = conv_by_half.shape[-1]
    border_rows = 2 * LARGEST_DILATION
    before = shifted(hidden[all_rows - border_rows :], "blk", 1)
    padded = jnp.concatenate([before, hidden], axis=0)
    slabs = jnp.stack(
        [
            lax.dynamic_slice_in_dim(padded, border_rows - tap_idx * dilation_factor, all_rows, 0)
            for tap_idx in range(taps)
        ]
    )
    chunk = 1024 if width % 1024 == 0 else width
    return pl.pallas_call(
        conv_gate_kernel,
        out_shape=jax.ShapeDtypeStruct((all_rows, own_width), jnp.bfloat16),
        grid=(taps, width // chunk),
        in_specs=[
            pl.BlockSpec((None, all_rows, chunk), lambda t, k: (t, 0, k)),
            pl.BlockSpec((None, None, 2, chunk, own_width), lambda t, k: (layer_idx, t, 0, k, 0)),
        ],
        out_specs=pl.BlockSpec((all_rows, own_width), lambda t, k: (0, 0)),
        scratch_shapes=[pltpu.VMEM((all_rows, own_width), jnp.float32)] * 2,
        compiler_params=pltpu.CompilerParams(dimension_semantics=("arbitrary", "arbitrary")),
        cost_estimate=pl.CostEstimate(
            flops=4 * taps * all_rows * width * own_width,
            transcendentals=2 * all_rows * own_width,
            bytes_accessed=2 * taps * (all_rows * width + 2 * width * own_width + all_rows * own_width // taps),
        ),
    )(slabs, conv_by_half)


def conv_share(gated, weight, tok_rows, tables):

    def term(start, count):
        return rounded_term(gated, weight)

    return ring_scatter_sum(
        term(jnp.int32(0), tok_rows * lax.axis_size("head")).astype(jnp.bfloat16), "head", tables
    )


def attention_portion_for(heads_out, out_block, tok_rows, tables):

    def term(start, count):
        return rounded_term(heads_out, out_block)

    return ring_scatter_sum(
        term(jnp.int32(0), tok_rows * lax.axis_size("head")).astype(jnp.bfloat16), "head", tables
    )


def attend(queries, keys_in, values_in, causal):
    scale = queries.shape[1] ** (-0.5)
    scores = jnp.einsum("qd,kd->qk", queries, keys_in, preferred_element_type=jnp.float32) * scale
    if causal:
        rows_q = lax.broadcasted_iota(jnp.int32, scores.shape, 0)
        rows_k = lax.broadcasted_iota(jnp.int32, scores.shape, 1)
        scores = jnp.where(rows_q >= rows_k, scores, -1e30)
    peak = jnp.max(scores, axis=1)
    probs = jnp.exp(scores - peak[:, None])
    denom = jnp.sum(probs, axis=1)
    weighted = jnp.dot(probs.astype(jnp.bfloat16), values_in, preferred_element_type=jnp.float32)
    return (peak, denom, weighted)


def neutral(count, head_size):
    return (
        jnp.full((count,), -1e30, jnp.float32),
        jnp.zeros((count,), jnp.float32),
        jnp.zeros((count, head_size), jnp.float32),
    )


def combine(first, second):
    peak = jnp.maximum(first[0], second[0])
    scale_one = jnp.exp(first[0] - peak)
    scale_two = jnp.exp(second[0] - peak)
    denom = first[1] * scale_one + second[1] * scale_two
    weighted = first[2] * scale_one[:, None] + second[2] * scale_two[:, None]
    return (peak, denom, weighted)


def per_device(stream, gains, dilations, w_conv, w_mix, w_qkv, w_out):
    blk_pos = lax.axis_index("blk")
    tok_rows = stream.shape[0]
    width = stream.shape[1]
    head_size = w_qkv.shape[3]
    layers = w_conv.shape[0]
    share = stream
    tables = ring_tables("head")
    state = ring_gather(stream, "head", tables)
    conv_by_half = jnp.transpose(w_conv, (0, 1, 3, 2, 4))
    for layer_idx in range(layers):
        gated = convolution_gate(
            normed(state, gains[layer_idx]), conv_by_half, layer_idx, dilations[layer_idx]
        )
        summed = conv_share(gated, w_mix[layer_idx], tok_rows, tables)
        share = (share.astype(jnp.float32) + summed).astype(jnp.bfloat16)
        state = ring_gather(share, "head", tables)
    all_rows = state.shape[0]
    attn_in = normed(state, gains[layers])
    qkv_parts = jnp.transpose(w_qkv[:, :, 0, :], (1, 0, 2))
    queries, keys_own, values_own = (
        jnp.dot(attn_in, qkv_parts[i], preferred_element_type=jnp.float32).astype(jnp.bfloat16)
        for i in range(3)
    )
    keys_prev, values_prev = shifted((keys_own, values_own), "blk", 1)
    own_part = attend(queries, keys_own, values_own, True)
    crossing_portion = lax.cond(
        blk_pos > 0,
        lambda: attend(queries, keys_prev, values_prev, False),
        lambda: neutral(all_rows, head_size),
    )
    peak, denom, weighted = combine(own_part, crossing_portion)
    heads_out = (weighted / denom[:, None]).astype(jnp.bfloat16)
    attn_share = attention_portion_for(heads_out, w_out[0], tok_rows, tables)
    return (share.astype(jnp.float32) + attn_share).astype(jnp.bfloat16)


def solution(mesh):
    placed = (
        P(("grp", "blk", "head"), None),
        P(),
        P(),
        P(None, None, None, None, "head"),
        P(None, "head", None),
        P(None, None, "head", None),
        P("head", None, None),
    )
    return jax.shard_map(
        per_device,
        mesh=mesh,
        in_specs=placed,
        out_specs=P(("grp", "blk", "head"), None),
        check_vma=False,
    )
```

```python
import jax
import jax.numpy as jnp
from jax import lax
from jax.sharding import PartitionSpec as P
from jax.experimental import pallas as pl
from jax.experimental.pallas import tpu as pltpu

LARGEST_DILATION = 64


def shifted(value, axis, by):
    length = lax.axis_size(axis)
    pairs = [(i, i + by) for i in range(length) if 0 <= i + by < length]
    return lax.ppermute(value, axis, pairs)


def ring_order(length):
    if length % 2:
        return list(range(length))
    return list(range(0, length, 2)) + list(range(length - 1, 0, -2))


def ring_tables(axis):
    length = lax.axis_size(axis)
    order = ring_order(length)
    place = [0] * length
    for p, h in enumerate(order):
        place[h] = p
    head_at = [[order[(place[h] + m) % length] for m in range(length)] for h in range(length)]
    offset_of = [[(place[j] - place[h]) % length for j in range(length)] for h in range(length)]
    table = jnp.array([head_at, offset_of], jnp.int32)
    mine = lax.dynamic_index_in_dim(table, lax.axis_index(axis), 1, keepdims=False)
    return mine[0], mine[1]


def ring_pairs(length):
    order = ring_order(length)
    forward = [(order[p], order[(p + 1) % length]) for p in range(length)]
    backward = [(order[p], order[(p - 1) % length]) for p in range(length)]
    return forward, backward


def ring_gather(value, axis, tables):
    length = lax.axis_size(axis)
    forward, backward = ring_pairs(length)
    ahead = length // 2
    behind = length - 1 - ahead
    rows = value.shape[0]
    split = behind < ahead and rows % 2 == 0
    half = rows // 2
    pieces = [None] * length
    pieces[0] = value
    fwd = value
    bwd = value
    for k in range(1, ahead + 1):
        if k == ahead and split:
            fwd = lax.ppermute(fwd[:half], axis, forward)
            bwd = lax.ppermute(bwd[half:], axis, backward)
            pieces[k] = jnp.concatenate([fwd, bwd], axis=0)
            break
        fwd = lax.ppermute(fwd, axis, forward)
        pieces[length - k] = fwd
        if k <= behind:
            bwd = lax.ppermute(bwd, axis, backward)
            pieces[k] = bwd
    stacked = jnp.stack(pieces)
    return jnp.take(stacked, tables[1], axis=0, mode="clip").reshape((length * rows,) + value.shape[1:])


def ring_scatter_sum(value, axis, tables):
    length = lax.axis_size(axis)
    forward, backward = ring_pairs(length)
    ahead = length // 2
    behind = length - 1 - ahead
    rows = value.shape[0] // length
    split = behind < ahead and rows % 2 == 0
    half = rows // 2
    blocks = value.reshape((length, rows) + value.shape[1:])
    by_offset = jnp.take(blocks, tables[0], axis=0, mode="clip")

    def own(offset):
        return by_offset[offset % length].astype(jnp.float32)

    def chain(offsets, pairs, first_rows):
        passed = None
        for step, offset in enumerate(offsets):
            part = own(offset)
            if step == 0:
                part = part[first_rows]
            elif step == 1 and passed.shape[0] != rows:
                part = part.at[first_rows].add(passed.astype(jnp.float32))
            else:
                part = part + passed.astype(jnp.float32)
            passed = lax.ppermute(part.astype(value.dtype), axis, pairs)
        return passed

    fwd_offsets = list(range(ahead, 0, -1))
    bwd_offsets = list(range(-behind, 0))
    fwd_rows = slice(0, rows)
    bwd_rows = slice(0, rows)
    if split:
        bwd_offsets = [-ahead] + bwd_offsets
        fwd_rows = slice(0, half)
        bwd_rows = slice(half, rows)
    total = own(0)
    total = total + chain(fwd_offsets, forward, fwd_rows).astype(jnp.float32)
    if bwd_offsets:
        total = total + chain(bwd_offsets, backward, bwd_rows).astype(jnp.float32)
    return total


def normed(values, gain):
    wide = values.astype(jnp.float32)
    scale = lax.rsqrt(jnp.mean(wide * wide, axis=-1, keepdims=True) + 1e-06)
    return (wide * scale * gain).astype(jnp.bfloat16)


def rounded_term(left, right):
    term = jnp.dot(left, right, preferred_element_type=jnp.float32)
    return lax.optimization_barrier(term.astype(jnp.bfloat16)).astype(jnp.float32)


def conv_gate_kernel(slab_ref, weight_ref, out_ref, filt_acc, gate_acc):
    tap = pl.program_id(0)
    chunk = pl.program_id(1)

    @pl.when((tap == 0) & (chunk == 0))
    def _():
        filt_acc[...] = jnp.zeros_like(filt_acc)
        gate_acc[...] = jnp.zeros_like(gate_acc)

    rows = slab_ref[...]
    weight = weight_ref[...]
    filt_acc[...] += jnp.dot(rows, weight[:, 0, :], preferred_element_type=jnp.float32)
    gate_acc[...] += jnp.dot(rows, weight[:, 1, :], preferred_element_type=jnp.float32)

    @pl.when((tap == pl.num_programs(0) - 1) & (chunk == pl.num_programs(1) - 1))
    def _():
        out_ref[...] = (jnp.tanh(filt_acc[...]) * jax.nn.sigmoid(gate_acc[...])).astype(out_ref.dtype)


def convolution_gate(hidden, kernel, layer_idx, dilation_factor):
    all_rows = hidden.shape[0]
    width = hidden.shape[1]
    taps = kernel.shape[1]
    own_width = kernel.shape[-1]
    border_rows = 2 * LARGEST_DILATION
    before = shifted(hidden[all_rows - border_rows :], "blk", 1)
    padded = jnp.concatenate([before, hidden], axis=0)
    slabs = jnp.stack(
        [
            lax.dynamic_slice_in_dim(padded, border_rows - tap_idx * dilation_factor, all_rows, 0)
            for tap_idx in range(taps)
        ]
    )
    chunk = 512 if width % 512 == 0 else width
    return pl.pallas_call(
        conv_gate_kernel,
        out_shape=jax.ShapeDtypeStruct((all_rows, own_width), jnp.bfloat16),
        grid=(taps, width // chunk),
        in_specs=[
            pl.BlockSpec((None, all_rows, chunk), lambda t, k: (t, 0, k)),
            pl.BlockSpec((None, None, chunk, 2, own_width), lambda t, k: (layer_idx, t, k, 0, 0)),
        ],
        out_specs=pl.BlockSpec((all_rows, own_width), lambda t, k: (0, 0)),
        scratch_shapes=[pltpu.VMEM((all_rows, own_width), jnp.float32)] * 2,
        compiler_params=pltpu.CompilerParams(dimension_semantics=("arbitrary", "arbitrary")),
        cost_estimate=pl.CostEstimate(
            flops=4 * taps * all_rows * width * own_width,
            transcendentals=2 * all_rows * own_width,
            bytes_accessed=2 * taps * (all_rows * width + 2 * width * own_width + all_rows * own_width // taps),
        ),
    )(slabs, kernel)


def conv_share(gated, weight, tok_rows, tables):

    def term(start, count):
        return rounded_term(gated, weight)

    return ring_scatter_sum(
        term(jnp.int32(0), tok_rows * lax.axis_size("head")).astype(jnp.bfloat16), "head", tables
    )


def attention_portion_for(heads_out, out_block, tok_rows, tables):

    def term(start, count):
        return rounded_term(heads_out, out_block)

    return ring_scatter_sum(
        term(jnp.int32(0), tok_rows * lax.axis_size("head")).astype(jnp.bfloat16), "head", tables
    )


def attend(queries, keys_in, values_in, causal):
    scale = queries.shape[1] ** (-0.5)
    scores = jnp.einsum("qd,kd->qk", queries, keys_in, preferred_element_type=jnp.float32) * scale
    if causal:
        rows_q = lax.broadcasted_iota(jnp.int32, scores.shape, 0)
        rows_k = lax.broadcasted_iota(jnp.int32, scores.shape, 1)
        scores = jnp.where(rows_q >= rows_k, scores, -1e30)
    peak = jnp.max(scores, axis=1)
    probs = jnp.exp(scores - peak[:, None])
    denom = jnp.sum(probs, axis=1)
    weighted = jnp.dot(probs.astype(jnp.bfloat16), values_in, preferred_element_type=jnp.float32)
    return (peak, denom, weighted)


def neutral(count, head_size):
    return (
        jnp.full((count,), -1e30, jnp.float32),
        jnp.zeros((count,), jnp.float32),
        jnp.zeros((count, head_size), jnp.float32),
    )


def combine(first, second):
    peak = jnp.maximum(first[0], second[0])
    scale_one = jnp.exp(first[0] - peak)
    scale_two = jnp.exp(second[0] - peak)
    denom = first[1] * scale_one + second[1] * scale_two
    weighted = first[2] * scale_one[:, None] + second[2] * scale_two[:, None]
    return (peak, denom, weighted)


def per_device(stream, gains, dilations, w_conv, w_mix, w_qkv, w_out):
    blk_pos = lax.axis_index("blk")
    tok_rows = stream.shape[0]
    width = stream.shape[1]
    head_size = w_qkv.shape[3]
    layers = w_conv.shape[0]
    share = stream
    tables = ring_tables("head")
    state = ring_gather(stream, "head", tables)
    for layer_idx in range(layers):
        gated = convolution_gate(
            normed(state, gains[layer_idx]), w_conv, layer_idx, dilations[layer_idx]
        )
        summed = conv_share(gated, w_mix[layer_idx], tok_rows, tables)
        share = (share.astype(jnp.float32) + summed).astype(jnp.bfloat16)
        state = ring_gather(share, "head", tables)
    all_rows = state.shape[0]
    attn_in = normed(state, gains[layers])
    qkv_parts = jnp.transpose(w_qkv[:, :, 0, :], (1, 0, 2))
    queries, keys_own, values_own = (
        jnp.dot(attn_in, qkv_parts[i], preferred_element_type=jnp.float32).astype(jnp.bfloat16)
        for i in range(3)
    )
    keys_prev, values_prev = shifted((keys_own, values_own), "blk", 1)
    own_part = attend(queries, keys_own, values_own, True)
    crossing_portion = lax.cond(
        blk_pos > 0,
        lambda: attend(queries, keys_prev, values_prev, False),
        lambda: neutral(all_rows, head_size),
    )
    peak, denom, weighted = combine(own_part, crossing_portion)
    heads_out = (weighted / denom[:, None]).astype(jnp.bfloat16)
    attn_share = attention_portion_for(heads_out, w_out[0], tok_rows, tables)
    return (share.astype(jnp.float32) + attn_share).astype(jnp.bfloat16)


def solution(mesh):
    placed = (
        P(("grp", "blk", "head"), None),
        P(),
        P(),
        P(None, None, None, None, "head"),
        P(None, "head", None),
        P(None, None, "head", None),
        P("head", None, None),
    )
    return jax.shard_map(
        per_device,
        mesh=mesh,
        in_specs=placed,
        out_specs=P(("grp", "blk", "head"), None),
        check_vma=False,
    )
```

```python
import jax
import jax.numpy as jnp
from jax import lax
from jax.sharding import PartitionSpec as P
from jax.experimental import pallas as pl
from jax.experimental.pallas import tpu as pltpu

LARGEST_DILATION = 64


def shifted(value, axis, by):
    length = lax.axis_size(axis)
    pairs = [(i, i + by) for i in range(length) if 0 <= i + by < length]
    return lax.ppermute(value, axis, pairs)


def ring_order(length):
    if length % 2:
        return list(range(length))
    return list(range(0, length, 2)) + list(range(length - 1, 0, -2))


def ring_tables(axis):
    length = lax.axis_size(axis)
    order = ring_order(length)
    place = [0] * length
    for p, h in enumerate(order):
        place[h] = p
    head_at = [[order[(place[h] + m) % length] for m in range(length)] for h in range(length)]
    offset_of = [[(place[j] - place[h]) % length for j in range(length)] for h in range(length)]
    table = jnp.array([head_at, offset_of], jnp.int32)
    mine = lax.dynamic_index_in_dim(table, lax.axis_index(axis), 1, keepdims=False)
    return mine[0], mine[1]


def ring_pairs(length):
    order = ring_order(length)
    forward = [(order[p], order[(p + 1) % length]) for p in range(length)]
    backward = [(order[p], order[(p - 1) % length]) for p in range(length)]
    return forward, backward


def ring_gather(value, axis, tables):
    length = lax.axis_size(axis)
    forward, backward = ring_pairs(length)
    ahead = length // 2
    behind = length - 1 - ahead
    rows = value.shape[0]
    split = behind < ahead and rows % 2 == 0
    half = rows // 2
    pieces = [None] * length
    pieces[0] = value
    fwd = value
    bwd = value
    for k in range(1, ahead + 1):
        if k == ahead and split:
            fwd = lax.ppermute(fwd[:half], axis, forward)
            bwd = lax.ppermute(bwd[half:], axis, backward)
            pieces[k] = jnp.concatenate([fwd, bwd], axis=0)
            break
        fwd = lax.ppermute(fwd, axis, forward)
        pieces[length - k] = fwd
        if k <= behind:
            bwd = lax.ppermute(bwd, axis, backward)
            pieces[k] = bwd
    stacked = jnp.stack(pieces)
    return jnp.take(stacked, tables[1], axis=0, mode="clip").reshape((length * rows,) + value.shape[1:])


def ring_ordered(rows_in, axis, tables):
    length = lax.axis_size(axis)
    blocks = rows_in.reshape((length, rows_in.shape[0] // length) + rows_in.shape[1:])
    return jnp.take(blocks, tables[0], axis=0, mode="clip").reshape(rows_in.shape)


def ring_scatter_sum(value, axis, tables):
    length = lax.axis_size(axis)
    forward, backward = ring_pairs(length)
    ahead = length // 2
    behind = length - 1 - ahead
    rows = value.shape[0] // length
    split = behind < ahead and rows % 2 == 0
    half = rows // 2
    by_offset = value.reshape((length, rows) + value.shape[1:])

    def own(offset):
        return by_offset[offset % length].astype(jnp.float32)

    def chain(offsets, pairs, first_rows):
        passed = None
        for step, offset in enumerate(offsets):
            part = own(offset)
            if step == 0:
                part = part[first_rows]
            elif step == 1 and passed.shape[0] != rows:
                part = part.at[first_rows].add(passed.astype(jnp.float32))
            else:
                part = part + passed.astype(jnp.float32)
            passed = lax.ppermute(part.astype(value.dtype), axis, pairs)
        return passed

    fwd_offsets = list(range(ahead, 0, -1))
    bwd_offsets = list(range(-behind, 0))
    fwd_rows = slice(0, rows)
    bwd_rows = slice(0, rows)
    if split:
        bwd_offsets = [-ahead] + bwd_offsets
        fwd_rows = slice(0, half)
        bwd_rows = slice(half, rows)
    total = own(0)
    total = total + chain(fwd_offsets, forward, fwd_rows).astype(jnp.float32)
    if bwd_offsets:
        total = total + chain(bwd_offsets, backward, bwd_rows).astype(jnp.float32)
    return total


def normed(values, gain):
    wide = values.astype(jnp.float32)
    scale = lax.rsqrt(jnp.mean(wide * wide, axis=-1, keepdims=True) + 1e-06)
    return (wide * scale * gain).astype(jnp.bfloat16)


def rounded_term(left, right):
    term = jnp.dot(left, right, preferred_element_type=jnp.float32)
    return lax.optimization_barrier(term.astype(jnp.bfloat16)).astype(jnp.float32)


def conv_gate_kernel(slab_ref, weight_ref, out_ref, filt_acc, gate_acc):
    tap = pl.program_id(0)
    chunk = pl.program_id(1)

    @pl.when((tap == 0) & (chunk == 0))
    def _():
        filt_acc[...] = jnp.zeros_like(filt_acc)
        gate_acc[...] = jnp.zeros_like(gate_acc)

    rows = slab_ref[...]
    filt_acc[...] += jnp.dot(rows, weight_ref[0], preferred_element_type=jnp.float32)
    gate_acc[...] += jnp.dot(rows, weight_ref[1], preferred_element_type=jnp.float32)

    @pl.when((tap == pl.num_programs(0) - 1) & (chunk == pl.num_programs(1) - 1))
    def _():
        out_ref[...] = (jnp.tanh(filt_acc[...]) * jax.nn.sigmoid(gate_acc[...])).astype(out_ref.dtype)


def convolution_gate(hidden, conv_by_half, layer_idx, dilation_factor):
    all_rows = hidden.shape[0]
    width = hidden.shape[1]
    taps = conv_by_half.shape[1]
    own_width = conv_by_half.shape[-1]
    border_rows = 2 * LARGEST_DILATION
    before = shifted(hidden[all_rows - border_rows :], "blk", 1)
    padded = jnp.concatenate([before, hidden], axis=0)
    slabs = jnp.stack(
        [
            lax.dynamic_slice_in_dim(padded, border_rows - tap_idx * dilation_factor, all_rows, 0)
            for tap_idx in range(taps)
        ]
    )
    chunk = width
    return pl.pallas_call(
        conv_gate_kernel,
        out_shape=jax.ShapeDtypeStruct((all_rows, own_width), jnp.bfloat16),
        grid=(taps, width // chunk),
        in_specs=[
            pl.BlockSpec((None, all_rows, chunk), lambda t, k: (t, 0, k)),
            pl.BlockSpec((None, None, 2, chunk, own_width), lambda t, k: (layer_idx, t, 0, k, 0)),
        ],
        out_specs=pl.BlockSpec((all_rows, own_width), lambda t, k: (0, 0)),
        scratch_shapes=[pltpu.VMEM((all_rows, own_width), jnp.float32)] * 2,
        compiler_params=pltpu.CompilerParams(dimension_semantics=("arbitrary", "arbitrary")),
        cost_estimate=pl.CostEstimate(
            flops=4 * taps * all_rows * width * own_width,
            transcendentals=2 * all_rows * own_width,
            bytes_accessed=2 * taps * (all_rows * width + 2 * width * own_width + all_rows * own_width // taps),
        ),
    )(slabs, conv_by_half)


def conv_share(gated, weight, tok_rows, tables):
    gated = ring_ordered(gated, "head", tables)

    def term(start, count):
        return rounded_term(gated, weight)

    return ring_scatter_sum(
        term(jnp.int32(0), tok_rows * lax.axis_size("head")).astype(jnp.bfloat16), "head", tables
    )


def attention_portion_for(heads_out, out_block, tok_rows, tables):
    heads_out = ring_ordered(heads_out, "head", tables)

    def term(start, count):
        return rounded_term(heads_out, out_block)

    return ring_scatter_sum(
        term(jnp.int32(0), tok_rows * lax.axis_size("head")).astype(jnp.bfloat16), "head", tables
    )


def attend(queries, keys_in, values_in, causal):
    scale = queries.shape[1] ** (-0.5)
    scores = jnp.einsum("qd,kd->qk", queries, keys_in, preferred_element_type=jnp.float32) * scale
    if causal:
        rows_q = lax.broadcasted_iota(jnp.int32, scores.shape, 0)
        rows_k = lax.broadcasted_iota(jnp.int32, scores.shape, 1)
        scores = jnp.where(rows_q >= rows_k, scores, -1e30)
    peak = jnp.max(scores, axis=1)
    probs = jnp.exp(scores - peak[:, None])
    denom = jnp.sum(probs, axis=1)
    weighted = jnp.dot(probs.astype(jnp.bfloat16), values_in, preferred_element_type=jnp.float32)
    return (peak, denom, weighted)


def neutral(count, head_size):
    return (
        jnp.full((count,), -1e30, jnp.float32),
        jnp.zeros((count,), jnp.float32),
        jnp.zeros((count, head_size), jnp.float32),
    )


def combine(first, second):
    peak = jnp.maximum(first[0], second[0])
    scale_one = jnp.exp(first[0] - peak)
    scale_two = jnp.exp(second[0] - peak)
    denom = first[1] * scale_one + second[1] * scale_two
    weighted = first[2] * scale_one[:, None] + second[2] * scale_two[:, None]
    return (peak, denom, weighted)


def per_device(stream, gains, dilations, w_conv, w_mix, w_qkv, w_out):
    blk_pos = lax.axis_index("blk")
    tok_rows = stream.shape[0]
    width = stream.shape[1]
    head_size = w_qkv.shape[3]
    layers = w_conv.shape[0]
    share = stream
    tables = ring_tables("head")
    state = ring_gather(stream, "head", tables)
    conv_by_half = jnp.transpose(w_conv, (0, 1, 3, 2, 4))
    for layer_idx in range(layers):
        gated = convolution_gate(
            normed(state, gains[layer_idx]), conv_by_half, layer_idx, dilations[layer_idx]
        )
        summed = conv_share(gated, w_mix[layer_idx], tok_rows, tables)
        share = (share.astype(jnp.float32) + summed).astype(jnp.bfloat16)
        state = ring_gather(share, "head", tables)
    all_rows = state.shape[0]
    attn_in = normed(state, gains[layers])
    qkv_parts = jnp.transpose(w_qkv[:, :, 0, :], (1, 0, 2))
    queries, keys_own, values_own = (
        jnp.dot(attn_in, qkv_parts[i], preferred_element_type=jnp.float32).astype(jnp.bfloat16)
        for i in range(3)
    )
    keys_prev, values_prev = shifted((keys_own, values_own), "blk", 1)
    own_part = attend(queries, keys_own, values_own, True)
    crossing_portion = lax.cond(
        blk_pos > 0,
        lambda: attend(queries, keys_prev, values_prev, False),
        lambda: neutral(all_rows, head_size),
    )
    peak, denom, weighted = combine(own_part, crossing_portion)
    heads_out = (weighted / denom[:, None]).astype(jnp.bfloat16)
    attn_share = attention_portion_for(heads_out, w_out[0], tok_rows, tables)
    return (share.astype(jnp.float32) + attn_share).astype(jnp.bfloat16)


def solution(mesh):
    placed = (
        P(("grp", "blk", "head"), None),
        P(),
        P(),
        P(None, None, None, None, "head"),
        P(None, "head", None),
        P(None, None, "head", None),
        P("head", None, None),
    )
    return jax.shard_map(
        per_device,
        mesh=mesh,
        in_specs=placed,
        out_specs=P(("grp", "blk", "head"), None),
        check_vma=False,
    )
```

```python
import jax
import jax.numpy as jnp
from jax import lax
from jax.sharding import PartitionSpec as P
from jax.experimental import pallas as pl
from jax.experimental.pallas import tpu as pltpu

LARGEST_DILATION = 64


def shifted(value, axis, by):
    length = lax.axis_size(axis)
    pairs = [(i, i + by) for i in range(length) if 0 <= i + by < length]
    return lax.ppermute(value, axis, pairs)


def ring_order(length):
    if length % 2:
        return list(range(length))
    return list(range(0, length, 2)) + list(range(length - 1, 0, -2))


def ring_tables(axis):
    length = lax.axis_size(axis)
    order = ring_order(length)
    place = [0] * length
    for p, h in enumerate(order):
        place[h] = p
    head_at = [[order[(place[h] + m) % length] for m in range(length)] for h in range(length)]
    offset_of = [[(place[j] - place[h]) % length for j in range(length)] for h in range(length)]
    table = jnp.array([head_at, offset_of], jnp.int32)
    mine = lax.dynamic_index_in_dim(table, lax.axis_index(axis), 1, keepdims=False)
    return mine[0], mine[1]


def ring_pairs(length):
    order = ring_order(length)
    forward = [(order[p], order[(p + 1) % length]) for p in range(length)]
    backward = [(order[p], order[(p - 1) % length]) for p in range(length)]
    return forward, backward


def ring_gather(value, axis, tables):
    length = lax.axis_size(axis)
    forward, backward = ring_pairs(length)
    ahead = length // 2
    behind = length - 1 - ahead
    rows = value.shape[0]
    split = behind < ahead and rows % 2 == 0
    half = rows // 2
    pieces = [None] * length
    pieces[0] = value
    fwd = value
    bwd = value
    for k in range(1, ahead + 1):
        if k == ahead and split:
            fwd = lax.ppermute(fwd[:half], axis, forward)
            bwd = lax.ppermute(bwd[half:], axis, backward)
            pieces[k] = jnp.concatenate([fwd, bwd], axis=0)
            break
        fwd = lax.ppermute(fwd, axis, forward)
        pieces[length - k] = fwd
        if k <= behind:
            bwd = lax.ppermute(bwd, axis, backward)
            pieces[k] = bwd
    stacked = jnp.stack(pieces)
    return jnp.take(stacked, tables[1], axis=0, mode="clip").reshape((length * rows,) + value.shape[1:])


def ring_ordered(rows_in, axis, tables):
    length = lax.axis_size(axis)
    blocks = rows_in.reshape((length, rows_in.shape[0] // length) + rows_in.shape[1:])
    return jnp.take(blocks, tables[0], axis=0, mode="clip").reshape(rows_in.shape)


def ring_scatter_sum(value, axis, tables):
    length = lax.axis_size(axis)
    forward, backward = ring_pairs(length)
    ahead = length // 2
    behind = length - 1 - ahead
    rows = value.shape[0] // length
    split = behind < ahead and rows % 2 == 0
    half = rows // 2
    by_offset = value.reshape((length, rows) + value.shape[1:])

    def own(offset):
        return by_offset[offset % length].astype(jnp.float32)

    def chain(offsets, pairs, first_rows):
        passed = None
        for step, offset in enumerate(offsets):
            part = own(offset)
            if step == 0:
                part = part[first_rows]
            elif step == 1 and passed.shape[0] != rows:
                part = part.at[first_rows].add(passed.astype(jnp.float32))
            else:
                part = part + passed.astype(jnp.float32)
            passed = lax.ppermute(part.astype(value.dtype), axis, pairs)
        return passed

    fwd_offsets = list(range(ahead, 0, -1))
    bwd_offsets = list(range(-behind, 0))
    fwd_rows = slice(0, rows)
    bwd_rows = slice(0, rows)
    if split:
        bwd_offsets = [-ahead] + bwd_offsets
        fwd_rows = slice(0, half)
        bwd_rows = slice(half, rows)
    total = own(0)
    total = total + chain(fwd_offsets, forward, fwd_rows).astype(jnp.float32)
    if bwd_offsets:
        total = total + chain(bwd_offsets, backward, bwd_rows).astype(jnp.float32)
    return total


def normed(values, gain):
    wide = values.astype(jnp.float32)
    scale = lax.rsqrt(jnp.mean(wide * wide, axis=-1, keepdims=True) + 1e-06)
    return (wide * scale * gain).astype(jnp.bfloat16)


def rounded_term(left, right):
    term = jnp.dot(left, right, preferred_element_type=jnp.float32)
    return lax.optimization_barrier(term.astype(jnp.bfloat16)).astype(jnp.float32)


def conv_gate_kernel(slab_ref, gain_ref, weight_ref, out_ref, filt_acc, gate_acc):
    tap = pl.program_id(0)
    chunk = pl.program_id(1)

    @pl.when((tap == 0) & (chunk == 0))
    def _():
        filt_acc[...] = jnp.zeros_like(filt_acc)
        gate_acc[...] = jnp.zeros_like(gate_acc)

    wide = slab_ref[...].astype(jnp.float32)
    scale = lax.rsqrt(jnp.mean(wide * wide, axis=-1, keepdims=True) + 1e-06)
    rows = (wide * scale * gain_ref[...]).astype(jnp.bfloat16)
    filt_acc[...] += jnp.dot(rows, weight_ref[0], preferred_element_type=jnp.float32)
    gate_acc[...] += jnp.dot(rows, weight_ref[1], preferred_element_type=jnp.float32)

    @pl.when((tap == pl.num_programs(0) - 1) & (chunk == pl.num_programs(1) - 1))
    def _():
        out_ref[...] = (jnp.tanh(filt_acc[...]) * jax.nn.sigmoid(gate_acc[...])).astype(out_ref.dtype)


def convolution_gate(state, gain, conv_by_half, layer_idx, dilation_factor):
    hidden = state
    all_rows = hidden.shape[0]
    width = hidden.shape[1]
    taps = conv_by_half.shape[1]
    own_width = conv_by_half.shape[-1]
    border_rows = 2 * LARGEST_DILATION
    before = shifted(hidden[all_rows - border_rows :], "blk", 1)
    padded = jnp.concatenate([before, hidden], axis=0)
    slabs = jnp.stack(
        [
            lax.dynamic_slice_in_dim(padded, border_rows - tap_idx * dilation_factor, all_rows, 0)
            for tap_idx in range(taps)
        ]
    )
    chunk = width
    return pl.pallas_call(
        conv_gate_kernel,
        out_shape=jax.ShapeDtypeStruct((all_rows, own_width), jnp.bfloat16),
        grid=(taps, width // chunk),
        in_specs=[
            pl.BlockSpec((None, all_rows, chunk), lambda t, k: (t, 0, k)),
            pl.BlockSpec((1, width), lambda t, k: (0, 0)),
            pl.BlockSpec((None, None, 2, chunk, own_width), lambda t, k: (layer_idx, t, 0, k, 0)),
        ],
        out_specs=pl.BlockSpec((all_rows, own_width), lambda t, k: (0, 0)),
        scratch_shapes=[pltpu.VMEM((all_rows, own_width), jnp.float32)] * 2,
        compiler_params=pltpu.CompilerParams(dimension_semantics=("arbitrary", "arbitrary")),
        cost_estimate=pl.CostEstimate(
            flops=4 * taps * all_rows * width * own_width,
            transcendentals=2 * all_rows * own_width,
            bytes_accessed=2 * taps * (all_rows * width + 2 * width * own_width + all_rows * own_width // taps),
        ),
    )(slabs, gain.reshape(1, width), conv_by_half)


def conv_share(gated, weight, tok_rows, tables):
    gated = ring_ordered(gated, "head", tables)

    def term(start, count):
        return rounded_term(gated, weight)

    return ring_scatter_sum(
        term(jnp.int32(0), tok_rows * lax.axis_size("head")).astype(jnp.bfloat16), "head", tables
    )


def attention_portion_for(heads_out, out_block, tok_rows, tables):
    heads_out = ring_ordered(heads_out, "head", tables)

    def term(start, count):
        return rounded_term(heads_out, out_block)

    return ring_scatter_sum(
        term(jnp.int32(0), tok_rows * lax.axis_size("head")).astype(jnp.bfloat16), "head", tables
    )


def attend(queries, keys_in, values_in, causal):
    scale = queries.shape[1] ** (-0.5)
    scores = jnp.einsum("qd,kd->qk", queries, keys_in, preferred_element_type=jnp.float32) * scale
    if causal:
        rows_q = lax.broadcasted_iota(jnp.int32, scores.shape, 0)
        rows_k = lax.broadcasted_iota(jnp.int32, scores.shape, 1)
        scores = jnp.where(rows_q >= rows_k, scores, -1e30)
    peak = jnp.max(scores, axis=1)
    probs = jnp.exp(scores - peak[:, None])
    denom = jnp.sum(probs, axis=1)
    weighted = jnp.dot(probs.astype(jnp.bfloat16), values_in, preferred_element_type=jnp.float32)
    return (peak, denom, weighted)


def neutral(count, head_size):
    return (
        jnp.full((count,), -1e30, jnp.float32),
        jnp.zeros((count,), jnp.float32),
        jnp.zeros((count, head_size), jnp.float32),
    )


def combine(first, second):
    peak = jnp.maximum(first[0], second[0])
    scale_one = jnp.exp(first[0] - peak)
    scale_two = jnp.exp(second[0] - peak)
    denom = first[1] * scale_one + second[1] * scale_two
    weighted = first[2] * scale_one[:, None] + second[2] * scale_two[:, None]
    return (peak, denom, weighted)


def per_device(stream, gains, dilations, w_conv, w_mix, w_qkv, w_out):
    blk_pos = lax.axis_index("blk")
    tok_rows = stream.shape[0]
    width = stream.shape[1]
    head_size = w_qkv.shape[3]
    layers = w_conv.shape[0]
    share = stream
    tables = ring_tables("head")
    state = ring_gather(stream, "head", tables)
    conv_by_half = jnp.transpose(w_conv, (0, 1, 3, 2, 4))
    for layer_idx in range(layers):
        gated = convolution_gate(
            state, gains[layer_idx], conv_by_half, layer_idx, dilations[layer_idx]
        )
        summed = conv_share(gated, w_mix[layer_idx], tok_rows, tables)
        share = (share.astype(jnp.float32) + summed).astype(jnp.bfloat16)
        state = ring_gather(share, "head", tables)
    all_rows = state.shape[0]
    attn_in = normed(state, gains[layers])
    qkv_parts = jnp.transpose(w_qkv[:, :, 0, :], (1, 0, 2))
    queries, keys_own, values_own = (
        jnp.dot(attn_in, qkv_parts[i], preferred_element_type=jnp.float32).astype(jnp.bfloat16)
        for i in range(3)
    )
    keys_prev, values_prev = shifted((keys_own, values_own), "blk", 1)
    own_part = attend(queries, keys_own, values_own, True)
    crossing_portion = lax.cond(
        blk_pos > 0,
        lambda: attend(queries, keys_prev, values_prev, False),
        lambda: neutral(all_rows, head_size),
    )
    peak, denom, weighted = combine(own_part, crossing_portion)
    heads_out = (weighted / denom[:, None]).astype(jnp.bfloat16)
    attn_share = attention_portion_for(heads_out, w_out[0], tok_rows, tables)
    return (share.astype(jnp.float32) + attn_share).astype(jnp.bfloat16)


def solution(mesh):
    placed = (
        P(("grp", "blk", "head"), None),
        P(),
        P(),
        P(None, None, None, None, "head"),
        P(None, "head", None),
        P(None, None, "head", None),
        P("head", None, None),
    )
    return jax.shard_map(
        per_device,
        mesh=mesh,
        in_specs=placed,
        out_specs=P(("grp", "blk", "head"), None),
        check_vma=False,
    )
```

```python
import jax
import jax.numpy as jnp
from jax import lax
from jax.sharding import PartitionSpec as P
from jax.experimental import pallas as pl
from jax.experimental.pallas import tpu as pltpu

LARGEST_DILATION = 64


def shifted(value, axis, by):
    length = lax.axis_size(axis)
    pairs = [(i, i + by) for i in range(length) if 0 <= i + by < length]
    return lax.ppermute(value, axis, pairs)


def ring_order(length):
    if length % 2:
        return list(range(length))
    return list(range(0, length, 2)) + list(range(length - 1, 0, -2))


def ring_tables(axis):
    length = lax.axis_size(axis)
    order = ring_order(length)
    place = [0] * length
    for p, h in enumerate(order):
        place[h] = p
    head_at = [[order[(place[h] + m) % length] for m in range(length)] for h in range(length)]
    offset_of = [[(place[j] - place[h]) % length for j in range(length)] for h in range(length)]
    table = jnp.array([head_at, offset_of], jnp.int32)
    mine = lax.dynamic_index_in_dim(table, lax.axis_index(axis), 1, keepdims=False)
    return mine[0], mine[1]


def ring_pairs(length):
    order = ring_order(length)
    forward = [(order[p], order[(p + 1) % length]) for p in range(length)]
    backward = [(order[p], order[(p - 1) % length]) for p in range(length)]
    return forward, backward


def ring_gather(value, axis, tables, direct=1):
    length = lax.axis_size(axis)
    forward, backward = ring_pairs(length)
    order = ring_order(length)
    ahead = length // 2
    behind = length - 1 - ahead
    direct = max(1, min(direct, behind))
    rows = value.shape[0]
    split = behind < ahead and rows % 2 == 0
    half = rows // 2
    pieces = [None] * length
    pieces[0] = value
    fwd = value
    bwd = value
    for k in range(1, direct + 1):
        fwd = lax.ppermute(value, axis, [(order[p], order[(p + k) % length]) for p in range(length)])
        bwd = lax.ppermute(value, axis, [(order[p], order[(p - k) % length]) for p in range(length)])
        pieces[length - k] = fwd
        pieces[k] = bwd
    for k in range(direct + 1, ahead + 1):
        if k == ahead and split:
            fwd = lax.ppermute(fwd[:half], axis, forward)
            bwd = lax.ppermute(bwd[half:], axis, backward)
            pieces[k] = jnp.concatenate([fwd, bwd], axis=0)
            break
        fwd = lax.ppermute(fwd, axis, forward)
        pieces[length - k] = fwd
        if k <= behind:
            bwd = lax.ppermute(bwd, axis, backward)
            pieces[k] = bwd
    stacked = jnp.stack(pieces)
    return jnp.take(stacked, tables[1], axis=0, mode="clip").reshape((length * rows,) + value.shape[1:])


def ring_ordered(rows_in, axis, tables):
    length = lax.axis_size(axis)
    blocks = rows_in.reshape((length, rows_in.shape[0] // length) + rows_in.shape[1:])
    return jnp.take(blocks, tables[0], axis=0, mode="clip").reshape(rows_in.shape)


def ring_scatter_sum(value, axis, tables):
    length = lax.axis_size(axis)
    forward, backward = ring_pairs(length)
    ahead = length // 2
    behind = length - 1 - ahead
    rows = value.shape[0] // length
    split = behind < ahead and rows % 2 == 0
    half = rows // 2
    by_offset = value.reshape((length, rows) + value.shape[1:])

    def own(offset):
        return by_offset[offset % length].astype(jnp.float32)

    def chain(offsets, pairs, first_rows):
        passed = None
        for step, offset in enumerate(offsets):
            part = own(offset)
            if step == 0:
                part = part[first_rows]
            elif step == 1 and passed.shape[0] != rows:
                part = part.at[first_rows].add(passed.astype(jnp.float32))
            else:
                part = part + passed.astype(jnp.float32)
            passed = lax.ppermute(part.astype(value.dtype), axis, pairs)
        return passed

    fwd_offsets = list(range(ahead, 0, -1))
    bwd_offsets = list(range(-behind, 0))
    fwd_rows = slice(0, rows)
    bwd_rows = slice(0, rows)
    if split:
        bwd_offsets = [-ahead] + bwd_offsets
        fwd_rows = slice(0, half)
        bwd_rows = slice(half, rows)
    total = own(0)
    total = total + chain(fwd_offsets, forward, fwd_rows).astype(jnp.float32)
    if bwd_offsets:
        total = total + chain(bwd_offsets, backward, bwd_rows).astype(jnp.float32)
    return total


def normed(values, gain):
    wide = values.astype(jnp.float32)
    scale = lax.rsqrt(jnp.mean(wide * wide, axis=-1, keepdims=True) + 1e-06)
    return (wide * scale * gain).astype(jnp.bfloat16)


def rounded_term(left, right):
    term = jnp.dot(left, right, preferred_element_type=jnp.float32)
    return lax.optimization_barrier(term.astype(jnp.bfloat16)).astype(jnp.float32)


def conv_gate_kernel(slab_ref, gain_ref, weight_ref, out_ref, filt_acc, gate_acc):
    tap = pl.program_id(0)
    chunk = pl.program_id(1)

    @pl.when((tap == 0) & (chunk == 0))
    def _():
        filt_acc[...] = jnp.zeros_like(filt_acc)
        gate_acc[...] = jnp.zeros_like(gate_acc)

    wide = slab_ref[...].astype(jnp.float32)
    scale = lax.rsqrt(jnp.mean(wide * wide, axis=-1, keepdims=True) + 1e-06)
    rows = (wide * scale * gain_ref[...]).astype(jnp.bfloat16)
    filt_acc[...] += jnp.dot(rows, weight_ref[0], preferred_element_type=jnp.float32)
    gate_acc[...] += jnp.dot(rows, weight_ref[1], preferred_element_type=jnp.float32)

    @pl.when((tap == pl.num_programs(0) - 1) & (chunk == pl.num_programs(1) - 1))
    def _():
        out_ref[...] = (jnp.tanh(filt_acc[...]) * jax.nn.sigmoid(gate_acc[...])).astype(out_ref.dtype)


def convolution_gate(state, gain, conv_by_half, layer_idx, dilation_factor):
    hidden = state
    all_rows = hidden.shape[0]
    width = hidden.shape[1]
    taps = conv_by_half.shape[1]
    own_width = conv_by_half.shape[-1]
    border_rows = 2 * LARGEST_DILATION
    before = shifted(hidden[all_rows - border_rows :], "blk", 1)
    padded = jnp.concatenate([before, hidden], axis=0)
    slabs = jnp.stack(
        [
            lax.dynamic_slice_in_dim(padded, border_rows - tap_idx * dilation_factor, all_rows, 0)
            for tap_idx in range(taps)
        ]
    )
    chunk = width
    return pl.pallas_call(
        conv_gate_kernel,
        out_shape=jax.ShapeDtypeStruct((all_rows, own_width), jnp.bfloat16),
        grid=(taps, width // chunk),
        in_specs=[
            pl.BlockSpec((None, all_rows, chunk), lambda t, k: (t, 0, k)),
            pl.BlockSpec((1, width), lambda t, k: (0, 0)),
            pl.BlockSpec((None, None, 2, chunk, own_width), lambda t, k: (layer_idx, t, 0, k, 0)),
        ],
        out_specs=pl.BlockSpec((all_rows, own_width), lambda t, k: (0, 0)),
        scratch_shapes=[pltpu.VMEM((all_rows, own_width), jnp.float32)] * 2,
        compiler_params=pltpu.CompilerParams(dimension_semantics=("arbitrary", "arbitrary")),
        cost_estimate=pl.CostEstimate(
            flops=4 * taps * all_rows * width * own_width,
            transcendentals=2 * all_rows * own_width,
            bytes_accessed=2 * taps * (all_rows * width + 2 * width * own_width + all_rows * own_width // taps),
        ),
    )(slabs, gain.reshape(1, width), conv_by_half)


def conv_share(gated, weight, tok_rows, tables):
    gated = ring_ordered(gated, "head", tables)

    def term(start, count):
        return rounded_term(gated, weight)

    return ring_scatter_sum(
        term(jnp.int32(0), tok_rows * lax.axis_size("head")).astype(jnp.bfloat16), "head", tables
    )


def attention_portion_for(heads_out, out_block, tok_rows, tables):
    heads_out = ring_ordered(heads_out, "head", tables)

    def term(start, count):
        return rounded_term(heads_out, out_block)

    return ring_scatter_sum(
        term(jnp.int32(0), tok_rows * lax.axis_size("head")).astype(jnp.bfloat16), "head", tables
    )


def attend(queries, keys_in, values_in, causal):
    scale = queries.shape[1] ** (-0.5)
    scores = jnp.einsum("qd,kd->qk", queries, keys_in, preferred_element_type=jnp.float32) * scale
    if causal:
        rows_q = lax.broadcasted_iota(jnp.int32, scores.shape, 0)
        rows_k = lax.broadcasted_iota(jnp.int32, scores.shape, 1)
        scores = jnp.where(rows_q >= rows_k, scores, -1e30)
    peak = jnp.max(scores, axis=1)
    probs = jnp.exp(scores - peak[:, None])
    denom = jnp.sum(probs, axis=1)
    weighted = jnp.dot(probs.astype(jnp.bfloat16), values_in, preferred_element_type=jnp.float32)
    return (peak, denom, weighted)


def neutral(count, head_size):
    return (
        jnp.full((count,), -1e30, jnp.float32),
        jnp.zeros((count,), jnp.float32),
        jnp.zeros((count, head_size), jnp.float32),
    )


def combine(first, second):
    peak = jnp.maximum(first[0], second[0])
    scale_one = jnp.exp(first[0] - peak)
    scale_two = jnp.exp(second[0] - peak)
    denom = first[1] * scale_one + second[1] * scale_two
    weighted = first[2] * scale_one[:, None] + second[2] * scale_two[:, None]
    return (peak, denom, weighted)


def per_device(stream, gains, dilations, w_conv, w_mix, w_qkv, w_out):
    blk_pos = lax.axis_index("blk")
    tok_rows = stream.shape[0]
    width = stream.shape[1]
    head_size = w_qkv.shape[3]
    layers = w_conv.shape[0]
    share = stream
    tables = ring_tables("head")
    state = ring_gather(stream, "head", tables, direct=2)
    conv_by_half = jnp.transpose(w_conv, (0, 1, 3, 2, 4))
    for layer_idx in range(layers):
        gated = convolution_gate(
            state, gains[layer_idx], conv_by_half, layer_idx, dilations[layer_idx]
        )
        summed = conv_share(gated, w_mix[layer_idx], tok_rows, tables)
        share = (share.astype(jnp.float32) + summed).astype(jnp.bfloat16)
        state = ring_gather(share, "head", tables)
    all_rows = state.shape[0]
    attn_in = normed(state, gains[layers])
    qkv_parts = jnp.transpose(w_qkv[:, :, 0, :], (1, 0, 2))
    queries, keys_own, values_own = (
        jnp.dot(attn_in, qkv_parts[i], preferred_element_type=jnp.float32).astype(jnp.bfloat16)
        for i in range(3)
    )
    keys_prev, values_prev = shifted((keys_own, values_own), "blk", 1)
    own_part = attend(queries, keys_own, values_own, True)
    crossing_portion = lax.cond(
        blk_pos > 0,
        lambda: attend(queries, keys_prev, values_prev, False),
        lambda: neutral(all_rows, head_size),
    )
    peak, denom, weighted = combine(own_part, crossing_portion)
    heads_out = (weighted / denom[:, None]).astype(jnp.bfloat16)
    attn_share = attention_portion_for(heads_out, w_out[0], tok_rows, tables)
    return (share.astype(jnp.float32) + attn_share).astype(jnp.bfloat16)


def solution(mesh):
    placed = (
        P(("grp", "blk", "head"), None),
        P(),
        P(),
        P(None, None, None, None, "head"),
        P(None, "head", None),
        P(None, None, "head", None),
        P("head", None, None),
    )
    return jax.shard_map(
        per_device,
        mesh=mesh,
        in_specs=placed,
        out_specs=P(("grp", "blk", "head"), None),
        check_vma=False,
    )
```

```python
import jax
import jax.numpy as jnp
from jax import lax
from jax.sharding import PartitionSpec as P
from jax.experimental import pallas as pl
from jax.experimental.pallas import tpu as pltpu

LARGEST_DILATION = 64


def shifted(value, axis, by):
    length = lax.axis_size(axis)
    pairs = [(i, i + by) for i in range(length) if 0 <= i + by < length]
    return lax.ppermute(value, axis, pairs)


def ring_order(length):
    if length % 2:
        return list(range(length))
    return list(range(0, length, 2)) + list(range(length - 1, 0, -2))


def ring_tables(axis):
    length = lax.axis_size(axis)
    order = ring_order(length)
    place = [0] * length
    for p, h in enumerate(order):
        place[h] = p
    head_at = [[order[(place[h] + m) % length] for m in range(length)] for h in range(length)]
    offset_of = [[(place[j] - place[h]) % length for j in range(length)] for h in range(length)]
    table = jnp.array([head_at, offset_of], jnp.int32)
    mine = lax.dynamic_index_in_dim(table, lax.axis_index(axis), 1, keepdims=False)
    return mine[0], mine[1]


def ring_pairs(length):
    order = ring_order(length)
    forward = [(order[p], order[(p + 1) % length]) for p in range(length)]
    backward = [(order[p], order[(p - 1) % length]) for p in range(length)]
    return forward, backward


def ring_gather(value, axis, tables, direct=1):
    length = lax.axis_size(axis)
    forward, backward = ring_pairs(length)
    order = ring_order(length)
    ahead = length // 2
    behind = length - 1 - ahead
    direct = max(1, min(direct, behind))
    rows = value.shape[0]
    split = behind < ahead and rows % 2 == 0
    half = rows // 2
    pieces = [None] * length
    pieces[0] = value
    fwd = value
    bwd = value
    for k in range(1, direct + 1):
        fwd = lax.ppermute(value, axis, [(order[p], order[(p + k) % length]) for p in range(length)])
        bwd = lax.ppermute(value, axis, [(order[p], order[(p - k) % length]) for p in range(length)])
        pieces[length - k] = fwd
        pieces[k] = bwd
    for k in range(direct + 1, ahead + 1):
        if k == ahead and split:
            fwd = lax.ppermute(fwd[:half], axis, forward)
            bwd = lax.ppermute(bwd[half:], axis, backward)
            pieces[k] = jnp.concatenate([fwd, bwd], axis=0)
            break
        fwd = lax.ppermute(fwd, axis, forward)
        pieces[length - k] = fwd
        if k <= behind:
            bwd = lax.ppermute(bwd, axis, backward)
            pieces[k] = bwd
    stacked = jnp.stack(pieces)
    return jnp.take(stacked, tables[1], axis=0, mode="clip").reshape((length * rows,) + value.shape[1:])


def ring_ordered(rows_in, axis, tables):
    length = lax.axis_size(axis)
    blocks = rows_in.reshape((length, rows_in.shape[0] // length) + rows_in.shape[1:])
    return jnp.take(blocks, tables[0], axis=0, mode="clip").reshape(rows_in.shape)


def ring_scatter_sum(value, axis, tables):
    length = lax.axis_size(axis)
    forward, backward = ring_pairs(length)
    ahead = length // 2
    behind = length - 1 - ahead
    rows = value.shape[0] // length
    split = behind < ahead and rows % 2 == 0
    half = rows // 2
    by_offset = value.reshape((length, rows) + value.shape[1:])

    def own(offset):
        return by_offset[offset % length].astype(jnp.float32)

    def chain(offsets, pairs, first_rows):
        passed = None
        for step, offset in enumerate(offsets):
            part = own(offset)
            if step == 0:
                part = part[first_rows]
            elif step == 1 and passed.shape[0] != rows:
                part = part.at[first_rows].add(passed.astype(jnp.float32))
            else:
                part = part + passed.astype(jnp.float32)
            passed = lax.ppermute(part.astype(value.dtype), axis, pairs)
        return passed

    fwd_offsets = list(range(ahead, 0, -1))
    bwd_offsets = list(range(-behind, 0))
    fwd_rows = slice(0, rows)
    bwd_rows = slice(0, rows)
    if split:
        bwd_offsets = [-ahead] + bwd_offsets
        fwd_rows = slice(0, half)
        bwd_rows = slice(half, rows)
    total = own(0)
    total = total + chain(fwd_offsets, forward, fwd_rows).astype(jnp.float32)
    if bwd_offsets:
        total = total + chain(bwd_offsets, backward, bwd_rows).astype(jnp.float32)
    return total


def normed(values, gain):
    wide = values.astype(jnp.float32)
    scale = lax.rsqrt(jnp.mean(wide * wide, axis=-1, keepdims=True) + 1e-06)
    return (wide * scale * gain).astype(jnp.bfloat16)


def rounded_term(left, right):
    term = jnp.dot(left, right, preferred_element_type=jnp.float32)
    return lax.optimization_barrier(term.astype(jnp.bfloat16)).astype(jnp.float32)


def normed_rows(slab_ref, gain_ref):
    wide = slab_ref[...].astype(jnp.float32)
    scale = lax.rsqrt(jnp.mean(wide * wide, axis=-1, keepdims=True) + 1e-06)
    return (wide * scale * gain_ref[...]).astype(jnp.bfloat16)


def first_tap_kernel(slab_ref, gain_ref, weight_ref, filt_ref, gate_ref):
    rows = normed_rows(slab_ref, gain_ref)
    weight = weight_ref[...]
    filt_ref[...] = jnp.dot(rows, weight[0], preferred_element_type=jnp.float32)
    gate_ref[...] = jnp.dot(rows, weight[1], preferred_element_type=jnp.float32)


def later_taps_kernel(slab_ref, gain_ref, weight_ref, filt_in, gate_in, out_ref, filt_acc, gate_acc):
    tap = pl.program_id(0)

    @pl.when(tap == 0)
    def _():
        filt_acc[...] = filt_in[...]
        gate_acc[...] = gate_in[...]

    rows = normed_rows(slab_ref, gain_ref)
    weight = weight_ref[...]
    filt_acc[...] += jnp.dot(rows, weight[0], preferred_element_type=jnp.float32)
    gate_acc[...] += jnp.dot(rows, weight[1], preferred_element_type=jnp.float32)

    @pl.when(tap == pl.num_programs(0) - 1)
    def _():
        out_ref[...] = (jnp.tanh(filt_acc[...]) * jax.nn.sigmoid(gate_acc[...])).astype(out_ref.dtype)


def convolution_gate(state, gain, conv_by_half, layer_idx, dilation_factor):
    all_rows = state.shape[0]
    width = state.shape[1]
    taps = conv_by_half.shape[1]
    own_width = conv_by_half.shape[-1]
    border_rows = 2 * LARGEST_DILATION
    gain_row = gain.reshape(1, width)
    acc_shape = jax.ShapeDtypeStruct((all_rows, own_width), jnp.float32)
    weight_bytes = 2 * 2 * width * own_width
    filt, gate = pl.pallas_call(
        first_tap_kernel,
        out_shape=(acc_shape, acc_shape),
        grid=(1,),
        in_specs=[
            pl.BlockSpec((all_rows, width), lambda t: (0, 0)),
            pl.BlockSpec((1, width), lambda t: (0, 0)),
            pl.BlockSpec((None, None, 2, width, own_width), lambda t: (layer_idx, 0, 0, 0, 0)),
        ],
        out_specs=(
            pl.BlockSpec((all_rows, own_width), lambda t: (0, 0)),
            pl.BlockSpec((all_rows, own_width), lambda t: (0, 0)),
        ),
        cost_estimate=pl.CostEstimate(
            flops=4 * all_rows * width * own_width,
            transcendentals=0,
            bytes_accessed=2 * all_rows * width + weight_bytes + 8 * all_rows * own_width,
        ),
    )(state, gain_row, conv_by_half)
    before = shifted(state[all_rows - border_rows :], "blk", 1)
    padded = jnp.concatenate([before, state], axis=0)
    slabs = jnp.stack(
        [
            lax.dynamic_slice_in_dim(padded, border_rows - tap_idx * dilation_factor, all_rows, 0)
            for tap_idx in range(1, taps)
        ]
    )
    return pl.pallas_call(
        later_taps_kernel,
        out_shape=jax.ShapeDtypeStruct((all_rows, own_width), jnp.bfloat16),
        grid=(taps - 1,),
        in_specs=[
            pl.BlockSpec((None, all_rows, width), lambda t: (t, 0, 0)),
            pl.BlockSpec((1, width), lambda t: (0, 0)),
            pl.BlockSpec((None, None, 2, width, own_width), lambda t: (layer_idx, t + 1, 0, 0, 0)),
            pl.BlockSpec((all_rows, own_width), lambda t: (0, 0)),
            pl.BlockSpec((all_rows, own_width), lambda t: (0, 0)),
        ],
        out_specs=pl.BlockSpec((all_rows, own_width), lambda t: (0, 0)),
        scratch_shapes=[pltpu.VMEM((all_rows, own_width), jnp.float32)] * 2,
        compiler_params=pltpu.CompilerParams(dimension_semantics=("arbitrary",)),
        cost_estimate=pl.CostEstimate(
            flops=4 * (taps - 1) * all_rows * width * own_width,
            transcendentals=2 * all_rows * own_width,
            bytes_accessed=(taps - 1) * (2 * all_rows * width + weight_bytes) + 10 * all_rows * own_width,
        ),
    )(slabs, gain_row, conv_by_half, filt, gate)


def conv_share(gated, weight, tok_rows, tables):
    gated = ring_ordered(gated, "head", tables)

    def term(start, count):
        return rounded_term(gated, weight)

    return ring_scatter_sum(
        term(jnp.int32(0), tok_rows * lax.axis_size("head")).astype(jnp.bfloat16), "head", tables
    )


def attention_portion_for(heads_out, out_block, tok_rows, tables):
    heads_out = ring_ordered(heads_out, "head", tables)

    def term(start, count):
        return rounded_term(heads_out, out_block)

    return ring_scatter_sum(
        term(jnp.int32(0), tok_rows * lax.axis_size("head")).astype(jnp.bfloat16), "head", tables
    )


def attend(queries, keys_in, values_in, causal):
    scale = queries.shape[1] ** (-0.5)
    scores = jnp.einsum("qd,kd->qk", queries, keys_in, preferred_element_type=jnp.float32) * scale
    if causal:
        rows_q = lax.broadcasted_iota(jnp.int32, scores.shape, 0)
        rows_k = lax.broadcasted_iota(jnp.int32, scores.shape, 1)
        scores = jnp.where(rows_q >= rows_k, scores, -1e30)
    peak = jnp.max(scores, axis=1)
    probs = jnp.exp(scores - peak[:, None])
    denom = jnp.sum(probs, axis=1)
    weighted = jnp.dot(probs.astype(jnp.bfloat16), values_in, preferred_element_type=jnp.float32)
    return (peak, denom, weighted)


def neutral(count, head_size):
    return (
        jnp.full((count,), -1e30, jnp.float32),
        jnp.zeros((count,), jnp.float32),
        jnp.zeros((count, head_size), jnp.float32),
    )


def combine(first, second):
    peak = jnp.maximum(first[0], second[0])
    scale_one = jnp.exp(first[0] - peak)
    scale_two = jnp.exp(second[0] - peak)
    denom = first[1] * scale_one + second[1] * scale_two
    weighted = first[2] * scale_one[:, None] + second[2] * scale_two[:, None]
    return (peak, denom, weighted)


def per_device(stream, gains, dilations, w_conv, w_mix, w_qkv, w_out):
    blk_pos = lax.axis_index("blk")
    tok_rows = stream.shape[0]
    width = stream.shape[1]
    head_size = w_qkv.shape[3]
    layers = w_conv.shape[0]
    share = stream
    tables = ring_tables("head")
    state = ring_gather(stream, "head", tables, direct=2)
    conv_by_half = jnp.transpose(w_conv, (0, 1, 3, 2, 4))
    for layer_idx in range(layers):
        gated = convolution_gate(
            state, gains[layer_idx], conv_by_half, layer_idx, dilations[layer_idx]
        )
        summed = conv_share(gated, w_mix[layer_idx], tok_rows, tables)
        share = (share.astype(jnp.float32) + summed).astype(jnp.bfloat16)
        state = ring_gather(share, "head", tables)
    all_rows = state.shape[0]
    attn_in = normed(state, gains[layers])
    qkv_parts = jnp.transpose(w_qkv[:, :, 0, :], (1, 0, 2))
    queries, keys_own, values_own = (
        jnp.dot(attn_in, qkv_parts[i], preferred_element_type=jnp.float32).astype(jnp.bfloat16)
        for i in range(3)
    )
    keys_prev, values_prev = shifted((keys_own, values_own), "blk", 1)
    own_part = attend(queries, keys_own, values_own, True)
    crossing_portion = lax.cond(
        blk_pos > 0,
        lambda: attend(queries, keys_prev, values_prev, False),
        lambda: neutral(all_rows, head_size),
    )
    peak, denom, weighted = combine(own_part, crossing_portion)
    heads_out = (weighted / denom[:, None]).astype(jnp.bfloat16)
    attn_share = attention_portion_for(heads_out, w_out[0], tok_rows, tables)
    return (share.astype(jnp.float32) + attn_share).astype(jnp.bfloat16)


def solution(mesh):
    placed = (
        P(("grp", "blk", "head"), None),
        P(),
        P(),
        P(None, None, None, None, "head"),
        P(None, "head", None),
        P(None, None, "head", None),
        P("head", None, None),
    )
    return jax.shard_map(
        per_device,
        mesh=mesh,
        in_specs=placed,
        out_specs=P(("grp", "blk", "head"), None),
        check_vma=False,
    )
```

```python
import jax
import jax.numpy as jnp
from jax import lax
from jax.sharding import PartitionSpec as P
from jax.experimental import pallas as pl
from jax.experimental.pallas import tpu as pltpu

LARGEST_DILATION = 64


def shifted(value, axis, by):
    length = lax.axis_size(axis)
    pairs = [(i, i + by) for i in range(length) if 0 <= i + by < length]
    return lax.ppermute(value, axis, pairs)


def ring_order(length):
    if length % 2:
        return list(range(length))
    return list(range(0, length, 2)) + list(range(length - 1, 0, -2))


def ring_tables(axis):
    length = lax.axis_size(axis)
    order = ring_order(length)
    place = [0] * length
    for p, h in enumerate(order):
        place[h] = p
    head_at = [[order[(place[h] + m) % length] for m in range(length)] for h in range(length)]
    offset_of = [[(place[j] - place[h]) % length for j in range(length)] for h in range(length)]
    table = jnp.array([head_at, offset_of], jnp.int32)
    mine = lax.dynamic_index_in_dim(table, lax.axis_index(axis), 1, keepdims=False)
    return mine[0], mine[1]


def ring_pairs(length):
    order = ring_order(length)
    forward = [(order[p], order[(p + 1) % length]) for p in range(length)]
    backward = [(order[p], order[(p - 1) % length]) for p in range(length)]
    return forward, backward


def ring_gather(value, axis, tables, direct=1):
    length = lax.axis_size(axis)
    forward, backward = ring_pairs(length)
    order = ring_order(length)
    ahead = length // 2
    behind = length - 1 - ahead
    direct = max(1, min(direct, behind))
    rows = value.shape[0]
    split = behind < ahead and rows % 2 == 0
    half = rows // 2
    pieces = [None] * length
    pieces[0] = value
    fwd = value
    bwd = value
    for k in range(1, direct + 1):
        fwd = lax.ppermute(value, axis, [(order[p], order[(p + k) % length]) for p in range(length)])
        bwd = lax.ppermute(value, axis, [(order[p], order[(p - k) % length]) for p in range(length)])
        pieces[length - k] = fwd
        pieces[k] = bwd
    for k in range(direct + 1, ahead + 1):
        if k == ahead and split:
            fwd = lax.ppermute(fwd[:half], axis, forward)
            bwd = lax.ppermute(bwd[half:], axis, backward)
            pieces[k] = jnp.concatenate([fwd, bwd], axis=0)
            break
        fwd = lax.ppermute(fwd, axis, forward)
        pieces[length - k] = fwd
        if k <= behind:
            bwd = lax.ppermute(bwd, axis, backward)
            pieces[k] = bwd
    stacked = jnp.stack(pieces)
    return jnp.take(stacked, tables[1], axis=0, mode="clip").reshape((length * rows,) + value.shape[1:])


def ring_ordered(rows_in, axis, tables):
    length = lax.axis_size(axis)
    blocks = rows_in.reshape((length, rows_in.shape[0] // length) + rows_in.shape[1:])
    return jnp.take(blocks, tables[0], axis=0, mode="clip").reshape(rows_in.shape)


def ring_scatter_sum(value, axis, tables, far=None):
    length = lax.axis_size(axis)
    forward, backward = ring_pairs(length)
    ahead = length // 2
    behind = length - 1 - ahead
    rows = value.shape[0] // length
    split = behind < ahead and rows % 2 == 0
    half = rows // 2
    by_offset = value.reshape((length, rows) + value.shape[1:])

    def own(offset):
        if far is not None and offset % length == ahead:
            return far.astype(jnp.float32)
        return by_offset[offset % length].astype(jnp.float32)

    def chain(offsets, pairs, first_rows):
        passed = None
        for step, offset in enumerate(offsets):
            part = own(offset)
            if step == 0:
                part = part[first_rows]
            elif step == 1 and passed.shape[0] != rows:
                part = part.at[first_rows].add(passed.astype(jnp.float32))
            else:
                part = part + passed.astype(jnp.float32)
            passed = lax.ppermute(part.astype(value.dtype), axis, pairs)
        return passed

    fwd_offsets = list(range(ahead, 0, -1))
    bwd_offsets = list(range(-behind, 0))
    fwd_rows = slice(0, rows)
    bwd_rows = slice(0, rows)
    if split:
        bwd_offsets = [-ahead] + bwd_offsets
        fwd_rows = slice(0, half)
        bwd_rows = slice(half, rows)
    total = own(0)
    total = total + chain(fwd_offsets, forward, fwd_rows).astype(jnp.float32)
    if bwd_offsets:
        total = total + chain(bwd_offsets, backward, bwd_rows).astype(jnp.float32)
    return total


def normed(values, gain):
    wide = values.astype(jnp.float32)
    scale = lax.rsqrt(jnp.mean(wide * wide, axis=-1, keepdims=True) + 1e-06)
    return (wide * scale * gain).astype(jnp.bfloat16)


def rounded_term(left, right):
    term = jnp.dot(left, right, preferred_element_type=jnp.float32)
    return lax.optimization_barrier(term.astype(jnp.bfloat16)).astype(jnp.float32)


def conv_gate_kernel(slab_ref, gain_ref, weight_ref, out_ref, filt_acc, gate_acc):
    tap = pl.program_id(0)
    chunk = pl.program_id(1)

    @pl.when((tap == 0) & (chunk == 0))
    def _():
        filt_acc[...] = jnp.zeros_like(filt_acc)
        gate_acc[...] = jnp.zeros_like(gate_acc)

    wide = slab_ref[...].astype(jnp.float32)
    scale = lax.rsqrt(jnp.mean(wide * wide, axis=-1, keepdims=True) + 1e-06)
    rows = (wide * scale * gain_ref[...]).astype(jnp.bfloat16)
    filt_acc[...] += jnp.dot(rows, weight_ref[0], preferred_element_type=jnp.float32)
    gate_acc[...] += jnp.dot(rows, weight_ref[1], preferred_element_type=jnp.float32)

    @pl.when((tap == pl.num_programs(0) - 1) & (chunk == pl.num_programs(1) - 1))
    def _():
        out_ref[...] = (jnp.tanh(filt_acc[...]) * jax.nn.sigmoid(gate_acc[...])).astype(out_ref.dtype)


def convolution_gate(state, gain, conv_by_half, layer_idx, dilation_factor):
    hidden = state
    all_rows = hidden.shape[0]
    width = hidden.shape[1]
    taps = conv_by_half.shape[1]
    own_width = conv_by_half.shape[-1]
    border_rows = 2 * LARGEST_DILATION
    before = shifted(hidden[all_rows - border_rows :], "blk", 1)
    padded = jnp.concatenate([before, hidden], axis=0)
    slabs = jnp.stack(
        [
            lax.dynamic_slice_in_dim(padded, border_rows - tap_idx * dilation_factor, all_rows, 0)
            for tap_idx in range(taps)
        ]
    )
    chunk = width
    return pl.pallas_call(
        conv_gate_kernel,
        out_shape=jax.ShapeDtypeStruct((all_rows, own_width), jnp.bfloat16),
        grid=(taps, width // chunk),
        in_specs=[
            pl.BlockSpec((None, all_rows, chunk), lambda t, k: (t, 0, k)),
            pl.BlockSpec((1, width), lambda t, k: (0, 0)),
            pl.BlockSpec((None, None, 2, chunk, own_width), lambda t, k: (layer_idx, t, 0, k, 0)),
        ],
        out_specs=pl.BlockSpec((all_rows, own_width), lambda t, k: (0, 0)),
        scratch_shapes=[pltpu.VMEM((all_rows, own_width), jnp.float32)] * 2,
        compiler_params=pltpu.CompilerParams(dimension_semantics=("arbitrary", "arbitrary")),
        cost_estimate=pl.CostEstimate(
            flops=4 * taps * all_rows * width * own_width,
            transcendentals=2 * all_rows * own_width,
            bytes_accessed=2 * taps * (all_rows * width + 2 * width * own_width + all_rows * own_width // taps),
        ),
    )(slabs, gain.reshape(1, width), conv_by_half)


def far_rows(ordered, tok_rows):
    return ordered[(lax.axis_size("head") // 2) * tok_rows :][:tok_rows]


def conv_share(gated, weight, tok_rows, tables):
    gated = ring_ordered(gated, "head", tables)

    def term(start, count):
        return rounded_term(gated, weight)

    return ring_scatter_sum(
        term(jnp.int32(0), tok_rows * lax.axis_size("head")).astype(jnp.bfloat16),
        "head",
        tables,
        far=rounded_term(far_rows(gated, tok_rows), weight).astype(jnp.bfloat16),
    )


def attention_portion_for(heads_out, out_block, tok_rows, tables):
    heads_out = ring_ordered(heads_out, "head", tables)

    def term(start, count):
        return rounded_term(heads_out, out_block)

    return ring_scatter_sum(
        term(jnp.int32(0), tok_rows * lax.axis_size("head")).astype(jnp.bfloat16),
        "head",
        tables,
        far=rounded_term(far_rows(heads_out, tok_rows), out_block).astype(jnp.bfloat16),
    )


def attend(queries, keys_in, values_in, causal):
    scale = queries.shape[1] ** (-0.5)
    scores = jnp.einsum("qd,kd->qk", queries, keys_in, preferred_element_type=jnp.float32) * scale
    if causal:
        rows_q = lax.broadcasted_iota(jnp.int32, scores.shape, 0)
        rows_k = lax.broadcasted_iota(jnp.int32, scores.shape, 1)
        scores = jnp.where(rows_q >= rows_k, scores, -1e30)
    peak = jnp.max(scores, axis=1)
    probs = jnp.exp(scores - peak[:, None])
    denom = jnp.sum(probs, axis=1)
    weighted = jnp.dot(probs.astype(jnp.bfloat16), values_in, preferred_element_type=jnp.float32)
    return (peak, denom, weighted)


def neutral(count, head_size):
    return (
        jnp.full((count,), -1e30, jnp.float32),
        jnp.zeros((count,), jnp.float32),
        jnp.zeros((count, head_size), jnp.float32),
    )


def combine(first, second):
    peak = jnp.maximum(first[0], second[0])
    scale_one = jnp.exp(first[0] - peak)
    scale_two = jnp.exp(second[0] - peak)
    denom = first[1] * scale_one + second[1] * scale_two
    weighted = first[2] * scale_one[:, None] + second[2] * scale_two[:, None]
    return (peak, denom, weighted)


def per_device(stream, gains, dilations, w_conv, w_mix, w_qkv, w_out):
    blk_pos = lax.axis_index("blk")
    tok_rows = stream.shape[0]
    width = stream.shape[1]
    head_size = w_qkv.shape[3]
    layers = w_conv.shape[0]
    share = stream
    tables = ring_tables("head")
    state = ring_gather(stream, "head", tables, direct=2)
    conv_by_half = jnp.transpose(w_conv, (0, 1, 3, 2, 4))
    for layer_idx in range(layers):
        gated = convolution_gate(
            state, gains[layer_idx], conv_by_half, layer_idx, dilations[layer_idx]
        )
        summed = conv_share(gated, w_mix[layer_idx], tok_rows, tables)
        share = (share.astype(jnp.float32) + summed).astype(jnp.bfloat16)
        state = ring_gather(share, "head", tables)
    all_rows = state.shape[0]
    attn_in = normed(state, gains[layers])
    qkv_parts = jnp.transpose(w_qkv[:, :, 0, :], (1, 0, 2))
    queries, keys_own, values_own = (
        jnp.dot(attn_in, qkv_parts[i], preferred_element_type=jnp.float32).astype(jnp.bfloat16)
        for i in range(3)
    )
    keys_prev, values_prev = shifted((keys_own, values_own), "blk", 1)
    own_part = attend(queries, keys_own, values_own, True)
    crossing_portion = lax.cond(
        blk_pos > 0,
        lambda: attend(queries, keys_prev, values_prev, False),
        lambda: neutral(all_rows, head_size),
    )
    peak, denom, weighted = combine(own_part, crossing_portion)
    heads_out = (weighted / denom[:, None]).astype(jnp.bfloat16)
    attn_share = attention_portion_for(heads_out, w_out[0], tok_rows, tables)
    return (share.astype(jnp.float32) + attn_share).astype(jnp.bfloat16)


def solution(mesh):
    placed = (
        P(("grp", "blk", "head"), None),
        P(),
        P(),
        P(None, None, None, None, "head"),
        P(None, "head", None),
        P(None, None, "head", None),
        P("head", None, None),
    )
    return jax.shard_map(
        per_device,
        mesh=mesh,
        in_specs=placed,
        out_specs=P(("grp", "blk", "head"), None),
        check_vma=False,
    )
```

```python
import jax
import jax.numpy as jnp
from jax import lax
from jax.sharding import PartitionSpec as P
from jax.experimental import pallas as pl
from jax.experimental.pallas import tpu as pltpu

LARGEST_DILATION = 64


def shifted(value, axis, by):
    length = lax.axis_size(axis)
    pairs = [(i, i + by) for i in range(length) if 0 <= i + by < length]
    return lax.ppermute(value, axis, pairs)


def ring_order(length):
    if length % 2:
        return list(range(length))
    return list(range(0, length, 2)) + list(range(length - 1, 0, -2))


def ring_tables(axis):
    length = lax.axis_size(axis)
    order = ring_order(length)
    place = [0] * length
    for p, h in enumerate(order):
        place[h] = p
    head_at = [[order[(place[h] + m) % length] for m in range(length)] for h in range(length)]
    offset_of = [[(place[j] - place[h]) % length for j in range(length)] for h in range(length)]
    table = jnp.array([head_at, offset_of], jnp.int32)
    mine = lax.dynamic_index_in_dim(table, lax.axis_index(axis), 1, keepdims=False)
    return mine[0], mine[1]


def ring_pairs(length):
    order = ring_order(length)
    forward = [(order[p], order[(p + 1) % length]) for p in range(length)]
    backward = [(order[p], order[(p - 1) % length]) for p in range(length)]
    return forward, backward


def ring_gather(value, axis, tables, direct=1):
    length = lax.axis_size(axis)
    forward, backward = ring_pairs(length)
    order = ring_order(length)
    ahead = length // 2
    behind = length - 1 - ahead
    direct = max(1, min(direct, behind))
    rows = value.shape[0]
    split = behind < ahead and rows % 2 == 0
    half = rows // 2
    pieces = [None] * length
    pieces[0] = value
    fwd = value
    bwd = value
    for k in range(1, direct + 1):
        fwd = lax.ppermute(value, axis, [(order[p], order[(p + k) % length]) for p in range(length)])
        bwd = lax.ppermute(value, axis, [(order[p], order[(p - k) % length]) for p in range(length)])
        pieces[length - k] = fwd
        pieces[k] = bwd
    for k in range(direct + 1, ahead + 1):
        if k == ahead and split:
            fwd = lax.ppermute(fwd[:half], axis, forward)
            bwd = lax.ppermute(bwd[half:], axis, backward)
            pieces[k] = jnp.concatenate([fwd, bwd], axis=0)
            break
        fwd = lax.ppermute(fwd, axis, forward)
        pieces[length - k] = fwd
        if k <= behind:
            bwd = lax.ppermute(bwd, axis, backward)
            pieces[k] = bwd
    stacked = jnp.stack(pieces)
    return jnp.take(stacked, tables[1], axis=0, mode="clip").reshape((length * rows,) + value.shape[1:])


def ring_ordered(rows_in, axis, tables):
    length = lax.axis_size(axis)
    blocks = rows_in.reshape((length, rows_in.shape[0] // length) + rows_in.shape[1:])
    return jnp.take(blocks, tables[0], axis=0, mode="clip").reshape(rows_in.shape)


def ring_scatter_sum(value, axis, tables, far=None):
    length = lax.axis_size(axis)
    forward, backward = ring_pairs(length)
    ahead = length // 2
    behind = length - 1 - ahead
    rows = value.shape[0] // length
    split = behind < ahead and rows % 2 == 0
    half = rows // 2
    by_offset = value.reshape((length, rows) + value.shape[1:])

    def own(offset):
        if far is not None and offset % length == ahead:
            return far.astype(jnp.float32)
        return by_offset[offset % length].astype(jnp.float32)

    def chain(offsets, pairs, first_rows):
        passed = None
        for step, offset in enumerate(offsets):
            part = own(offset)
            if step == 0:
                part = part[first_rows]
            elif step == 1 and passed.shape[0] != rows:
                part = part.at[first_rows].add(passed.astype(jnp.float32))
            else:
                part = part + passed.astype(jnp.float32)
            passed = lax.ppermute(part.astype(value.dtype), axis, pairs)
        return passed

    fwd_offsets = list(range(ahead, 0, -1))
    bwd_offsets = list(range(-behind, 0))
    fwd_rows = slice(0, rows)
    bwd_rows = slice(0, rows)
    if split:
        bwd_offsets = [-ahead] + bwd_offsets
        fwd_rows = slice(0, half)
        bwd_rows = slice(half, rows)
    total = own(0)
    total = total + chain(fwd_offsets, forward, fwd_rows).astype(jnp.float32)
    if bwd_offsets:
        total = total + chain(bwd_offsets, backward, bwd_rows).astype(jnp.float32)
    return total


def normed(values, gain):
    wide = values.astype(jnp.float32)
    scale = lax.rsqrt(jnp.mean(wide * wide, axis=-1, keepdims=True) + 1e-06)
    return (wide * scale * gain).astype(jnp.bfloat16)


def rounded_term(left, right):
    term = jnp.dot(left, right, preferred_element_type=jnp.float32)
    return lax.optimization_barrier(term.astype(jnp.bfloat16)).astype(jnp.float32)


def conv_gate_kernel(slab_ref, scale_ref, gain_ref, weight_ref, out_ref, filt_acc, gate_acc):
    tap = pl.program_id(0)
    chunk = pl.program_id(1)

    @pl.when((tap == 0) & (chunk == 0))
    def _():
        filt_acc[...] = jnp.zeros_like(filt_acc)
        gate_acc[...] = jnp.zeros_like(gate_acc)

    rows = (slab_ref[...].astype(jnp.float32) * scale_ref[...] * gain_ref[...]).astype(jnp.bfloat16)
    filt_acc[...] += jnp.dot(rows, weight_ref[0], preferred_element_type=jnp.float32)
    gate_acc[...] += jnp.dot(rows, weight_ref[1], preferred_element_type=jnp.float32)

    @pl.when((tap == pl.num_programs(0) - 1) & (chunk == pl.num_programs(1) - 1))
    def _():
        out_ref[...] = (jnp.tanh(filt_acc[...]) * jax.nn.sigmoid(gate_acc[...])).astype(out_ref.dtype)


def convolution_gate(state, gain, conv_by_half, layer_idx, dilation_factor):
    hidden = state
    all_rows = hidden.shape[0]
    width = hidden.shape[1]
    taps = conv_by_half.shape[1]
    own_width = conv_by_half.shape[-1]
    border_rows = 2 * LARGEST_DILATION
    before = shifted(hidden[all_rows - border_rows :], "blk", 1)
    padded = jnp.concatenate([before, hidden], axis=0)
    wide = padded.astype(jnp.float32)
    row_scale = lax.rsqrt(jnp.mean(wide * wide, axis=-1, keepdims=True) + 1e-06)
    starts = [border_rows - tap_idx * dilation_factor for tap_idx in range(taps)]
    slabs = jnp.stack([lax.dynamic_slice_in_dim(padded, s, all_rows, 0) for s in starts])
    scales = jnp.stack([lax.dynamic_slice_in_dim(row_scale, s, all_rows, 0) for s in starts])
    chunk = width // 2 if width % 256 == 0 else width
    return pl.pallas_call(
        conv_gate_kernel,
        out_shape=jax.ShapeDtypeStruct((all_rows, own_width), jnp.bfloat16),
        grid=(taps, width // chunk),
        in_specs=[
            pl.BlockSpec((None, all_rows, chunk), lambda t, k: (t, 0, k)),
            pl.BlockSpec((None, all_rows, 1), lambda t, k: (t, 0, 0)),
            pl.BlockSpec((1, chunk), lambda t, k: (0, k)),
            pl.BlockSpec((None, None, 2, chunk, own_width), lambda t, k: (layer_idx, t, 0, k, 0)),
        ],
        out_specs=pl.BlockSpec((all_rows, own_width), lambda t, k: (0, 0)),
        scratch_shapes=[pltpu.VMEM((all_rows, own_width), jnp.float32)] * 2,
        compiler_params=pltpu.CompilerParams(dimension_semantics=("arbitrary", "arbitrary")),
        cost_estimate=pl.CostEstimate(
            flops=4 * taps * all_rows * width * own_width,
            transcendentals=2 * all_rows * own_width,
            bytes_accessed=2 * taps * (all_rows * width + 2 * width * own_width + all_rows * own_width // taps),
        ),
    )(slabs, scales, gain.reshape(1, width), conv_by_half)


def far_rows(ordered, tok_rows):
    return ordered[(lax.axis_size("head") // 2) * tok_rows :][:tok_rows]


def conv_share(gated, weight, tok_rows, tables):
    gated = ring_ordered(gated, "head", tables)

    def term(start, count):
        return rounded_term(gated, weight)

    return ring_scatter_sum(
        term(jnp.int32(0), tok_rows * lax.axis_size("head")).astype(jnp.bfloat16),
        "head",
        tables,
        far=rounded_term(far_rows(gated, tok_rows), weight).astype(jnp.bfloat16),
    )


def attention_portion_for(heads_out, out_block, tok_rows, tables):
    heads_out = ring_ordered(heads_out, "head", tables)

    def term(start, count):
        return rounded_term(heads_out, out_block)

    return ring_scatter_sum(
        term(jnp.int32(0), tok_rows * lax.axis_size("head")).astype(jnp.bfloat16),
        "head",
        tables,
        far=rounded_term(far_rows(heads_out, tok_rows), out_block).astype(jnp.bfloat16),
    )


def attend(queries, keys_in, values_in, causal):
    scale = queries.shape[1] ** (-0.5)
    scores = jnp.einsum("qd,kd->qk", queries, keys_in, preferred_element_type=jnp.float32) * scale
    if causal:
        rows_q = lax.broadcasted_iota(jnp.int32, scores.shape, 0)
        rows_k = lax.broadcasted_iota(jnp.int32, scores.shape, 1)
        scores = jnp.where(rows_q >= rows_k, scores, -1e30)
    peak = jnp.max(scores, axis=1)
    probs = jnp.exp(scores - peak[:, None])
    denom = jnp.sum(probs, axis=1)
    weighted = jnp.dot(probs.astype(jnp.bfloat16), values_in, preferred_element_type=jnp.float32)
    return (peak, denom, weighted)


def neutral(count, head_size):
    return (
        jnp.full((count,), -1e30, jnp.float32),
        jnp.zeros((count,), jnp.float32),
        jnp.zeros((count, head_size), jnp.float32),
    )


def combine(first, second):
    peak = jnp.maximum(first[0], second[0])
    scale_one = jnp.exp(first[0] - peak)
    scale_two = jnp.exp(second[0] - peak)
    denom = first[1] * scale_one + second[1] * scale_two
    weighted = first[2] * scale_one[:, None] + second[2] * scale_two[:, None]
    return (peak, denom, weighted)


def per_device(stream, gains, dilations, w_conv, w_mix, w_qkv, w_out):
    blk_pos = lax.axis_index("blk")
    tok_rows = stream.shape[0]
    width = stream.shape[1]
    head_size = w_qkv.shape[3]
    layers = w_conv.shape[0]
    share = stream
    tables = ring_tables("head")
    state = ring_gather(stream, "head", tables, direct=2)
    conv_by_half = jnp.transpose(w_conv, (0, 1, 3, 2, 4))
    for layer_idx in range(layers):
        gated = convolution_gate(
            state, gains[layer_idx], conv_by_half, layer_idx, dilations[layer_idx]
        )
        summed = conv_share(gated, w_mix[layer_idx], tok_rows, tables)
        share = (share.astype(jnp.float32) + summed).astype(jnp.bfloat16)
        state = ring_gather(share, "head", tables)
    all_rows = state.shape[0]
    attn_in = normed(state, gains[layers])
    qkv_parts = jnp.transpose(w_qkv[:, :, 0, :], (1, 0, 2))
    queries, keys_own, values_own = (
        jnp.dot(attn_in, qkv_parts[i], preferred_element_type=jnp.float32).astype(jnp.bfloat16)
        for i in range(3)
    )
    keys_prev, values_prev = shifted((keys_own, values_own), "blk", 1)
    own_part = attend(queries, keys_own, values_own, True)
    crossing_portion = lax.cond(
        blk_pos > 0,
        lambda: attend(queries, keys_prev, values_prev, False),
        lambda: neutral(all_rows, head_size),
    )
    peak, denom, weighted = combine(own_part, crossing_portion)
    heads_out = (weighted / denom[:, None]).astype(jnp.bfloat16)
    attn_share = attention_portion_for(heads_out, w_out[0], tok_rows, tables)
    return (share.astype(jnp.float32) + attn_share).astype(jnp.bfloat16)


def solution(mesh):
    placed = (
        P(("grp", "blk", "head"), None),
        P(),
        P(),
        P(None, None, None, None, "head"),
        P(None, "head", None),
        P(None, None, "head", None),
        P("head", None, None),
    )
    return jax.shard_map(
        per_device,
        mesh=mesh,
        in_specs=placed,
        out_specs=P(("grp", "blk", "head"), None),
        check_vma=False,
    )
```

```python
import jax
import jax.numpy as jnp
from jax import lax
from jax.sharding import PartitionSpec as P
from jax.experimental import pallas as pl
from jax.experimental.pallas import tpu as pltpu

LARGEST_DILATION = 64


def shifted(value, axis, by):
    length = lax.axis_size(axis)
    pairs = [(i, i + by) for i in range(length) if 0 <= i + by < length]
    return lax.ppermute(value, axis, pairs)


def ring_order(length):
    if length % 2:
        return list(range(length))
    return list(range(0, length, 2)) + list(range(length - 1, 0, -2))


def ring_tables(axis):
    length = lax.axis_size(axis)
    order = ring_order(length)
    place = [0] * length
    for p, h in enumerate(order):
        place[h] = p
    head_at = [[order[(place[h] + m) % length] for m in range(length)] for h in range(length)]
    offset_of = [[(place[j] - place[h]) % length for j in range(length)] for h in range(length)]
    table = jnp.array([head_at, offset_of], jnp.int32)
    mine = lax.dynamic_index_in_dim(table, lax.axis_index(axis), 1, keepdims=False)
    return mine[0], mine[1]


def ring_pairs(length):
    order = ring_order(length)
    forward = [(order[p], order[(p + 1) % length]) for p in range(length)]
    backward = [(order[p], order[(p - 1) % length]) for p in range(length)]
    return forward, backward


def ring_gather(value, axis, tables, direct=1):
    length = lax.axis_size(axis)
    forward, backward = ring_pairs(length)
    order = ring_order(length)
    ahead = length // 2
    behind = length - 1 - ahead
    direct = max(1, min(direct, behind))
    rows = value.shape[0]
    split = behind < ahead and rows % 2 == 0
    half = rows // 2
    pieces = [None] * length
    pieces[0] = value
    fwd = value
    bwd = value
    for k in range(1, direct + 1):
        fwd = lax.ppermute(value, axis, [(order[p], order[(p + k) % length]) for p in range(length)])
        bwd = lax.ppermute(value, axis, [(order[p], order[(p - k) % length]) for p in range(length)])
        pieces[length - k] = fwd
        pieces[k] = bwd
    for k in range(direct + 1, ahead + 1):
        if k == ahead and split:
            fwd = lax.ppermute(fwd[:half], axis, forward)
            bwd = lax.ppermute(bwd[half:], axis, backward)
            pieces[k] = jnp.concatenate([fwd, bwd], axis=0)
            break
        fwd = lax.ppermute(fwd, axis, forward)
        pieces[length - k] = fwd
        if k <= behind:
            bwd = lax.ppermute(bwd, axis, backward)
            pieces[k] = bwd
    stacked = jnp.stack(pieces)
    return jnp.take(stacked, tables[1], axis=0, mode="clip").reshape((length * rows,) + value.shape[1:])


def ring_ordered(rows_in, axis, tables):
    length = lax.axis_size(axis)
    blocks = rows_in.reshape((length, rows_in.shape[0] // length) + rows_in.shape[1:])
    return jnp.take(blocks, tables[0], axis=0, mode="clip").reshape(rows_in.shape)


def ring_scatter_sum(value, axis, tables, far=None):
    length = lax.axis_size(axis)
    forward, backward = ring_pairs(length)
    ahead = length // 2
    behind = length - 1 - ahead
    rows = value.shape[0] // length
    split = behind < ahead and rows % 2 == 0
    half = rows // 2
    by_offset = value.reshape((length, rows) + value.shape[1:])

    def own(offset):
        if far is not None and offset % length == ahead:
            return far.astype(jnp.float32)
        return by_offset[offset % length].astype(jnp.float32)

    def chain(offsets, pairs, first_rows):
        passed = None
        for step, offset in enumerate(offsets):
            part = own(offset)
            if step == 0:
                part = part[first_rows]
            elif step == 1 and passed.shape[0] != rows:
                part = part.at[first_rows].add(passed.astype(jnp.float32))
            else:
                part = part + passed.astype(jnp.float32)
            passed = lax.ppermute(part.astype(value.dtype), axis, pairs)
        return passed

    fwd_offsets = list(range(ahead, 0, -1))
    bwd_offsets = list(range(-behind, 0))
    fwd_rows = slice(0, rows)
    bwd_rows = slice(0, rows)
    if split:
        bwd_offsets = [-ahead] + bwd_offsets
        fwd_rows = slice(0, half)
        bwd_rows = slice(half, rows)
    total = own(0)
    total = total + chain(fwd_offsets, forward, fwd_rows).astype(jnp.float32)
    if bwd_offsets:
        total = total + chain(bwd_offsets, backward, bwd_rows).astype(jnp.float32)
    return total


def normed(values, gain):
    wide = values.astype(jnp.float32)
    scale = lax.rsqrt(jnp.mean(wide * wide, axis=-1, keepdims=True) + 1e-06)
    return (wide * scale * gain).astype(jnp.bfloat16)


def rounded_term(left, right):
    term = jnp.dot(left, right, preferred_element_type=jnp.float32)
    return lax.optimization_barrier(term.astype(jnp.bfloat16)).astype(jnp.float32)


def conv_gate_kernel(head_at_ref, slab_ref, gain_ref, weight_ref, mix_ref, out_ref, filt_acc, gate_acc, gated, ordered):
    tap = pl.program_id(0)
    chunk = pl.program_id(1)

    @pl.when((tap == 0) & (chunk == 0))
    def _():
        filt_acc[...] = jnp.zeros_like(filt_acc)
        gate_acc[...] = jnp.zeros_like(gate_acc)

    wide = slab_ref[...].astype(jnp.float32)
    scale = lax.rsqrt(jnp.mean(wide * wide, axis=-1, keepdims=True) + 1e-06)
    rows = (wide * scale * gain_ref[...]).astype(jnp.bfloat16)
    filt_acc[...] += jnp.dot(rows, weight_ref[0], preferred_element_type=jnp.float32)
    gate_acc[...] += jnp.dot(rows, weight_ref[1], preferred_element_type=jnp.float32)

    @pl.when((tap == pl.num_programs(0) - 1) & (chunk == pl.num_programs(1) - 1))
    def _():
        gated[...] = (jnp.tanh(filt_acc[...]) * jax.nn.sigmoid(gate_acc[...])).astype(jnp.bfloat16).astype(jnp.float32)
        blocks = head_at_ref.shape[0]
        block_rows = gated.shape[0] // blocks
        for m in range(blocks):
            start = pl.multiple_of(head_at_ref[m] * block_rows, block_rows)
            ordered[m * block_rows : (m + 1) * block_rows, :] = gated[pl.ds(start, block_rows), :]
        out_ref[...] = jnp.dot(
            ordered[...].astype(jnp.bfloat16), mix_ref[...], preferred_element_type=jnp.float32
        ).astype(out_ref.dtype)


def convolution_gate(state, gain, conv_by_half, layer_idx, dilation_factor, w_mix, head_at):
    hidden = state
    all_rows = hidden.shape[0]
    width = hidden.shape[1]
    taps = conv_by_half.shape[1]
    own_width = conv_by_half.shape[-1]
    border_rows = 2 * LARGEST_DILATION
    before = shifted(hidden[all_rows - border_rows :], "blk", 1)
    padded = jnp.concatenate([before, hidden], axis=0)
    slabs = jnp.stack(
        [
            lax.dynamic_slice_in_dim(padded, border_rows - tap_idx * dilation_factor, all_rows, 0)
            for tap_idx in range(taps)
        ]
    )
    chunk = width
    return pl.pallas_call(
        conv_gate_kernel,
        out_shape=jax.ShapeDtypeStruct((all_rows, width), jnp.bfloat16),
        grid_spec=pltpu.PrefetchScalarGridSpec(
            num_scalar_prefetch=1,
            grid=(taps, width // chunk),
            in_specs=[
                pl.BlockSpec((None, all_rows, chunk), lambda t, k, h: (t, 0, k)),
                pl.BlockSpec((1, width), lambda t, k, h: (0, 0)),
                pl.BlockSpec((None, None, 2, chunk, own_width), lambda t, k, h: (layer_idx, t, 0, k, 0)),
                pl.BlockSpec((None, own_width, width), lambda t, k, h: (layer_idx, 0, 0)),
            ],
            out_specs=pl.BlockSpec((all_rows, width), lambda t, k, h: (0, 0)),
            scratch_shapes=[pltpu.VMEM((all_rows, own_width), jnp.float32)] * 4,
        ),
        compiler_params=pltpu.CompilerParams(dimension_semantics=("arbitrary", "arbitrary")),
        cost_estimate=pl.CostEstimate(
            flops=4 * taps * all_rows * width * own_width,
            transcendentals=2 * all_rows * own_width,
            bytes_accessed=2 * taps * (all_rows * width + 2 * width * own_width + all_rows * own_width // taps),
        ),
    )(head_at, slabs, gain.reshape(1, width), conv_by_half, w_mix)


def far_rows(ordered, tok_rows):
    return ordered[(lax.axis_size("head") // 2) * tok_rows :][:tok_rows]


def conv_share(gated, weight, tok_rows, tables):
    gated = ring_ordered(gated, "head", tables)

    def term(start, count):
        return rounded_term(gated, weight)

    return ring_scatter_sum(
        term(jnp.int32(0), tok_rows * lax.axis_size("head")).astype(jnp.bfloat16),
        "head",
        tables,
        far=rounded_term(far_rows(gated, tok_rows), weight).astype(jnp.bfloat16),
    )


def attention_portion_for(heads_out, out_block, tok_rows, tables):
    heads_out = ring_ordered(heads_out, "head", tables)

    def term(start, count):
        return rounded_term(heads_out, out_block)

    return ring_scatter_sum(
        term(jnp.int32(0), tok_rows * lax.axis_size("head")).astype(jnp.bfloat16),
        "head",
        tables,
        far=rounded_term(far_rows(heads_out, tok_rows), out_block).astype(jnp.bfloat16),
    )


def attend(queries, keys_in, values_in, causal):
    scale = queries.shape[1] ** (-0.5)
    scores = jnp.einsum("qd,kd->qk", queries, keys_in, preferred_element_type=jnp.float32) * scale
    if causal:
        rows_q = lax.broadcasted_iota(jnp.int32, scores.shape, 0)
        rows_k = lax.broadcasted_iota(jnp.int32, scores.shape, 1)
        scores = jnp.where(rows_q >= rows_k, scores, -1e30)
    peak = jnp.max(scores, axis=1)
    probs = jnp.exp(scores - peak[:, None])
    denom = jnp.sum(probs, axis=1)
    weighted = jnp.dot(probs.astype(jnp.bfloat16), values_in, preferred_element_type=jnp.float32)
    return (peak, denom, weighted)


def neutral(count, head_size):
    return (
        jnp.full((count,), -1e30, jnp.float32),
        jnp.zeros((count,), jnp.float32),
        jnp.zeros((count, head_size), jnp.float32),
    )


def combine(first, second):
    peak = jnp.maximum(first[0], second[0])
    scale_one = jnp.exp(first[0] - peak)
    scale_two = jnp.exp(second[0] - peak)
    denom = first[1] * scale_one + second[1] * scale_two
    weighted = first[2] * scale_one[:, None] + second[2] * scale_two[:, None]
    return (peak, denom, weighted)


def per_device(stream, gains, dilations, w_conv, w_mix, w_qkv, w_out):
    blk_pos = lax.axis_index("blk")
    tok_rows = stream.shape[0]
    width = stream.shape[1]
    head_size = w_qkv.shape[3]
    layers = w_conv.shape[0]
    share = stream
    tables = ring_tables("head")
    state = ring_gather(stream, "head", tables, direct=2)
    conv_by_half = jnp.transpose(w_conv, (0, 1, 3, 2, 4))
    for layer_idx in range(layers):
        mixed_rows = convolution_gate(
            state, gains[layer_idx], conv_by_half, layer_idx, dilations[layer_idx], w_mix, tables[0]
        )
        summed = ring_scatter_sum(mixed_rows, "head", tables)
        share = (share.astype(jnp.float32) + summed).astype(jnp.bfloat16)
        state = ring_gather(share, "head", tables)
    all_rows = state.shape[0]
    attn_in = normed(state, gains[layers])
    qkv_parts = jnp.transpose(w_qkv[:, :, 0, :], (1, 0, 2))
    queries, keys_own, values_own = (
        jnp.dot(attn_in, qkv_parts[i], preferred_element_type=jnp.float32).astype(jnp.bfloat16)
        for i in range(3)
    )
    keys_prev, values_prev = shifted((keys_own, values_own), "blk", 1)
    own_part = attend(queries, keys_own, values_own, True)
    crossing_portion = lax.cond(
        blk_pos > 0,
        lambda: attend(queries, keys_prev, values_prev, False),
        lambda: neutral(all_rows, head_size),
    )
    peak, denom, weighted = combine(own_part, crossing_portion)
    heads_out = (weighted / denom[:, None]).astype(jnp.bfloat16)
    attn_share = attention_portion_for(heads_out, w_out[0], tok_rows, tables)
    return (share.astype(jnp.float32) + attn_share).astype(jnp.bfloat16)


def solution(mesh):
    placed = (
        P(("grp", "blk", "head"), None),
        P(),
        P(),
        P(None, None, None, None, "head"),
        P(None, "head", None),
        P(None, None, "head", None),
        P("head", None, None),
    )
    return jax.shard_map(
        per_device,
        mesh=mesh,
        in_specs=placed,
        out_specs=P(("grp", "blk", "head"), None),
        check_vma=False,
    )
```

```python
import jax
import jax.numpy as jnp
from jax import lax
from jax.sharding import PartitionSpec as P
from jax.experimental import pallas as pl
from jax.experimental.pallas import tpu as pltpu

LARGEST_DILATION = 64


def shifted(value, axis, by):
    length = lax.axis_size(axis)
    pairs = [(i, i + by) for i in range(length) if 0 <= i + by < length]
    return lax.ppermute(value, axis, pairs)


def ring_order(length):
    if length % 2:
        return list(range(length))
    return list(range(0, length, 2)) + list(range(length - 1, 0, -2))


def ring_tables(axis):
    length = lax.axis_size(axis)
    order = ring_order(length)
    place = [0] * length
    for p, h in enumerate(order):
        place[h] = p
    head_at = [[order[(place[h] + m) % length] for m in range(length)] for h in range(length)]
    offset_of = [[(place[j] - place[h]) % length for j in range(length)] for h in range(length)]
    table = jnp.array([head_at, offset_of], jnp.int32)
    mine = lax.dynamic_index_in_dim(table, lax.axis_index(axis), 1, keepdims=False)
    return mine[0], mine[1]


def ring_pairs(length):
    order = ring_order(length)
    forward = [(order[p], order[(p + 1) % length]) for p in range(length)]
    backward = [(order[p], order[(p - 1) % length]) for p in range(length)]
    return forward, backward


def ring_gather(value, axis, tables, direct=1):
    length = lax.axis_size(axis)
    forward, backward = ring_pairs(length)
    order = ring_order(length)
    ahead = length // 2
    behind = length - 1 - ahead
    direct = max(1, min(direct, behind))
    rows = value.shape[0]
    split = behind < ahead and rows % 2 == 0
    half = rows // 2
    pieces = [None] * length
    pieces[0] = value
    fwd = value
    bwd = value
    for k in range(1, direct + 1):
        fwd = lax.ppermute(value, axis, [(order[p], order[(p + k) % length]) for p in range(length)])
        bwd = lax.ppermute(value, axis, [(order[p], order[(p - k) % length]) for p in range(length)])
        pieces[length - k] = fwd
        pieces[k] = bwd
    for k in range(direct + 1, ahead + 1):
        if k == ahead and split:
            fwd = lax.ppermute(fwd[:half], axis, forward)
            bwd = lax.ppermute(bwd[half:], axis, backward)
            pieces[k] = jnp.concatenate([fwd, bwd], axis=0)
            break
        fwd = lax.ppermute(fwd, axis, forward)
        pieces[length - k] = fwd
        if k <= behind:
            bwd = lax.ppermute(bwd, axis, backward)
            pieces[k] = bwd
    stacked = jnp.stack(pieces)
    return jnp.take(stacked, tables[1], axis=0, mode="clip").reshape((length * rows,) + value.shape[1:])


def ring_ordered(rows_in, axis, tables):
    length = lax.axis_size(axis)
    blocks = rows_in.reshape((length, rows_in.shape[0] // length) + rows_in.shape[1:])
    return jnp.take(blocks, tables[0], axis=0, mode="clip").reshape(rows_in.shape)


def ring_scatter_sum(value, axis, tables, far=None):
    length = lax.axis_size(axis)
    forward, backward = ring_pairs(length)
    ahead = length // 2
    behind = length - 1 - ahead
    rows = value.shape[0] // length
    split = behind < ahead and rows % 2 == 0
    half = rows // 2
    by_offset = value.reshape((length, rows) + value.shape[1:])

    def own(offset):
        if far is not None and offset % length == ahead:
            return far.astype(jnp.float32)
        return by_offset[offset % length].astype(jnp.float32)

    def chain(offsets, pairs, first_rows):
        passed = None
        for step, offset in enumerate(offsets):
            part = own(offset)
            if step == 0:
                part = part[first_rows]
            elif step == 1 and passed.shape[0] != rows:
                part = part.at[first_rows].add(passed.astype(jnp.float32))
            else:
                part = part + passed.astype(jnp.float32)
            passed = lax.ppermute(part.astype(value.dtype), axis, pairs)
        return passed

    fwd_offsets = list(range(ahead, 0, -1))
    bwd_offsets = list(range(-behind, 0))
    fwd_rows = slice(0, rows)
    bwd_rows = slice(0, rows)
    if split:
        bwd_offsets = [-ahead] + bwd_offsets
        fwd_rows = slice(0, half)
        bwd_rows = slice(half, rows)
    total = own(0)
    total = total + chain(fwd_offsets, forward, fwd_rows).astype(jnp.float32)
    if bwd_offsets:
        total = total + chain(bwd_offsets, backward, bwd_rows).astype(jnp.float32)
    return total


def normed(values, gain):
    wide = values.astype(jnp.float32)
    scale = lax.rsqrt(jnp.mean(wide * wide, axis=-1, keepdims=True) + 1e-06)
    return (wide * scale * gain).astype(jnp.bfloat16)


def rounded_term(left, right):
    term = jnp.dot(left, right, preferred_element_type=jnp.float32)
    return lax.optimization_barrier(term.astype(jnp.bfloat16)).astype(jnp.float32)


def conv_gate_kernel(slab_ref, gain_ref, weight_ref, out_ref, filt_acc, gate_acc, normed_rows):
    tap = pl.program_id(0)
    half = pl.program_id(1)

    @pl.when((tap == 0) & (half == 0))
    def _():
        filt_acc[...] = jnp.zeros_like(filt_acc)
        gate_acc[...] = jnp.zeros_like(gate_acc)

    @pl.when(half == 0)
    def _():
        wide = slab_ref[...].astype(jnp.float32)
        scale = lax.rsqrt(jnp.mean(wide * wide, axis=-1, keepdims=True) + 1e-06)
        normed_rows[...] = (wide * scale * gain_ref[...]).astype(jnp.bfloat16)
        filt_acc[...] += jnp.dot(normed_rows[...], weight_ref[...], preferred_element_type=jnp.float32)

    @pl.when(half == 1)
    def _():
        gate_acc[...] += jnp.dot(normed_rows[...], weight_ref[...], preferred_element_type=jnp.float32)

    @pl.when((tap == pl.num_programs(0) - 1) & (half == 1))
    def _():
        out_ref[...] = (jnp.tanh(filt_acc[...]) * jax.nn.sigmoid(gate_acc[...])).astype(out_ref.dtype)


def convolution_gate(state, gain, conv_by_half, layer_idx, dilation_factor):
    hidden = state
    all_rows = hidden.shape[0]
    width = hidden.shape[1]
    taps = conv_by_half.shape[1]
    own_width = conv_by_half.shape[-1]
    border_rows = 2 * LARGEST_DILATION
    before = shifted(hidden[all_rows - border_rows :], "blk", 1)
    padded = jnp.concatenate([before, hidden], axis=0)
    slabs = jnp.stack(
        [
            lax.dynamic_slice_in_dim(padded, border_rows - tap_idx * dilation_factor, all_rows, 0)
            for tap_idx in range(taps)
        ]
    )
    return pl.pallas_call(
        conv_gate_kernel,
        out_shape=jax.ShapeDtypeStruct((all_rows, own_width), jnp.bfloat16),
        grid=(taps, 2),
        in_specs=[
            pl.BlockSpec((None, all_rows, width), lambda t, g: (t, 0, 0)),
            pl.BlockSpec((1, width), lambda t, g: (0, 0)),
            pl.BlockSpec((None, None, None, width, own_width), lambda t, g: (layer_idx, t, g, 0, 0)),
        ],
        out_specs=pl.BlockSpec((all_rows, own_width), lambda t, g: (0, 0)),
        scratch_shapes=[pltpu.VMEM((all_rows, own_width), jnp.float32)] * 2
        + [pltpu.VMEM((all_rows, width), jnp.bfloat16)],
        compiler_params=pltpu.CompilerParams(dimension_semantics=("arbitrary", "arbitrary")),
        cost_estimate=pl.CostEstimate(
            flops=4 * taps * all_rows * width * own_width,
            transcendentals=2 * all_rows * own_width,
            bytes_accessed=2 * taps * (all_rows * width + 2 * width * own_width + all_rows * own_width // taps),
        ),
    )(slabs, gain.reshape(1, width), conv_by_half)


def far_rows(ordered, tok_rows):
    return ordered[(lax.axis_size("head") // 2) * tok_rows :][:tok_rows]


def conv_share(gated, weight, tok_rows, tables):
    gated = ring_ordered(gated, "head", tables)

    def term(start, count):
        return rounded_term(gated, weight)

    return ring_scatter_sum(
        term(jnp.int32(0), tok_rows * lax.axis_size("head")).astype(jnp.bfloat16),
        "head",
        tables,
        far=rounded_term(far_rows(gated, tok_rows), weight).astype(jnp.bfloat16),
    )


def attention_portion_for(heads_out, out_block, tok_rows, tables):
    heads_out = ring_ordered(heads_out, "head", tables)

    def term(start, count):
        return rounded_term(heads_out, out_block)

    return ring_scatter_sum(
        term(jnp.int32(0), tok_rows * lax.axis_size("head")).astype(jnp.bfloat16),
        "head",
        tables,
        far=rounded_term(far_rows(heads_out, tok_rows), out_block).astype(jnp.bfloat16),
    )


def attend(queries, keys_in, values_in, causal):
    scale = queries.shape[1] ** (-0.5)
    scores = jnp.einsum("qd,kd->qk", queries, keys_in, preferred_element_type=jnp.float32) * scale
    if causal:
        rows_q = lax.broadcasted_iota(jnp.int32, scores.shape, 0)
        rows_k = lax.broadcasted_iota(jnp.int32, scores.shape, 1)
        scores = jnp.where(rows_q >= rows_k, scores, -1e30)
    peak = jnp.max(scores, axis=1)
    probs = jnp.exp(scores - peak[:, None])
    denom = jnp.sum(probs, axis=1)
    weighted = jnp.dot(probs.astype(jnp.bfloat16), values_in, preferred_element_type=jnp.float32)
    return (peak, denom, weighted)


def neutral(count, head_size):
    return (
        jnp.full((count,), -1e30, jnp.float32),
        jnp.zeros((count,), jnp.float32),
        jnp.zeros((count, head_size), jnp.float32),
    )


def combine(first, second):
    peak = jnp.maximum(first[0], second[0])
    scale_one = jnp.exp(first[0] - peak)
    scale_two = jnp.exp(second[0] - peak)
    denom = first[1] * scale_one + second[1] * scale_two
    weighted = first[2] * scale_one[:, None] + second[2] * scale_two[:, None]
    return (peak, denom, weighted)


def per_device(stream, gains, dilations, w_conv, w_mix, w_qkv, w_out):
    blk_pos = lax.axis_index("blk")
    tok_rows = stream.shape[0]
    width = stream.shape[1]
    head_size = w_qkv.shape[3]
    layers = w_conv.shape[0]
    share = stream
    tables = ring_tables("head")
    state = ring_gather(stream, "head", tables, direct=2)
    conv_by_half = jnp.transpose(w_conv, (0, 1, 3, 2, 4))
    for layer_idx in range(layers):
        gated = convolution_gate(
            state, gains[layer_idx], conv_by_half, layer_idx, dilations[layer_idx]
        )
        summed = conv_share(gated, w_mix[layer_idx], tok_rows, tables)
        share = (share.astype(jnp.float32) + summed).astype(jnp.bfloat16)
        state = ring_gather(share, "head", tables)
    all_rows = state.shape[0]
    attn_in = normed(state, gains[layers])
    qkv_parts = jnp.transpose(w_qkv[:, :, 0, :], (1, 0, 2))
    queries, keys_own, values_own = (
        jnp.dot(attn_in, qkv_parts[i], preferred_element_type=jnp.float32).astype(jnp.bfloat16)
        for i in range(3)
    )
    keys_prev, values_prev = shifted((keys_own, values_own), "blk", 1)
    own_part = attend(queries, keys_own, values_own, True)
    crossing_portion = lax.cond(
        blk_pos > 0,
        lambda: attend(queries, keys_prev, values_prev, False),
        lambda: neutral(all_rows, head_size),
    )
    peak, denom, weighted = combine(own_part, crossing_portion)
    heads_out = (weighted / denom[:, None]).astype(jnp.bfloat16)
    attn_share = attention_portion_for(heads_out, w_out[0], tok_rows, tables)
    return (share.astype(jnp.float32) + attn_share).astype(jnp.bfloat16)


def solution(mesh):
    placed = (
        P(("grp", "blk", "head"), None),
        P(),
        P(),
        P(None, None, None, None, "head"),
        P(None, "head", None),
        P(None, None, "head", None),
        P("head", None, None),
    )
    return jax.shard_map(
        per_device,
        mesh=mesh,
        in_specs=placed,
        out_specs=P(("grp", "blk", "head"), None),
        check_vma=False,
    )
```

```python
import jax
import jax.numpy as jnp
from jax import lax
from jax.sharding import PartitionSpec as P
from jax.experimental import pallas as pl
from jax.experimental.pallas import tpu as pltpu

LARGEST_DILATION = 64


def shifted(value, axis, by):
    length = lax.axis_size(axis)
    pairs = [(i, i + by) for i in range(length) if 0 <= i + by < length]
    return lax.ppermute(value, axis, pairs)


def ring_order(length):
    if length % 2:
        return list(range(length))
    return list(range(0, length, 2)) + list(range(length - 1, 0, -2))


def ring_tables(axis):
    length = lax.axis_size(axis)
    order = ring_order(length)
    place = [0] * length
    for p, h in enumerate(order):
        place[h] = p
    head_at = [[order[(place[h] + m) % length] for m in range(length)] for h in range(length)]
    offset_of = [[(place[j] - place[h]) % length for j in range(length)] for h in range(length)]
    table = jnp.array([head_at, offset_of], jnp.int32)
    mine = lax.dynamic_index_in_dim(table, lax.axis_index(axis), 1, keepdims=False)
    return mine[0], mine[1]


def ring_pairs(length):
    order = ring_order(length)
    forward = [(order[p], order[(p + 1) % length]) for p in range(length)]
    backward = [(order[p], order[(p - 1) % length]) for p in range(length)]
    return forward, backward


def ring_gather(value, axis, tables, direct=1):
    length = lax.axis_size(axis)
    forward, backward = ring_pairs(length)
    order = ring_order(length)
    ahead = length // 2
    behind = length - 1 - ahead
    direct = max(1, min(direct, behind))
    rows = value.shape[0]
    split = behind < ahead and rows % 2 == 0
    half = rows // 2
    pieces = [None] * length
    pieces[0] = value
    fwd = value
    bwd = value
    for k in range(1, direct + 1):
        fwd = lax.ppermute(value, axis, [(order[p], order[(p + k) % length]) for p in range(length)])
        bwd = lax.ppermute(value, axis, [(order[p], order[(p - k) % length]) for p in range(length)])
        pieces[length - k] = fwd
        pieces[k] = bwd
    for k in range(direct + 1, ahead + 1):
        if k == ahead and split:
            fwd = lax.ppermute(fwd[:half], axis, forward)
            bwd = lax.ppermute(bwd[half:], axis, backward)
            pieces[k] = jnp.concatenate([fwd, bwd], axis=0)
            break
        fwd = lax.ppermute(fwd, axis, forward)
        pieces[length - k] = fwd
        if k <= behind:
            bwd = lax.ppermute(bwd, axis, backward)
            pieces[k] = bwd
    stacked = jnp.stack(pieces)
    return jnp.take(stacked, tables[1], axis=0, mode="clip").reshape((length * rows,) + value.shape[1:])


def ring_ordered(rows_in, axis, tables):
    length = lax.axis_size(axis)
    blocks = rows_in.reshape((length, rows_in.shape[0] // length) + rows_in.shape[1:])
    return jnp.take(blocks, tables[0], axis=0, mode="clip").reshape(rows_in.shape)


def ring_scatter_sum(value, axis, tables, far=None):
    length = lax.axis_size(axis)
    forward, backward = ring_pairs(length)
    ahead = length // 2
    behind = length - 1 - ahead
    rows = value.shape[0] // length
    split = behind < ahead and rows % 2 == 0
    half = rows // 2
    by_offset = value.reshape((length, rows) + value.shape[1:])

    def own(offset):
        if far is not None and offset % length == ahead:
            return far.astype(jnp.float32)
        return by_offset[offset % length].astype(jnp.float32)

    def chain(offsets, pairs, first_rows):
        passed = None
        for step, offset in enumerate(offsets):
            part = own(offset)
            if step == 0:
                part = part[first_rows]
            elif step == 1 and passed.shape[0] != rows:
                part = part.at[first_rows].add(passed.astype(jnp.float32))
            else:
                part = part + passed.astype(jnp.float32)
            passed = lax.ppermute(part.astype(value.dtype), axis, pairs)
        return passed

    fwd_offsets = list(range(ahead, 0, -1))
    bwd_offsets = list(range(-behind, 0))
    fwd_rows = slice(0, rows)
    bwd_rows = slice(0, rows)
    if split:
        bwd_offsets = [-ahead] + bwd_offsets
        fwd_rows = slice(0, half)
        bwd_rows = slice(half, rows)
    total = own(0)
    total = total + chain(fwd_offsets, forward, fwd_rows).astype(jnp.float32)
    if bwd_offsets:
        total = total + chain(bwd_offsets, backward, bwd_rows).astype(jnp.float32)
    return total


def normed(values, gain):
    wide = values.astype(jnp.float32)
    scale = lax.rsqrt(jnp.mean(wide * wide, axis=-1, keepdims=True) + 1e-06)
    return (wide * scale * gain).astype(jnp.bfloat16)


def rounded_term(left, right):
    term = jnp.dot(left, right, preferred_element_type=jnp.float32)
    return lax.optimization_barrier(term.astype(jnp.bfloat16)).astype(jnp.float32)


def conv_gate_kernel(slab_ref, gain_ref, weight_ref, out_ref, filt_acc, gate_acc):
    tap = pl.program_id(0)
    chunk = pl.program_id(1)

    @pl.when((tap == 0) & (chunk == 0))
    def _():
        filt_acc[...] = jnp.zeros_like(filt_acc)
        gate_acc[...] = jnp.zeros_like(gate_acc)

    wide = slab_ref[...].astype(jnp.float32)
    scale = lax.rsqrt(jnp.mean(wide * wide, axis=-1, keepdims=True) + 1e-06)
    rows = (wide * scale * gain_ref[...]).astype(jnp.bfloat16)
    filt_acc[...] += jnp.dot(rows, weight_ref[0], preferred_element_type=jnp.float32)
    gate_acc[...] += jnp.dot(rows, weight_ref[1], preferred_element_type=jnp.float32)

    @pl.when((tap == pl.num_programs(0) - 1) & (chunk == pl.num_programs(1) - 1))
    def _():
        out_ref[...] = (jnp.tanh(filt_acc[...]) * jax.nn.sigmoid(gate_acc[...])).astype(out_ref.dtype)


def convolution_gate(state, gain, conv_by_half, layer_idx, dilation_factor):
    hidden = state
    all_rows = hidden.shape[0]
    width = hidden.shape[1]
    taps = conv_by_half.shape[1]
    own_width = conv_by_half.shape[-1]
    border_rows = 2 * LARGEST_DILATION
    before = shifted(hidden[all_rows - border_rows :], "blk", 1)
    padded = jnp.concatenate([before, hidden], axis=0)
    slabs = jnp.stack(
        [
            lax.dynamic_slice_in_dim(padded, border_rows - tap_idx * dilation_factor, all_rows, 0)
            for tap_idx in range(taps)
        ]
    )
    chunk = width
    return pl.pallas_call(
        conv_gate_kernel,
        out_shape=jax.ShapeDtypeStruct((all_rows, own_width), jnp.bfloat16),
        grid=(taps, width // chunk),
        in_specs=[
            pl.BlockSpec((None, all_rows, chunk), lambda t, k: (t, 0, k)),
            pl.BlockSpec((1, width), lambda t, k: (0, 0)),
            pl.BlockSpec((None, None, 2, chunk, own_width), lambda t, k: (layer_idx, t, 0, k, 0)),
        ],
        out_specs=pl.BlockSpec((all_rows, own_width), lambda t, k: (0, 0)),
        scratch_shapes=[pltpu.VMEM((all_rows, own_width), jnp.float32)] * 2,
        compiler_params=pltpu.CompilerParams(dimension_semantics=("arbitrary", "arbitrary")),
        cost_estimate=pl.CostEstimate(
            flops=4 * taps * all_rows * width * own_width,
            transcendentals=2 * all_rows * own_width,
            bytes_accessed=2 * taps * (all_rows * width + 2 * width * own_width + all_rows * own_width // taps),
        ),
    )(slabs, gain.reshape(1, width), conv_by_half)


def far_rows(ordered, tok_rows):
    return ordered[(lax.axis_size("head") // 2) * tok_rows :][:tok_rows]


def conv_share(gated, weight, tok_rows, tables):
    gated = ring_ordered(gated, "head", tables)

    def term(start, count):
        return rounded_term(gated, weight)

    return ring_scatter_sum(
        term(jnp.int32(0), tok_rows * lax.axis_size("head")).astype(jnp.bfloat16),
        "head",
        tables,
        far=rounded_term(far_rows(gated, tok_rows), weight).astype(jnp.bfloat16),
    )


def attention_portion_for(heads_out, out_block, tok_rows, tables):
    heads_out = ring_ordered(heads_out, "head", tables)

    def term(start, count):
        return rounded_term(heads_out, out_block)

    return ring_scatter_sum(
        term(jnp.int32(0), tok_rows * lax.axis_size("head")).astype(jnp.bfloat16),
        "head",
        tables,
        far=rounded_term(far_rows(heads_out, tok_rows), out_block).astype(jnp.bfloat16),
    )


def attend(queries, keys_in, values_in, causal):
    scale = queries.shape[1] ** (-0.5)
    scores = jnp.einsum("qd,kd->qk", queries, keys_in, preferred_element_type=jnp.float32) * scale
    if causal:
        rows_q = lax.broadcasted_iota(jnp.int32, scores.shape, 0)
        rows_k = lax.broadcasted_iota(jnp.int32, scores.shape, 1)
        scores = jnp.where(rows_q >= rows_k, scores, -1e30)
    peak = jnp.max(scores, axis=1)
    probs = jnp.exp(scores - peak[:, None])
    denom = jnp.sum(probs, axis=1)
    weighted = jnp.dot(probs.astype(jnp.bfloat16), values_in, preferred_element_type=jnp.float32)
    return (peak, denom, weighted)


def neutral(count, head_size):
    return (
        jnp.full((count,), -1e30, jnp.float32),
        jnp.zeros((count,), jnp.float32),
        jnp.zeros((count, head_size), jnp.float32),
    )


def combine(first, second):
    peak = jnp.maximum(first[0], second[0])
    scale_one = jnp.exp(first[0] - peak)
    scale_two = jnp.exp(second[0] - peak)
    denom = first[1] * scale_one + second[1] * scale_two
    weighted = first[2] * scale_one[:, None] + second[2] * scale_two[:, None]
    return (peak, denom, weighted)


def per_device(stream, gains, dilations, w_conv, w_mix, w_qkv, w_out):
    blk_pos = lax.axis_index("blk")
    tok_rows = stream.shape[0]
    width = stream.shape[1]
    head_size = w_qkv.shape[3]
    layers = w_conv.shape[0]
    share = stream
    tables = ring_tables("head")
    state = ring_gather(stream, "head", tables, direct=3)
    conv_by_half = jnp.transpose(w_conv, (0, 1, 3, 2, 4))
    for layer_idx in range(layers):
        gated = convolution_gate(
            state, gains[layer_idx], conv_by_half, layer_idx, dilations[layer_idx]
        )
        summed = conv_share(gated, w_mix[layer_idx], tok_rows, tables)
        share = (share.astype(jnp.float32) + summed).astype(jnp.bfloat16)
        state = ring_gather(share, "head", tables)
    all_rows = state.shape[0]
    attn_in = normed(state, gains[layers])
    qkv_parts = jnp.transpose(w_qkv[:, :, 0, :], (1, 0, 2))
    queries, keys_own, values_own = (
        jnp.dot(attn_in, qkv_parts[i], preferred_element_type=jnp.float32).astype(jnp.bfloat16)
        for i in range(3)
    )
    keys_prev, values_prev = shifted((keys_own, values_own), "blk", 1)
    own_part = attend(queries, keys_own, values_own, True)
    crossing_portion = lax.cond(
        blk_pos > 0,
        lambda: attend(queries, keys_prev, values_prev, False),
        lambda: neutral(all_rows, head_size),
    )
    peak, denom, weighted = combine(own_part, crossing_portion)
    heads_out = (weighted / denom[:, None]).astype(jnp.bfloat16)
    attn_share = attention_portion_for(heads_out, w_out[0], tok_rows, tables)
    return (share.astype(jnp.float32) + attn_share).astype(jnp.bfloat16)


def solution(mesh):
    placed = (
        P(("grp", "blk", "head"), None),
        P(),
        P(),
        P(None, None, None, None, "head"),
        P(None, "head", None),
        P(None, None, "head", None),
        P("head", None, None),
    )
    return jax.shard_map(
        per_device,
        mesh=mesh,
        in_specs=placed,
        out_specs=P(("grp", "blk", "head"), None),
        check_vma=False,
    )
```

```python
import jax
import jax.numpy as jnp
from jax import lax
from jax.sharding import PartitionSpec as P
from jax.experimental import pallas as pl
from jax.experimental.pallas import tpu as pltpu

LARGEST_DILATION = 64


def shifted(value, axis, by):
    length = lax.axis_size(axis)
    pairs = [(i, i + by) for i in range(length) if 0 <= i + by < length]
    return lax.ppermute(value, axis, pairs)


def ring_order(length):
    if length % 2:
        return list(range(length))
    return list(range(0, length, 2)) + list(range(length - 1, 0, -2))


def ring_tables(axis):
    length = lax.axis_size(axis)
    order = ring_order(length)
    place = [0] * length
    for p, h in enumerate(order):
        place[h] = p
    head_at = [[order[(place[h] + m) % length] for m in range(length)] for h in range(length)]
    offset_of = [[(place[j] - place[h]) % length for j in range(length)] for h in range(length)]
    table = jnp.array([head_at, offset_of], jnp.int32)
    mine = lax.dynamic_index_in_dim(table, lax.axis_index(axis), 1, keepdims=False)
    return mine[0], mine[1]


def ring_pairs(length):
    order = ring_order(length)
    forward = [(order[p], order[(p + 1) % length]) for p in range(length)]
    backward = [(order[p], order[(p - 1) % length]) for p in range(length)]
    return forward, backward


def ring_gather(value, axis, tables, direct=1, tail_rows=0):
    length = lax.axis_size(axis)
    forward, backward = ring_pairs(length)
    order = ring_order(length)
    ahead = length // 2
    behind = length - 1 - ahead
    direct = max(1, min(direct, behind))
    rows = value.shape[0]
    split = behind < ahead and rows % 2 == 0
    half = rows // 2
    pieces = [None] * length
    pieces[0] = value
    fwd = value
    bwd = value
    for k in range(1, direct + 1):
        fwd = lax.ppermute(value, axis, [(order[p], order[(p + k) % length]) for p in range(length)])
        bwd = lax.ppermute(value, axis, [(order[p], order[(p - k) % length]) for p in range(length)])
        pieces[length - k] = fwd
        pieces[k] = bwd
    for k in range(direct + 1, ahead + 1):
        if k == ahead and split:
            fwd = lax.ppermute(fwd[:half], axis, forward)
            bwd = lax.ppermute(bwd[half:], axis, backward)
            pieces[k] = jnp.concatenate([fwd, bwd], axis=0)
            break
        fwd = lax.ppermute(fwd, axis, forward)
        pieces[length - k] = fwd
        if k <= behind:
            bwd = lax.ppermute(bwd, axis, backward)
            pieces[k] = bwd
    stacked = jnp.stack(pieces)
    whole = jnp.take(stacked, tables[1], axis=0, mode="clip").reshape((length * rows,) + value.shape[1:])
    if not tail_rows:
        return whole
    tail_blocks = tail_rows // rows
    tail = jnp.take(stacked, tables[1][length - tail_blocks :], axis=0, mode="clip")
    return whole, tail.reshape((tail_rows,) + value.shape[1:])


def ring_ordered(rows_in, axis, tables):
    length = lax.axis_size(axis)
    blocks = rows_in.reshape((length, rows_in.shape[0] // length) + rows_in.shape[1:])
    return jnp.take(blocks, tables[0], axis=0, mode="clip").reshape(rows_in.shape)


def ring_scatter_sum(value, axis, tables, far=None):
    length = lax.axis_size(axis)
    forward, backward = ring_pairs(length)
    ahead = length // 2
    behind = length - 1 - ahead
    rows = value.shape[0] // length
    split = behind < ahead and rows % 2 == 0
    half = rows // 2
    by_offset = value.reshape((length, rows) + value.shape[1:])

    def own(offset):
        if far is not None and offset % length == ahead:
            return far.astype(jnp.float32)
        return by_offset[offset % length].astype(jnp.float32)

    def chain(offsets, pairs, first_rows):
        passed = None
        for step, offset in enumerate(offsets):
            part = own(offset)
            if step == 0:
                part = part[first_rows]
            elif step == 1 and passed.shape[0] != rows:
                part = part.at[first_rows].add(passed.astype(jnp.float32))
            else:
                part = part + passed.astype(jnp.float32)
            passed = lax.ppermute(part.astype(value.dtype), axis, pairs)
        return passed

    fwd_offsets = list(range(ahead, 0, -1))
    bwd_offsets = list(range(-behind, 0))
    fwd_rows = slice(0, rows)
    bwd_rows = slice(0, rows)
    if split:
        bwd_offsets = [-ahead] + bwd_offsets
        fwd_rows = slice(0, half)
        bwd_rows = slice(half, rows)
    total = own(0)
    total = total + chain(fwd_offsets, forward, fwd_rows).astype(jnp.float32)
    if bwd_offsets:
        total = total + chain(bwd_offsets, backward, bwd_rows).astype(jnp.float32)
    return total


def normed(values, gain):
    wide = values.astype(jnp.float32)
    scale = lax.rsqrt(jnp.mean(wide * wide, axis=-1, keepdims=True) + 1e-06)
    return (wide * scale * gain).astype(jnp.bfloat16)


def rounded_term(left, right):
    term = jnp.dot(left, right, preferred_element_type=jnp.float32)
    return lax.optimization_barrier(term.astype(jnp.bfloat16)).astype(jnp.float32)


def conv_gate_kernel(slab_ref, gain_ref, weight_ref, out_ref, filt_acc, gate_acc):
    tap = pl.program_id(0)
    chunk = pl.program_id(1)

    @pl.when((tap == 0) & (chunk == 0))
    def _():
        filt_acc[...] = jnp.zeros_like(filt_acc)
        gate_acc[...] = jnp.zeros_like(gate_acc)

    wide = slab_ref[...].astype(jnp.float32)
    scale = lax.rsqrt(jnp.mean(wide * wide, axis=-1, keepdims=True) + 1e-06)
    rows = (wide * scale * gain_ref[...]).astype(jnp.bfloat16)
    filt_acc[...] += jnp.dot(rows, weight_ref[0], preferred_element_type=jnp.float32)
    gate_acc[...] += jnp.dot(rows, weight_ref[1], preferred_element_type=jnp.float32)

    @pl.when((tap == pl.num_programs(0) - 1) & (chunk == pl.num_programs(1) - 1))
    def _():
        out_ref[...] = (jnp.tanh(filt_acc[...]) * jax.nn.sigmoid(gate_acc[...])).astype(out_ref.dtype)


def convolution_gate(state, tail, gain, conv_by_half, layer_idx, dilation_factor):
    hidden = state
    all_rows = hidden.shape[0]
    width = hidden.shape[1]
    taps = conv_by_half.shape[1]
    own_width = conv_by_half.shape[-1]
    border_rows = 2 * LARGEST_DILATION
    before = shifted(tail, "blk", 1)
    padded = jnp.concatenate([before, hidden], axis=0)
    slabs = jnp.stack(
        [
            lax.dynamic_slice_in_dim(padded, border_rows - tap_idx * dilation_factor, all_rows, 0)
            for tap_idx in range(taps)
        ]
    )
    chunk = width
    return pl.pallas_call(
        conv_gate_kernel,
        out_shape=jax.ShapeDtypeStruct((all_rows, own_width), jnp.bfloat16),
        grid=(taps, width // chunk),
        in_specs=[
            pl.BlockSpec((None, all_rows, chunk), lambda t, k: (t, 0, k)),
            pl.BlockSpec((1, width), lambda t, k: (0, 0)),
            pl.BlockSpec((None, None, 2, chunk, own_width), lambda t, k: (layer_idx, t, 0, k, 0)),
        ],
        out_specs=pl.BlockSpec((all_rows, own_width), lambda t, k: (0, 0)),
        scratch_shapes=[pltpu.VMEM((all_rows, own_width), jnp.float32)] * 2,
        compiler_params=pltpu.CompilerParams(dimension_semantics=("arbitrary", "arbitrary")),
        cost_estimate=pl.CostEstimate(
            flops=4 * taps * all_rows * width * own_width,
            transcendentals=2 * all_rows * own_width,
            bytes_accessed=2 * taps * (all_rows * width + 2 * width * own_width + all_rows * own_width // taps),
        ),
    )(slabs, gain.reshape(1, width), conv_by_half)


def far_rows(ordered, tok_rows):
    return ordered[(lax.axis_size("head") // 2) * tok_rows :][:tok_rows]


def conv_share(gated, weight, tok_rows, tables):
    gated = ring_ordered(gated, "head", tables)

    def term(start, count):
        return rounded_term(gated, weight)

    return ring_scatter_sum(
        term(jnp.int32(0), tok_rows * lax.axis_size("head")).astype(jnp.bfloat16),
        "head",
        tables,
        far=rounded_term(far_rows(gated, tok_rows), weight).astype(jnp.bfloat16),
    )


def attention_portion_for(heads_out, out_block, tok_rows, tables):
    heads_out = ring_ordered(heads_out, "head", tables)

    def term(start, count):
        return rounded_term(heads_out, out_block)

    return ring_scatter_sum(
        term(jnp.int32(0), tok_rows * lax.axis_size("head")).astype(jnp.bfloat16),
        "head",
        tables,
        far=rounded_term(far_rows(heads_out, tok_rows), out_block).astype(jnp.bfloat16),
    )


def attend(queries, keys_in, values_in, causal):
    scale = queries.shape[1] ** (-0.5)
    scores = jnp.einsum("qd,kd->qk", queries, keys_in, preferred_element_type=jnp.float32) * scale
    if causal:
        rows_q = lax.broadcasted_iota(jnp.int32, scores.shape, 0)
        rows_k = lax.broadcasted_iota(jnp.int32, scores.shape, 1)
        scores = jnp.where(rows_q >= rows_k, scores, -1e30)
    peak = jnp.max(scores, axis=1)
    probs = jnp.exp(scores - peak[:, None])
    denom = jnp.sum(probs, axis=1)
    weighted = jnp.dot(probs.astype(jnp.bfloat16), values_in, preferred_element_type=jnp.float32)
    return (peak, denom, weighted)


def neutral(count, head_size):
    return (
        jnp.full((count,), -1e30, jnp.float32),
        jnp.zeros((count,), jnp.float32),
        jnp.zeros((count, head_size), jnp.float32),
    )


def combine(first, second):
    peak = jnp.maximum(first[0], second[0])
    scale_one = jnp.exp(first[0] - peak)
    scale_two = jnp.exp(second[0] - peak)
    denom = first[1] * scale_one + second[1] * scale_two
    weighted = first[2] * scale_one[:, None] + second[2] * scale_two[:, None]
    return (peak, denom, weighted)


def per_device(stream, gains, dilations, w_conv, w_mix, w_qkv, w_out):
    blk_pos = lax.axis_index("blk")
    tok_rows = stream.shape[0]
    width = stream.shape[1]
    head_size = w_qkv.shape[3]
    layers = w_conv.shape[0]
    share = stream
    tables = ring_tables("head")
    border_rows = 2 * LARGEST_DILATION
    state, tail = ring_gather(stream, "head", tables, direct=2, tail_rows=border_rows)
    conv_by_half = jnp.transpose(w_conv, (0, 1, 3, 2, 4))
    for layer_idx in range(layers):
        gated = convolution_gate(
            state, tail, gains[layer_idx], conv_by_half, layer_idx, dilations[layer_idx]
        )
        summed = conv_share(gated, w_mix[layer_idx], tok_rows, tables)
        share = (share.astype(jnp.float32) + summed).astype(jnp.bfloat16)
        if layer_idx + 1 < layers:
            state, tail = ring_gather(share, "head", tables, tail_rows=border_rows)
        else:
            state = ring_gather(share, "head", tables)
    all_rows = state.shape[0]
    attn_in = normed(state, gains[layers])
    qkv_parts = jnp.transpose(w_qkv[:, :, 0, :], (1, 0, 2))
    queries, keys_own, values_own = (
        jnp.dot(attn_in, qkv_parts[i], preferred_element_type=jnp.float32).astype(jnp.bfloat16)
        for i in range(3)
    )
    keys_prev, values_prev = shifted((keys_own, values_own), "blk", 1)
    own_part = attend(queries, keys_own, values_own, True)
    crossing_portion = lax.cond(
        blk_pos > 0,
        lambda: attend(queries, keys_prev, values_prev, False),
        lambda: neutral(all_rows, head_size),
    )
    peak, denom, weighted = combine(own_part, crossing_portion)
    heads_out = (weighted / denom[:, None]).astype(jnp.bfloat16)
    attn_share = attention_portion_for(heads_out, w_out[0], tok_rows, tables)
    return (share.astype(jnp.float32) + attn_share).astype(jnp.bfloat16)


def solution(mesh):
    placed = (
        P(("grp", "blk", "head"), None),
        P(),
        P(),
        P(None, None, None, None, "head"),
        P(None, "head", None),
        P(None, None, "head", None),
        P("head", None, None),
    )
    return jax.shard_map(
        per_device,
        mesh=mesh,
        in_specs=placed,
        out_specs=P(("grp", "blk", "head"), None),
        check_vma=False,
    )
```

```python
import jax
import jax.numpy as jnp
from jax import lax
from jax.sharding import PartitionSpec as P
from jax.experimental import pallas as pl
from jax.experimental.pallas import tpu as pltpu

LARGEST_DILATION = 64


def shifted(value, axis, by):
    length = lax.axis_size(axis)
    pairs = [(i, i + by) for i in range(length) if 0 <= i + by < length]
    return lax.ppermute(value, axis, pairs)


def ring_order(length):
    if length % 2:
        return list(range(length))
    return list(range(0, length, 2)) + list(range(length - 1, 0, -2))


def ring_tables(axis):
    length = lax.axis_size(axis)
    order = ring_order(length)
    place = [0] * length
    for p, h in enumerate(order):
        place[h] = p
    head_at = [[order[(place[h] + m) % length] for m in range(length)] for h in range(length)]
    offset_of = [[(place[j] - place[h]) % length for j in range(length)] for h in range(length)]
    table = jnp.array([head_at, offset_of], jnp.int32)
    mine = lax.dynamic_index_in_dim(table, lax.axis_index(axis), 1, keepdims=False)
    return mine[0], mine[1]


def ring_pairs(length):
    order = ring_order(length)
    forward = [(order[p], order[(p + 1) % length]) for p in range(length)]
    backward = [(order[p], order[(p - 1) % length]) for p in range(length)]
    return forward, backward


def ring_gather(value, axis, tables, direct=1, tail_rows=0):
    length = lax.axis_size(axis)
    forward, backward = ring_pairs(length)
    order = ring_order(length)
    ahead = length // 2
    behind = length - 1 - ahead
    direct = max(1, min(direct, behind))
    rows = value.shape[0]
    split = behind < ahead and rows % 2 == 0
    half = rows // 2
    pieces = [None] * length
    pieces[0] = value
    fwd = value
    bwd = value
    for k in range(1, direct + 1):
        fwd = lax.ppermute(value, axis, [(order[p], order[(p + k) % length]) for p in range(length)])
        bwd = lax.ppermute(value, axis, [(order[p], order[(p - k) % length]) for p in range(length)])
        pieces[length - k] = fwd
        pieces[k] = bwd
    for k in range(direct + 1, ahead + 1):
        if k == ahead and split:
            fwd = lax.ppermute(fwd[:half], axis, forward)
            bwd = lax.ppermute(bwd[half:], axis, backward)
            pieces[k] = jnp.concatenate([fwd, bwd], axis=0)
            break
        fwd = lax.ppermute(fwd, axis, forward)
        pieces[length - k] = fwd
        if k <= behind:
            bwd = lax.ppermute(bwd, axis, backward)
            pieces[k] = bwd
    stacked = jnp.stack(pieces)
    whole = jnp.take(stacked, tables[1], axis=0, mode="clip").reshape((length * rows,) + value.shape[1:])
    if not tail_rows:
        return whole
    tail_blocks = tail_rows // rows
    tail = jnp.take(stacked, tables[1][length - tail_blocks :], axis=0, mode="clip")
    return whole, tail.reshape((tail_rows,) + value.shape[1:])


def ring_ordered(rows_in, axis, tables):
    length = lax.axis_size(axis)
    blocks = rows_in.reshape((length, rows_in.shape[0] // length) + rows_in.shape[1:])
    return jnp.take(blocks, tables[0], axis=0, mode="clip").reshape(rows_in.shape)


def ring_scatter_sum(value, axis, tables, far=None):
    length = lax.axis_size(axis)
    forward, backward = ring_pairs(length)
    ahead = length // 2
    behind = length - 1 - ahead
    rows = value.shape[0] // length
    split = behind < ahead and rows % 2 == 0
    half = rows // 2
    by_offset = value.reshape((length, rows) + value.shape[1:])

    def own(offset):
        if far is not None and offset % length == ahead:
            return far.astype(jnp.float32)
        return by_offset[offset % length].astype(jnp.float32)

    def chain(offsets, pairs, first_rows):
        passed = None
        for step, offset in enumerate(offsets):
            part = own(offset)
            if step == 0:
                part = part[first_rows]
            elif step == 1 and passed.shape[0] != rows:
                part = part.at[first_rows].add(passed.astype(jnp.float32))
            else:
                part = part + passed.astype(jnp.float32)
            passed = lax.ppermute(part.astype(value.dtype), axis, pairs)
        return passed

    fwd_offsets = list(range(ahead, 0, -1))
    bwd_offsets = list(range(-behind, 0))
    fwd_rows = slice(0, rows)
    bwd_rows = slice(0, rows)
    if split:
        bwd_offsets = [-ahead] + bwd_offsets
        fwd_rows = slice(0, half)
        bwd_rows = slice(half, rows)
    total = own(0)
    total = total + chain(fwd_offsets, forward, fwd_rows).astype(jnp.float32)
    if bwd_offsets:
        total = total + chain(bwd_offsets, backward, bwd_rows).astype(jnp.float32)
    return total


def normed(values, gain):
    wide = values.astype(jnp.float32)
    scale = lax.rsqrt(jnp.mean(wide * wide, axis=-1, keepdims=True) + 1e-06)
    return (wide * scale * gain).astype(jnp.bfloat16)


def rounded_term(left, right):
    term = jnp.dot(left, right, preferred_element_type=jnp.float32)
    return lax.optimization_barrier(term.astype(jnp.bfloat16)).astype(jnp.float32)


def conv_gate_kernel(slab_ref, gain_ref, weight_ref, out_ref, filt_acc, gate_acc):
    tap = pl.program_id(0)
    chunk = pl.program_id(1)

    @pl.when((tap == 0) & (chunk == 0))
    def _():
        filt_acc[...] = jnp.zeros_like(filt_acc)
        gate_acc[...] = jnp.zeros_like(gate_acc)

    wide = slab_ref[...].astype(jnp.float32)
    scale = lax.rsqrt(jnp.mean(wide * wide, axis=-1, keepdims=True) + 1e-06)
    rows = (wide * scale * gain_ref[...]).astype(jnp.bfloat16)
    filt_acc[...] += jnp.dot(rows, weight_ref[0], preferred_element_type=jnp.float32)
    gate_acc[...] += jnp.dot(rows, weight_ref[1], preferred_element_type=jnp.float32)

    @pl.when((tap == pl.num_programs(0) - 1) & (chunk == pl.num_programs(1) - 1))
    def _():
        out_ref[...] = (jnp.tanh(filt_acc[...]) * jax.nn.sigmoid(gate_acc[...])).astype(out_ref.dtype)


def convolution_gate(state, tail, gain, conv_by_half, layer_idx, dilation_factor):
    hidden = state
    all_rows = hidden.shape[0]
    width = hidden.shape[1]
    taps = conv_by_half.shape[1]
    own_width = conv_by_half.shape[-1]
    border_rows = 2 * LARGEST_DILATION
    before = shifted(tail, "blk", 1)
    padded = jnp.concatenate([before, hidden], axis=0)
    slabs = jnp.stack(
        [
            lax.dynamic_slice_in_dim(padded, border_rows - tap_idx * dilation_factor, all_rows, 0)
            for tap_idx in range(taps)
        ]
    )
    chunk = width
    return pl.pallas_call(
        conv_gate_kernel,
        out_shape=jax.ShapeDtypeStruct((all_rows, own_width), jnp.bfloat16),
        grid=(taps, width // chunk),
        in_specs=[
            pl.BlockSpec((None, all_rows, chunk), lambda t, k: (t, 0, k)),
            pl.BlockSpec((1, width), lambda t, k: (0, 0)),
            pl.BlockSpec((None, None, 2, chunk, own_width), lambda t, k: (layer_idx, t, 0, k, 0)),
        ],
        out_specs=pl.BlockSpec((all_rows, own_width), lambda t, k: (0, 0)),
        scratch_shapes=[pltpu.VMEM((all_rows, own_width), jnp.float32)] * 2,
        compiler_params=pltpu.CompilerParams(dimension_semantics=("arbitrary", "arbitrary")),
        cost_estimate=pl.CostEstimate(
            flops=4 * taps * all_rows * width * own_width,
            transcendentals=2 * all_rows * own_width,
            bytes_accessed=2 * taps * (all_rows * width + 2 * width * own_width + all_rows * own_width // taps),
        ),
    )(slabs, gain.reshape(1, width), conv_by_half)


def far_rows(ordered, tok_rows):
    return ordered[(lax.axis_size("head") // 2) * tok_rows :][:tok_rows]


def conv_share(gated, weight, tok_rows, tables):
    gated = ring_ordered(gated, "head", tables)

    def term(start, count):
        return rounded_term(gated, weight)

    return ring_scatter_sum(
        term(jnp.int32(0), tok_rows * lax.axis_size("head")).astype(jnp.bfloat16),
        "head",
        tables,
        far=rounded_term(far_rows(gated, tok_rows), weight).astype(jnp.bfloat16),
    )


def attention_portion_for(heads_out, out_block, tok_rows, tables):
    heads_out = ring_ordered(heads_out, "head", tables)

    def term(start, count):
        return rounded_term(heads_out, out_block)

    return ring_scatter_sum(
        term(jnp.int32(0), tok_rows * lax.axis_size("head")).astype(jnp.bfloat16),
        "head",
        tables,
        far=rounded_term(far_rows(heads_out, tok_rows), out_block).astype(jnp.bfloat16),
    )


def attend(queries, keys_in, values_in, causal):
    scale = queries.shape[1] ** (-0.5)
    scores = jnp.einsum("qd,kd->qk", queries, keys_in, preferred_element_type=jnp.float32) * scale
    if causal:
        rows_q = lax.broadcasted_iota(jnp.int32, scores.shape, 0)
        rows_k = lax.broadcasted_iota(jnp.int32, scores.shape, 1)
        scores = jnp.where(rows_q >= rows_k, scores, -1e30)
    peak = jnp.max(scores, axis=1)
    probs = jnp.exp(scores - peak[:, None])
    denom = jnp.sum(probs, axis=1)
    weighted = jnp.dot(probs.astype(jnp.bfloat16), values_in, preferred_element_type=jnp.float32)
    return (peak, denom, weighted)


def neutral(count, head_size):
    return (
        jnp.full((count,), -1e30, jnp.float32),
        jnp.zeros((count,), jnp.float32),
        jnp.zeros((count, head_size), jnp.float32),
    )


def combine(first, second):
    peak = jnp.maximum(first[0], second[0])
    scale_one = jnp.exp(first[0] - peak)
    scale_two = jnp.exp(second[0] - peak)
    denom = first[1] * scale_one + second[1] * scale_two
    weighted = first[2] * scale_one[:, None] + second[2] * scale_two[:, None]
    return (peak, denom, weighted)


def per_device(stream, gains, dilations, w_conv, w_mix, w_qkv, w_out):
    blk_pos = lax.axis_index("blk")
    tok_rows = stream.shape[0]
    width = stream.shape[1]
    head_size = w_qkv.shape[3]
    layers = w_conv.shape[0]
    share = stream
    tables = ring_tables("head")
    border_rows = 2 * LARGEST_DILATION
    state, tail = ring_gather(stream, "head", tables, direct=2, tail_rows=border_rows)
    conv_by_half = jnp.transpose(w_conv, (0, 1, 3, 2, 4))
    for layer_idx in range(layers):
        gated = convolution_gate(
            state, tail, gains[layer_idx], conv_by_half, layer_idx, dilations[layer_idx]
        )
        summed = conv_share(gated, w_mix[layer_idx], tok_rows, tables)
        share = (share.astype(jnp.float32) + summed).astype(jnp.bfloat16)
        if layer_idx + 1 < layers:
            state, tail = ring_gather(share, "head", tables, tail_rows=border_rows)
        else:
            state = ring_gather(share, "head", tables)
    all_rows = state.shape[0]
    attn_in = normed(state, gains[layers])
    qkv_parts = jnp.transpose(w_qkv[:, :, 0, :], (1, 0, 2))
    queries, keys_own, values_own = (
        jnp.dot(attn_in, qkv_parts[i], preferred_element_type=jnp.float32).astype(jnp.bfloat16)
        for i in range(3)
    )
    keys_values_prev = shifted(jnp.concatenate([keys_own, values_own], axis=1), "blk", 1)
    keys_prev = keys_values_prev[:, :head_size]
    values_prev = keys_values_prev[:, head_size:]
    own_part = attend(queries, keys_own, values_own, True)
    crossing_portion = lax.cond(
        blk_pos > 0,
        lambda: attend(queries, keys_prev, values_prev, False),
        lambda: neutral(all_rows, head_size),
    )
    peak, denom, weighted = combine(own_part, crossing_portion)
    heads_out = (weighted / denom[:, None]).astype(jnp.bfloat16)
    attn_share = attention_portion_for(heads_out, w_out[0], tok_rows, tables)
    return (share.astype(jnp.float32) + attn_share).astype(jnp.bfloat16)


def solution(mesh):
    placed = (
        P(("grp", "blk", "head"), None),
        P(),
        P(),
        P(None, None, None, None, "head"),
        P(None, "head", None),
        P(None, None, "head", None),
        P("head", None, None),
    )
    return jax.shard_map(
        per_device,
        mesh=mesh,
        in_specs=placed,
        out_specs=P(("grp", "blk", "head"), None),
        check_vma=False,
    )
```
